32 devices in a mesh: slab: 4 (over x, core), chan: 2 (over y), filt: 4 (over z).
Axes of the slice: x: 2, y: 2, z: 4, core: 2. Of those that a mesh axis runs over, the one named last changes fastest.
Arguments:
- volume: bfloat16 [256, 8, 32, 128], P('chan', 'slab'), may hold values from -6 to 6
- plane_weight: bfloat16 [3, 3, 256, 256], P(None, None, 'chan', 'filt'), may hold values from -0.125 to 0.125
- depth_weight: bfloat16 [3, 256, 256], replicated, may hold values from -0.21875 to 0.21875
- grad_out: bfloat16 [256, 8, 32, 128], P('filt', 'slab', 'chan'), may hold values from -6 to 6
Outputs:
- output: bfloat16 [256, 8, 32, 128], P('filt', 'slab', 'chan')
- grad_in: bfloat16 [256, 8, 32, 128], P('chan', 'slab', 'filt')
The draws below stay inside these ranges and needn't reach their ends.
All inputs are finite; a program needn't handle non-finite values.
Results may differ from the reference program's by a relative error of at most 0.0049.
Values may be sent and summed in bfloat16 or wider, within the bound.
No kernel may reach another device: no remote copies, remote signals or barrier semaphores. Data moves between devices by JAX's collectives and lax.ppermute only.
A program may use at most 64 MiB of HBM per device.

```python
import jax
import jax.numpy as jnp

CIN = 256
CMID = 256
COUT = 256
H = 32
W = 128
D = 8


def steps_of(stream_key, extent, split, smallest, top_value):
    level = 1.0
    for position, shards_of in split:
        draws = jax.random.uniform(jax.random.fold_in(jax.random.fold_in(stream_key, 6), position), (shards_of,), jnp.float32, smallest / len(split), top_value / len(split))
        level = level * jnp.repeat(jnp.exp(draws), extent[position] // shards_of).reshape((-1,) + (1,) * (len(extent) - 1 - position))
    return level


def centred(own_key, extent, scale, most, split=(), dtype=jnp.bfloat16):
    gain = steps_of(own_key, extent, split, -0.22, 0.18) if split else 1.0
    values = jax.random.normal(own_key, extent, jnp.float32) * scale * gain
    return jnp.minimum(jnp.maximum(values, -most), most).astype(dtype)


def setup_inputs(seed: int = 0) -> dict:
    key_of = jax.random.split(jax.random.key(seed), 5)
    volume = centred(key_of[0], (CIN, D, H, W), 1.0, 6.0, ((0, 2), (1, 4)))
    plane_weight = centred(key_of[1], (3, 3, CIN, CMID), (9 * CIN) ** -0.5, 0.125, ((2, 2), (3, 4)))
    depth_weight = centred(key_of[2], (3, COUT, CMID), (3 * CMID) ** -0.5, 0.21875)
    grad_out = centred(key_of[3], (COUT, D, H, W), 1.0, 6.0, ((0, 4), (1, 4), (2, 2)))
    return {"volume": volume, "plane_weight": plane_weight, "depth_weight": depth_weight, "grad_out": grad_out}


def plane_ref(field, weight):
    rows = field.shape[2]
    cols = field.shape[3]
    padded = jnp.pad(field, ((0, 0), (0, 0), (1, 1), (1, 1)))
    total = jnp.zeros((weight.shape[3], field.shape[1], rows, cols), jnp.float32)
    for row_tap in range(3):
        for col_tap in range(3):
            window = padded[:, :, row_tap:row_tap + rows, col_tap:col_tap + cols]
            total = total + jnp.einsum("cm,czhw->mzhw", weight[row_tap, col_tap], window)
    return total


def reference(volume, plane_weight, depth_weight, grad_out):
    first = plane_weight.astype(jnp.float32)
    second = depth_weight.astype(jnp.float32)
    mid = plane_ref(volume.astype(jnp.float32), first).astype(jnp.bfloat16)
    depth = mid.shape[1]
    mid_pad = jnp.pad(mid.astype(jnp.float32), ((0, 0), (1, 1), (0, 0), (0, 0)))
    output = jnp.zeros((second.shape[1],) + mid.shape[1:], jnp.float32)
    for tap in range(3):
        output = output + jnp.einsum("om,mzhw->ozhw", second[tap], mid_pad[:, tap:tap + depth])
    output = output.astype(jnp.bfloat16)
    grad_pad = jnp.pad(grad_out.astype(jnp.float32), ((0, 0), (1, 1), (0, 0), (0, 0)))
    grad_mid = jnp.zeros(mid.shape, jnp.float32)
    for tap in range(3):
        grad_mid = grad_mid + jnp.einsum("om,ozhw->mzhw", second[tap], grad_pad[:, 2 - tap:2 - tap + depth])
    grad_mid = grad_mid.astype(jnp.bfloat16)
    flipped = jnp.transpose(first[::-1, ::-1], (0, 1, 3, 2))
    grad_in = plane_ref(grad_mid.astype(jnp.float32), flipped).astype(jnp.bfloat16)
    return output, grad_in
```

```python
import jax
import jax.numpy as jnp
from jax import lax
from jax.sharding import PartitionSpec as P

ROWS = ("chan", "filt")


def shift_pairs(n, k):
    return [(i, (i + k) % n) for i in range(n)]


def order_blocks(pieces, me, dim):
    n = len(pieces)
    if n == 1:
        return pieces[0]
    block = pieces[0].shape[dim]
    stacked = jnp.concatenate(pieces[::-1], axis=dim)
    return jnp.roll(stacked, (me + 1) * block, axis=dim)


def gather_blocks(x, axis, dim):
    n = lax.axis_size(axis)
    me = lax.axis_index(axis)
    pieces = [x] + [lax.ppermute(x, axis, shift_pairs(n, k)) for k in range(1, n)]
    return order_blocks(pieces, me, dim)


def scatter_blocks(x, axis, dim, gather_dim):
    n = lax.axis_size(axis)
    me = lax.axis_index(axis)
    size = x.shape[dim] // n
    take = lambda t: lax.dynamic_slice_in_dim(x, t * size, size, dim)
    pieces = [take(me)]
    for k in range(1, n):
        pieces.append(lax.ppermute(take((me + k) % n), axis, shift_pairs(n, k)))
    return order_blocks(pieces, me, gather_dim)


def halo(x, axis, dim, place=None):
    n = lax.axis_size(axis)
    place = place or (lambda i: i)
    up = [(place(i), place(i + 1)) for i in range(n - 1)]
    down = [(place(i + 1), place(i)) for i in range(n - 1)]
    length = x.shape[dim]
    before = lax.ppermute(lax.slice_in_dim(x, length - 1, length, axis=dim), axis, up)
    after = lax.ppermute(lax.slice_in_dim(x, 0, 1, axis=dim), axis, down)
    return jnp.concatenate([before, x, after], axis=dim)


def plane_conv(rows, weight, spec):
    return lax.conv_general_dilated(
        rows,
        weight,
        window_strides=(1, 1),
        padding=((0, 0), (1, 1)),
        dimension_numbers=("CNHW", spec, "CNHW"),
        preferred_element_type=jnp.float32,
    )


def depth_conv(padded, weight, spec):
    out = lax.conv_general_dilated(
        padded[None],
        weight[:, None, None],
        window_strides=(1, 1, 1),
        padding=((0, 0), (0, 0), (0, 0)),
        dimension_numbers=("NCDHW", spec, "NCDHW"),
        preferred_element_type=jnp.float32,
    )
    return out[0]


def forward(volume, weight, depth_weight):
    chans = lax.axis_size("chan")
    filts = lax.axis_size("filt")
    chan = lax.axis_index("chan")
    filt = lax.axis_index("filt")
    rows = volume.shape[2] // (chans * filts)
    padded = jnp.pad(volume, ((0, 0), (0, 0), (1, 1), (0, 0)))
    window = lambda group: lax.dynamic_slice_in_dim(padded, group * rows, rows + 2, 2)
    pieces = [window(chan * filts + filt)]
    for k in range(1, chans):
        target = (chan + k) % chans
        pieces.append(lax.ppermute(window(target * filts + filt), "chan", shift_pairs(chans, k)))
    all_channels = order_blocks(pieces, chan, 0)
    mid = plane_conv(all_channels, weight, "HWIO").astype(jnp.bfloat16)
    deep = halo(mid, "slab", 1)
    out = depth_conv(deep, depth_weight, "DHWOI").astype(jnp.bfloat16)
    return scatter_blocks(out, "filt", 0, 2)


def backward(grad_out, weight, depth_weight):
    chans = lax.axis_size("chan")
    filts = lax.axis_size("filt")
    chan = lax.axis_index("chan")
    filt = lax.axis_index("filt")
    rows = grad_out.shape[2] // filts
    group = filt * chans + chan
    own = group % filts
    place = lambda g: (g % chans) * filts + g // chans
    pieces = []
    for k in range(filts):
        pairs = [(c * filts + f, place(c * filts + (f + k) % filts)) for f in range(filts) for c in range(chans)]
        block = lax.dynamic_slice_in_dim(grad_out, ((filt + k) % filts) * rows, rows, 2)
        pieces.append(lax.ppermute(block, ROWS, pairs))
    all_filters = order_blocks(pieces, own, 0)
    deep = halo(all_filters, "slab", 1)
    grad_mid = depth_conv(deep, depth_weight[::-1], "DHWIO").astype(jnp.bfloat16)
    rimmed = halo(grad_mid, ROWS, 2, place)
    grad_in = plane_conv(rimmed, weight[::-1, ::-1], "HWOI").astype(jnp.bfloat16)
    return scatter_blocks(grad_in, "chan", 0, 2)


def local(volume, plane_weight, depth_weight, grad_out):
    weight = gather_blocks(gather_blocks(plane_weight, "filt", 3), "chan", 2)
    output = forward(volume, weight, depth_weight)
    grad_in = backward(grad_out, weight, depth_weight)
    return (output, grad_in)


def solution(mesh):
    placed = (
        P("chan", "slab", None, None),
        P(None, None, "chan", "filt"),
        P(),
        P("filt", "slab", "chan", None),
    )
    return jax.shard_map(
        local,
        mesh=mesh,
        in_specs=placed,
        out_specs=(P("filt", "slab", "chan", None), P("chan", "slab", "filt", None)),
        check_vma=False,
    )
```

```python
import jax
import jax.numpy as jnp
from jax import lax
from jax.sharding import PartitionSpec as P

ROWS = ("chan", "filt")


def shift_pairs(n, k):
    return [(i, (i + k) % n) for i in range(n)]


def order_blocks(pieces, me, dim):
    n = len(pieces)
    if n == 1:
        return pieces[0]
    block = pieces[0].shape[dim]
    stacked = jnp.concatenate(pieces[::-1], axis=dim)
    return jnp.roll(stacked, (me + 1) * block, axis=dim)


def gather_blocks(x, axis, dim):
    n = lax.axis_size(axis)
    me = lax.axis_index(axis)
    pieces = [x] + [lax.ppermute(x, axis, shift_pairs(n, k)) for k in range(1, n)]
    return order_blocks(pieces, me, dim)


def scatter_blocks(x, axis, dim, gather_dim):
    n = lax.axis_size(axis)
    me = lax.axis_index(axis)
    size = x.shape[dim] // n
    take = lambda t: lax.dynamic_slice_in_dim(x, t * size, size, dim)
    pieces = [take(me)]
    for k in range(1, n):
        pieces.append(lax.ppermute(take((me + k) % n), axis, shift_pairs(n, k)))
    return order_blocks(pieces, me, gather_dim)


def halo(x, axis, dim, place=None):
    n = lax.axis_size(axis)
    place = place or (lambda i: i)
    up = [(place(i), place(i + 1)) for i in range(n - 1)]
    down = [(place(i + 1), place(i)) for i in range(n - 1)]
    length = x.shape[dim]
    before = lax.ppermute(lax.slice_in_dim(x, length - 1, length, axis=dim), axis, up)
    after = lax.ppermute(lax.slice_in_dim(x, 0, 1, axis=dim), axis, down)
    return jnp.concatenate([before, x, after], axis=dim)


def plane_conv(rows, weight, spec):
    return lax.conv_general_dilated(
        rows,
        weight,
        window_strides=(1, 1),
        padding=((0, 0), (1, 1)),
        dimension_numbers=("CNHW", spec, "CNHW"),
        preferred_element_type=jnp.float32,
    )


def depth_conv(padded, weight, spec):
    out = lax.conv_general_dilated(
        padded[None],
        weight[:, None, None],
        window_strides=(1, 1, 1),
        padding=((0, 0), (0, 0), (0, 0)),
        dimension_numbers=("NCDHW", spec, "NCDHW"),
        preferred_element_type=jnp.float32,
    )
    return out[0]


def gather_weight(weight):
    filts = lax.axis_size("filt")
    chans = lax.axis_size("chan")
    spread = jnp.broadcast_to(weight[None], (filts,) + weight.shape)
    by_filt = lax.all_to_all(spread, "filt", 0, 0, tiled=True)
    spread = jnp.broadcast_to(by_filt[None], (chans,) + by_filt.shape)
    both = lax.all_to_all(spread, "chan", 0, 0, tiled=True)
    c_loc, m_loc = weight.shape[2:]
    whole = jnp.transpose(both, (2, 3, 0, 4, 1, 5))
    return whole.reshape(3, 3, chans * c_loc, filts * m_loc)


def forward(volume, weight, depth_weight):
    chans = lax.axis_size("chan")
    filts = lax.axis_size("filt")
    filt = lax.axis_index("filt")
    rows = volume.shape[2] // (chans * filts)
    padded = jnp.pad(volume, ((0, 0), (0, 0), (1, 1), (0, 0)))
    windows = jnp.stack(
        [lax.dynamic_slice_in_dim(padded, (t * filts + filt) * rows, rows + 2, 2) for t in range(chans)]
    )
    all_channels = lax.all_to_all(windows, "chan", 0, 0, tiled=True)
    all_channels = all_channels.reshape((-1,) + all_channels.shape[2:])
    mid = plane_conv(all_channels, weight, "HWIO").astype(jnp.bfloat16)
    deep = halo(mid, "slab", 1)
    out = depth_conv(deep, depth_weight, "DHWOI").astype(jnp.bfloat16)
    return lax.all_to_all(out, "filt", 0, 2, tiled=True)


def backward(grad_out, weight, depth_weight):
    chans = lax.axis_size("chan")
    filts = lax.axis_size("filt")
    chan = lax.axis_index("chan")
    filt = lax.axis_index("filt")
    rows = grad_out.shape[2] // filts
    rimmed = halo(grad_out, "chan", 2)
    windows = jnp.stack([lax.slice_in_dim(rimmed, t * rows, t * rows + rows + 2, axis=2) for t in range(filts)])
    all_filters = lax.all_to_all(windows, "filt", 0, 0, tiled=True)
    all_filters = all_filters.reshape((-1,) + all_filters.shape[2:])
    deep = halo(all_filters, "slab", 1)
    grad_mid = depth_conv(deep, depth_weight[::-1], "DHWIO").astype(jnp.bfloat16)
    grad_in = plane_conv(grad_mid, weight[::-1, ::-1], "HWOI").astype(jnp.bfloat16)
    place = lambda c, f: c * filts + f
    c_loc = grad_in.shape[0] // chans
    pieces = []
    for j in range(chans):
        pairs = []
        for c in range(chans):
            for f in range(filts):
                group = c * filts + f
                pairs.append((place(c, f), place((group + j) % chans, group // chans)))
        block = lax.dynamic_slice_in_dim(grad_in, ((chan * filts + filt + j) % chans) * c_loc, c_loc, 0)
        pieces.append(lax.ppermute(block, ROWS, pairs))
    return order_blocks(pieces, chan, 2)


def local(volume, plane_weight, depth_weight, grad_out):
    weight = gather_weight(plane_weight)
    output = forward(volume, weight, depth_weight)
    grad_in = backward(grad_out, weight, depth_weight)
    return (output, grad_in)


def solution(mesh):
    placed = (
        P("chan", "slab", None, None),
        P(None, None, "chan", "filt"),
        P(),
        P("filt", "slab", "chan", None),
    )
    return jax.shard_map(
        local,
        mesh=mesh,
        in_specs=placed,
        out_specs=(P("filt", "slab", "chan", None), P("chan", "slab", "filt", None)),
        check_vma=False,
    )
```

```python
import jax
import jax.numpy as jnp
from jax import lax
from jax.sharding import PartitionSpec as P

ROWS = ("chan", "filt")


def shift_pairs(n, k):
    return [(i, (i + k) % n) for i in range(n)]


def order_blocks(pieces, me, dim):
    n = len(pieces)
    if n == 1:
        return pieces[0]
    block = pieces[0].shape[dim]
    stacked = jnp.concatenate(pieces[::-1], axis=dim)
    return jnp.roll(stacked, (me + 1) * block, axis=dim)


def gather_blocks(x, axis, dim):
    n = lax.axis_size(axis)
    me = lax.axis_index(axis)
    pieces = [x] + [lax.ppermute(x, axis, shift_pairs(n, k)) for k in range(1, n)]
    return order_blocks(pieces, me, dim)


def scatter_blocks(x, axis, dim, gather_dim):
    n = lax.axis_size(axis)
    me = lax.axis_index(axis)
    size = x.shape[dim] // n
    take = lambda t: lax.dynamic_slice_in_dim(x, t * size, size, dim)
    pieces = [take(me)]
    for k in range(1, n):
        pieces.append(lax.ppermute(take((me + k) % n), axis, shift_pairs(n, k)))
    return order_blocks(pieces, me, gather_dim)


def halo(x, axis, dim, place=None):
    n = lax.axis_size(axis)
    place = place or (lambda i: i)
    up = [(place(i), place(i + 1)) for i in range(n - 1)]
    down = [(place(i + 1), place(i)) for i in range(n - 1)]
    length = x.shape[dim]
    before = lax.ppermute(lax.slice_in_dim(x, length - 1, length, axis=dim), axis, up)
    after = lax.ppermute(lax.slice_in_dim(x, 0, 1, axis=dim), axis, down)
    return jnp.concatenate([before, x, after], axis=dim)


def plane_conv(rows, weight, spec):
    return lax.conv_general_dilated(
        rows,
        weight,
        window_strides=(1, 1),
        padding=((0, 0), (1, 1)),
        dimension_numbers=("CNHW", spec, "CNHW"),
        preferred_element_type=jnp.float32,
    )


def depth_conv(padded, weight, spec):
    out = lax.conv_general_dilated(
        padded[None],
        weight[:, None, None],
        window_strides=(1, 1, 1),
        padding=((0, 0), (0, 0), (0, 0)),
        dimension_numbers=("NCDHW", spec, "NCDHW"),
        preferred_element_type=jnp.float32,
    )
    return out[0]


def gather_weight(weight):
    filts = lax.axis_size("filt")
    chans = lax.axis_size("chan")
    slabs = lax.axis_size("slab")
    core = lax.axis_index("slab") % 2
    c_loc, m_loc = weight.shape[2:]
    half = c_loc // 2
    mine = lax.dynamic_slice_in_dim(weight, core * half, half, 2)
    spread = jnp.broadcast_to(mine[None], (filts,) + mine.shape)
    by_filt = lax.all_to_all(spread, "filt", 0, 0, tiled=True)
    spread = jnp.broadcast_to(by_filt[None], (chans,) + by_filt.shape)
    both = lax.all_to_all(spread, "chan", 0, 0, tiled=True)
    other = lax.ppermute(both, "slab", [(i, i ^ 1) for i in range(slabs)])
    halves = jnp.where(core == 0, jnp.stack([both, other]), jnp.stack([other, both]))
    whole = jnp.transpose(halves, (3, 4, 1, 0, 5, 2, 6))
    return whole.reshape(3, 3, chans * c_loc, filts * m_loc)


def forward(volume, weight, depth_weight):
    chans = lax.axis_size("chan")
    filts = lax.axis_size("filt")
    filt = lax.axis_index("filt")
    rows = volume.shape[2] // (chans * filts)
    padded = jnp.pad(volume, ((0, 0), (0, 0), (1, 1), (0, 0)))
    windows = jnp.stack(
        [lax.dynamic_slice_in_dim(padded, (t * filts + filt) * rows, rows + 2, 2) for t in range(chans)]
    )
    all_channels = lax.all_to_all(windows, "chan", 0, 0, tiled=True)
    all_channels = all_channels.reshape((-1,) + all_channels.shape[2:])
    mid = plane_conv(all_channels, weight, "HWIO").astype(jnp.bfloat16)
    deep = halo(mid, "slab", 1)
    out = depth_conv(deep, depth_weight, "DHWOI").astype(jnp.bfloat16)
    return lax.all_to_all(out, "filt", 0, 2, tiled=True)


def backward(grad_out, weight, depth_weight):
    chans = lax.axis_size("chan")
    filts = lax.axis_size("filt")
    chan = lax.axis_index("chan")
    filt = lax.axis_index("filt")
    rows = grad_out.shape[2] // filts
    place = lambda g: (g % chans) * filts + g // chans
    pieces = []
    for k in range(filts):
        pairs = [(c * filts + f, place(c * filts + (f + k) % filts)) for f in range(filts) for c in range(chans)]
        block = lax.dynamic_slice_in_dim(grad_out, ((filt + k) % filts) * rows, rows, 2)
        pieces.append(lax.ppermute(block, ROWS, pairs))
    all_filters = order_blocks(pieces, (filt * chans + chan) % filts, 0)
    deep = halo(all_filters, "slab", 1)
    grad_mid = depth_conv(deep, depth_weight[::-1], "DHWIO").astype(jnp.bfloat16)
    rimmed = halo(grad_mid, ROWS, 2, place)
    grad_in = plane_conv(rimmed, weight[::-1, ::-1], "HWOI").astype(jnp.bfloat16)
    return lax.all_to_all(grad_in, "chan", 0, 2, tiled=True)


def local(volume, plane_weight, depth_weight, grad_out):
    weight = gather_weight(plane_weight)
    output = forward(volume, weight, depth_weight)
    grad_in = backward(grad_out, weight, depth_weight)
    return (output, grad_in)


def solution(mesh):
    placed = (
        P("chan", "slab", None, None),
        P(None, None, "chan", "filt"),
        P(),
        P("filt", "slab", "chan", None),
    )
    return jax.shard_map(
        local,
        mesh=mesh,
        in_specs=placed,
        out_specs=(P("filt", "slab", "chan", None), P("chan", "slab", "filt", None)),
        check_vma=False,
    )
```

```python
import jax
import jax.numpy as jnp
from jax import lax
from jax.sharding import PartitionSpec as P

ROWS = ("chan", "filt")


def shift_pairs(n, k):
    return [(i, (i + k) % n) for i in range(n)]


def order_blocks(pieces, me, dim):
    n = len(pieces)
    if n == 1:
        return pieces[0]
    block = pieces[0].shape[dim]
    stacked = jnp.concatenate(pieces[::-1], axis=dim)
    return jnp.roll(stacked, (me + 1) * block, axis=dim)


def gather_blocks(x, axis, dim):
    n = lax.axis_size(axis)
    me = lax.axis_index(axis)
    pieces = [x] + [lax.ppermute(x, axis, shift_pairs(n, k)) for k in range(1, n)]
    return order_blocks(pieces, me, dim)


def scatter_blocks(x, axis, dim, gather_dim):
    n = lax.axis_size(axis)
    me = lax.axis_index(axis)
    size = x.shape[dim] // n
    take = lambda t: lax.dynamic_slice_in_dim(x, t * size, size, dim)
    pieces = [take(me)]
    for k in range(1, n):
        pieces.append(lax.ppermute(take((me + k) % n), axis, shift_pairs(n, k)))
    return order_blocks(pieces, me, gather_dim)


def halo(x, axis, dim, place=None):
    n = lax.axis_size(axis)
    place = place or (lambda i: i)
    up = [(place(i), place(i + 1)) for i in range(n - 1)]
    down = [(place(i + 1), place(i)) for i in range(n - 1)]
    length = x.shape[dim]
    before = lax.ppermute(lax.slice_in_dim(x, length - 1, length, axis=dim), axis, up)
    after = lax.ppermute(lax.slice_in_dim(x, 0, 1, axis=dim), axis, down)
    return jnp.concatenate([before, x, after], axis=dim)


def plane_conv(rows, weight, spec):
    return lax.conv_general_dilated(
        rows,
        weight,
        window_strides=(1, 1),
        padding=((0, 0), (1, 1)),
        dimension_numbers=("CNHW", spec, "CNHW"),
        preferred_element_type=jnp.float32,
    )


def depth_conv(padded, weight, spec):
    out = lax.conv_general_dilated(
        padded[None],
        weight[:, None, None],
        window_strides=(1, 1, 1),
        padding=((0, 0), (0, 0), (0, 0)),
        dimension_numbers=("NCDHW", spec, "NCDHW"),
        preferred_element_type=jnp.float32,
    )
    return out[0]


def spread_weight(weight):
    filts = lax.axis_size("filt")
    core = lax.axis_index("slab") % 2
    half = weight.shape[2] // 2
    mine = lax.dynamic_slice_in_dim(weight, core * half, half, 2)
    return jnp.broadcast_to(mine[None], (filts,) + mine.shape)


def finish_weight(by_filt, c_loc):
    chans = lax.axis_size("chan")
    slabs = lax.axis_size("slab")
    core = lax.axis_index("slab") % 2
    filts, m_loc = by_filt.shape[0], by_filt.shape[-1]
    spread = jnp.broadcast_to(by_filt[None], (chans,) + by_filt.shape)
    both = lax.all_to_all(spread, "chan", 0, 0, tiled=True)
    other = lax.ppermute(both, "slab", [(i, i ^ 1) for i in range(slabs)])
    halves = jnp.where(core == 0, jnp.stack([both, other]), jnp.stack([other, both]))
    whole = jnp.transpose(halves, (3, 4, 1, 0, 5, 2, 6))
    return whole.reshape(3, 3, chans * c_loc, filts * m_loc)


def send_filt(parts):
    filts = lax.axis_size("filt")
    flat = [p.reshape(filts, -1) for p in parts]
    sizes = [f.shape[1] for f in flat]
    got = lax.all_to_all(jnp.concatenate(flat, axis=1), "filt", 0, 0, tiled=True)
    out, at = [], 0
    for p, n in zip(parts, sizes):
        out.append(got[:, at : at + n].reshape(p.shape))
        at += n
    return out


def forward(volume, weight, depth_weight):
    chans = lax.axis_size("chan")
    filts = lax.axis_size("filt")
    filt = lax.axis_index("filt")
    rows = volume.shape[2] // (chans * filts)
    padded = jnp.pad(volume, ((0, 0), (0, 0), (1, 1), (0, 0)))
    windows = jnp.stack(
        [lax.dynamic_slice_in_dim(padded, (t * filts + filt) * rows, rows + 2, 2) for t in range(chans)]
    )
    all_channels = lax.all_to_all(windows, "chan", 0, 0, tiled=True)
    all_channels = all_channels.reshape((-1,) + all_channels.shape[2:])
    mid = plane_conv(all_channels, weight, "HWIO").astype(jnp.bfloat16)
    deep = halo(mid, "slab", 1)
    out = depth_conv(deep, depth_weight, "DHWOI").astype(jnp.bfloat16)
    return lax.all_to_all(out, "filt", 0, 2, tiled=True)


def grad_windows(grad_out):
    filts = lax.axis_size("filt")
    rows = grad_out.shape[2] // filts
    rimmed = halo(grad_out, "chan", 2)
    return jnp.stack([lax.slice_in_dim(rimmed, t * rows, t * rows + rows + 2, axis=2) for t in range(filts)])


def backward(windows, weight, depth_weight):
    chans = lax.axis_size("chan")
    filts = lax.axis_size("filt")
    chan = lax.axis_index("chan")
    filt = lax.axis_index("filt")
    all_filters = windows.reshape((-1,) + windows.shape[2:])
    deep = halo(all_filters, "slab", 1)
    grad_mid = depth_conv(deep, depth_weight[::-1], "DHWIO").astype(jnp.bfloat16)
    grad_in = plane_conv(grad_mid, weight[::-1, ::-1], "HWOI").astype(jnp.bfloat16)
    place = lambda c, f: c * filts + f
    c_loc = grad_in.shape[0] // chans
    pieces = []
    for j in range(chans):
        pairs = []
        for c in range(chans):
            for f in range(filts):
                group = c * filts + f
                pairs.append((place(c, f), place((group + j) % chans, group // chans)))
        block = lax.dynamic_slice_in_dim(grad_in, ((chan * filts + filt + j) % chans) * c_loc, c_loc, 0)
        pieces.append(lax.ppermute(block, ROWS, pairs))
    return order_blocks(pieces, chan, 2)


def local(volume, plane_weight, depth_weight, grad_out):
    by_filt, windows = send_filt([spread_weight(plane_weight), grad_windows(grad_out)])
    weight = finish_weight(by_filt, plane_weight.shape[2])
    output = forward(volume, weight, depth_weight)
    grad_in = backward(windows, weight, depth_weight)
    return (output, grad_in)


def solution(mesh):
    placed = (
        P("chan", "slab", None, None),
        P(None, None, "chan", "filt"),
        P(),
        P("filt", "slab", "chan", None),
    )
    return jax.shard_map(
        local,
        mesh=mesh,
        in_specs=placed,
        out_specs=(P("filt", "slab", "chan", None), P("chan", "slab", "filt", None)),
        check_vma=False,
    )
```

```python
import jax
import jax.numpy as jnp
from jax import lax
from jax.sharding import PartitionSpec as P

ROWS = ("chan", "filt")


def shift_pairs(n, k):
    return [(i, (i + k) % n) for i in range(n)]


def order_blocks(pieces, me, dim):
    n = len(pieces)
    if n == 1:
        return pieces[0]
    block = pieces[0].shape[dim]
    stacked = jnp.concatenate(pieces[::-1], axis=dim)
    return jnp.roll(stacked, (me + 1) * block, axis=dim)


def gather_blocks(x, axis, dim):
    n = lax.axis_size(axis)
    me = lax.axis_index(axis)
    pieces = [x] + [lax.ppermute(x, axis, shift_pairs(n, k)) for k in range(1, n)]
    return order_blocks(pieces, me, dim)


def scatter_blocks(x, axis, dim, gather_dim):
    n = lax.axis_size(axis)
    me = lax.axis_index(axis)
    size = x.shape[dim] // n
    take = lambda t: lax.dynamic_slice_in_dim(x, t * size, size, dim)
    pieces = [take(me)]
    for k in range(1, n):
        pieces.append(lax.ppermute(take((me + k) % n), axis, shift_pairs(n, k)))
    return order_blocks(pieces, me, gather_dim)


def halo(x, axis, dim, place=None):
    n = lax.axis_size(axis)
    place = place or (lambda i: i)
    up = [(place(i), place(i + 1)) for i in range(n - 1)]
    down = [(place(i + 1), place(i)) for i in range(n - 1)]
    length = x.shape[dim]
    before = lax.ppermute(lax.slice_in_dim(x, length - 1, length, axis=dim), axis, up)
    after = lax.ppermute(lax.slice_in_dim(x, 0, 1, axis=dim), axis, down)
    return jnp.concatenate([before, x, after], axis=dim)


def plane_conv(rows, weight, spec):
    return lax.conv_general_dilated(
        rows,
        weight,
        window_strides=(1, 1),
        padding=((0, 0), (1, 1)),
        dimension_numbers=("CNHW", spec, "CNHW"),
        preferred_element_type=jnp.float32,
    )


def depth_conv(padded, weight, spec):
    out = lax.conv_general_dilated(
        padded[None],
        weight[:, None, None],
        window_strides=(1, 1, 1),
        padding=((0, 0), (0, 0), (0, 0)),
        dimension_numbers=("NCDHW", spec, "NCDHW"),
        preferred_element_type=jnp.float32,
    )
    return out[0]


def gather_weight(weight):
    filts = lax.axis_size("filt")
    chans = lax.axis_size("chan")
    spread = jnp.broadcast_to(weight[None], (filts,) + weight.shape)
    by_filt = lax.all_to_all(spread, "filt", 0, 0, tiled=True)
    both = gather_blocks(by_filt[None], "chan", 0)
    c_loc, m_loc = weight.shape[2:]
    whole = jnp.transpose(both, (2, 3, 0, 4, 1, 5))
    return whole.reshape(3, 3, chans * c_loc, filts * m_loc)


def forward(volume, weight, depth_weight):
    chans = lax.axis_size("chan")
    filts = lax.axis_size("filt")
    filt = lax.axis_index("filt")
    rows = volume.shape[2] // (chans * filts)
    padded = jnp.pad(volume, ((0, 0), (0, 0), (1, 1), (0, 0)))
    chan = lax.axis_index("chan")
    window = lambda group: lax.dynamic_slice_in_dim(padded, group * rows, rows + 2, 2)
    pieces = [window(chan * filts + filt)]
    for k in range(1, chans):
        target = (chan + k) % chans
        pieces.append(lax.ppermute(window(target * filts + filt), "chan", shift_pairs(chans, k)))
    all_channels = order_blocks(pieces, chan, 0)
    mid = plane_conv(all_channels, weight, "HWIO").astype(jnp.bfloat16)
    deep = halo(mid, "slab", 1)
    out = depth_conv(deep, depth_weight, "DHWOI").astype(jnp.bfloat16)
    return lax.all_to_all(out, "filt", 0, 2, tiled=True)


def backward(grad_out, weight, depth_weight):
    chans = lax.axis_size("chan")
    filts = lax.axis_size("filt")
    chan = lax.axis_index("chan")
    filt = lax.axis_index("filt")
    rows = grad_out.shape[2] // filts
    rimmed = halo(grad_out, "chan", 2)
    windows = jnp.stack([lax.slice_in_dim(rimmed, t * rows, t * rows + rows + 2, axis=2) for t in range(filts)])
    all_filters = lax.all_to_all(windows, "filt", 0, 0, tiled=True)
    all_filters = all_filters.reshape((-1,) + all_filters.shape[2:])
    deep = halo(all_filters, "slab", 1)
    grad_mid = depth_conv(deep, depth_weight[::-1], "DHWIO").astype(jnp.bfloat16)
    grad_in = plane_conv(grad_mid, weight[::-1, ::-1], "HWOI").astype(jnp.bfloat16)
    place = lambda c, f: c * filts + f
    c_loc = grad_in.shape[0] // chans
    pieces = []
    for j in range(chans):
        pairs = []
        for c in range(chans):
            for f in range(filts):
                group = c * filts + f
                pairs.append((place(c, f), place((group + j) % chans, group // chans)))
        block = lax.dynamic_slice_in_dim(grad_in, ((chan * filts + filt + j) % chans) * c_loc, c_loc, 0)
        pieces.append(lax.ppermute(block, ROWS, pairs))
    return order_blocks(pieces, chan, 2)


def local(volume, plane_weight, depth_weight, grad_out):
    weight = gather_weight(plane_weight)
    output = forward(volume, weight, depth_weight)
    grad_in = backward(grad_out, weight, depth_weight)
    return (output, grad_in)


def solution(mesh):
    placed = (
        P("chan", "slab", None, None),
        P(None, None, "chan", "filt"),
        P(),
        P("filt", "slab", "chan", None),
    )
    return jax.shard_map(
        local,
        mesh=mesh,
        in_specs=placed,
        out_specs=(P("filt", "slab", "chan", None), P("chan", "slab", "filt", None)),
        check_vma=False,
    )
```

```python
import jax
import jax.numpy as jnp
from jax import lax
from jax.sharding import PartitionSpec as P

ROWS = ("chan", "filt")


def shift_pairs(n, k):
    return [(i, (i + k) % n) for i in range(n)]


def order_blocks(pieces, me, dim):
    n = len(pieces)
    if n == 1:
        return pieces[0]
    block = pieces[0].shape[dim]
    stacked = jnp.concatenate(pieces[::-1], axis=dim)
    return jnp.roll(stacked, (me + 1) * block, axis=dim)


def gather_blocks(x, axis, dim):
    n = lax.axis_size(axis)
    me = lax.axis_index(axis)
    pieces = [x] + [lax.ppermute(x, axis, shift_pairs(n, k)) for k in range(1, n)]
    return order_blocks(pieces, me, dim)


def scatter_blocks(x, axis, dim, gather_dim):
    n = lax.axis_size(axis)
    me = lax.axis_index(axis)
    size = x.shape[dim] // n
    take = lambda t: lax.dynamic_slice_in_dim(x, t * size, size, dim)
    pieces = [take(me)]
    for k in range(1, n):
        pieces.append(lax.ppermute(take((me + k) % n), axis, shift_pairs(n, k)))
    return order_blocks(pieces, me, gather_dim)


def halo(x, axis, dim, place=None):
    n = lax.axis_size(axis)
    place = place or (lambda i: i)
    up = [(place(i), place(i + 1)) for i in range(n - 1)]
    down = [(place(i + 1), place(i)) for i in range(n - 1)]
    length = x.shape[dim]
    before = lax.ppermute(lax.slice_in_dim(x, length - 1, length, axis=dim), axis, up)
    after = lax.ppermute(lax.slice_in_dim(x, 0, 1, axis=dim), axis, down)
    return jnp.concatenate([before, x, after], axis=dim)


def plane_conv(rows, weight, spec):
    return lax.conv_general_dilated(
        rows,
        weight,
        window_strides=(1, 1),
        padding=((0, 0), (1, 1)),
        dimension_numbers=("CNHW", spec, "CNHW"),
        preferred_element_type=jnp.float32,
    )


def depth_conv(padded, weight, spec):
    out = lax.conv_general_dilated(
        padded[None],
        weight[:, None, None],
        window_strides=(1, 1, 1),
        padding=((0, 0), (0, 0), (0, 0)),
        dimension_numbers=("NCDHW", spec, "NCDHW"),
        preferred_element_type=jnp.float32,
    )
    return out[0]


def gather_weight(weight):
    filts = lax.axis_size("filt")
    chans = lax.axis_size("chan")
    slabs = lax.axis_size("slab")
    core = lax.axis_index("slab") % 2
    c_loc, m_loc = weight.shape[2:]
    half = c_loc // 2
    mine = lax.dynamic_slice_in_dim(weight, core * half, half, 2)
    spread = jnp.broadcast_to(mine[None], (filts,) + mine.shape)
    by_filt = lax.all_to_all(spread, "filt", 0, 0, tiled=True)
    both = gather_blocks(by_filt[None], "chan", 0)
    other = lax.ppermute(both, "slab", [(i, i ^ 1) for i in range(slabs)])
    halves = jnp.roll(jnp.stack([both, other]), core, axis=0)
    whole = jnp.transpose(halves, (3, 4, 1, 0, 5, 2, 6))
    return whole.reshape(3, 3, chans * c_loc, filts * m_loc)


def forward(volume, weight, depth_weight):
    chans = lax.axis_size("chan")
    filts = lax.axis_size("filt")
    filt = lax.axis_index("filt")
    rows = volume.shape[2] // (chans * filts)
    padded = jnp.pad(volume, ((0, 0), (0, 0), (1, 1), (0, 0)))
    chan = lax.axis_index("chan")
    window = lambda group: lax.dynamic_slice_in_dim(padded, group * rows, rows + 2, 2)
    pieces = [window(chan * filts + filt)]
    for k in range(1, chans):
        target = (chan + k) % chans
        pieces.append(lax.ppermute(window(target * filts + filt), "chan", shift_pairs(chans, k)))
    all_channels = order_blocks(pieces, chan, 0)
    mid = plane_conv(all_channels, weight, "HWIO").astype(jnp.bfloat16)
    deep = halo(mid, "slab", 1)
    out = depth_conv(deep, depth_weight, "DHWOI").astype(jnp.bfloat16)
    return lax.all_to_all(out, "filt", 0, 2, tiled=True)


def backward(grad_out, weight, depth_weight):
    chans = lax.axis_size("chan")
    filts = lax.axis_size("filt")
    chan = lax.axis_index("chan")
    filt = lax.axis_index("filt")
    rows = grad_out.shape[2] // filts
    rimmed = halo(grad_out, "chan", 2)
    windows = jnp.stack([lax.slice_in_dim(rimmed, t * rows, t * rows + rows + 2, axis=2) for t in range(filts)])
    all_filters = lax.all_to_all(windows, "filt", 0, 0, tiled=True)
    all_filters = all_filters.reshape((-1,) + all_filters.shape[2:])
    deep = halo(all_filters, "slab", 1)
    grad_mid = depth_conv(deep, depth_weight[::-1], "DHWIO").astype(jnp.bfloat16)
    grad_in = plane_conv(grad_mid, weight[::-1, ::-1], "HWOI").astype(jnp.bfloat16)
    place = lambda c, f: c * filts + f
    c_loc = grad_in.shape[0] // chans
    pieces = []
    for j in range(chans):
        pairs = []
        for c in range(chans):
            for f in range(filts):
                group = c * filts + f
                pairs.append((place(c, f), place((group + j) % chans, group // chans)))
        block = lax.dynamic_slice_in_dim(grad_in, ((chan * filts + filt + j) % chans) * c_loc, c_loc, 0)
        pieces.append(lax.ppermute(block, ROWS, pairs))
    return order_blocks(pieces, chan, 2)


def local(volume, plane_weight, depth_weight, grad_out):
    weight = gather_weight(plane_weight)
    output = forward(volume, weight, depth_weight)
    grad_in = backward(grad_out, weight, depth_weight)
    return (output, grad_in)


def solution(mesh):
    placed = (
        P("chan", "slab", None, None),
        P(None, None, "chan", "filt"),
        P(),
        P("filt", "slab", "chan", None),
    )
    return jax.shard_map(
        local,
        mesh=mesh,
        in_specs=placed,
        out_specs=(P("filt", "slab", "chan", None), P("chan", "slab", "filt", None)),
        check_vma=False,
    )
```

```python
import jax
import jax.numpy as jnp
from jax import lax
from jax.sharding import PartitionSpec as P

ROWS = ("chan", "filt")


def shift_pairs(n, k):
    return [(i, (i + k) % n) for i in range(n)]


def order_blocks(pieces, me, dim):
    n = len(pieces)
    if n == 1:
        return pieces[0]
    block = pieces[0].shape[dim]
    stacked = jnp.concatenate(pieces[::-1], axis=dim)
    return jnp.roll(stacked, (me + 1) * block, axis=dim)


def gather_blocks(x, axis, dim):
    n = lax.axis_size(axis)
    me = lax.axis_index(axis)
    pieces = [x] + [lax.ppermute(x, axis, shift_pairs(n, k)) for k in range(1, n)]
    return order_blocks(pieces, me, dim)


def scatter_blocks(x, axis, dim, gather_dim):
    n = lax.axis_size(axis)
    me = lax.axis_index(axis)
    size = x.shape[dim] // n
    take = lambda t: lax.dynamic_slice_in_dim(x, t * size, size, dim)
    pieces = [take(me)]
    for k in range(1, n):
        pieces.append(lax.ppermute(take((me + k) % n), axis, shift_pairs(n, k)))
    return order_blocks(pieces, me, gather_dim)


def halo(x, axis, dim, place=None):
    n = lax.axis_size(axis)
    place = place or (lambda i: i)
    up = [(place(i), place(i + 1)) for i in range(n - 1)]
    down = [(place(i + 1), place(i)) for i in range(n - 1)]
    length = x.shape[dim]
    before = lax.ppermute(lax.slice_in_dim(x, length - 1, length, axis=dim), axis, up)
    after = lax.ppermute(lax.slice_in_dim(x, 0, 1, axis=dim), axis, down)
    return jnp.concatenate([before, x, after], axis=dim)


def plane_conv(rows, weight, spec):
    return lax.conv_general_dilated(
        rows,
        weight,
        window_strides=(1, 1),
        padding=((0, 0), (1, 1)),
        dimension_numbers=("CNHW", spec, "CNHW"),
        preferred_element_type=jnp.float32,
    )


def depth_conv(padded, weight, spec):
    out = lax.conv_general_dilated(
        padded[None],
        weight[:, None, None],
        window_strides=(1, 1, 1),
        padding=((0, 0), (0, 0), (0, 0)),
        dimension_numbers=("NCDHW", spec, "NCDHW"),
        preferred_element_type=jnp.float32,
    )
    return out[0]


def gather_weight(weight):
    filts = lax.axis_size("filt")
    chans = lax.axis_size("chan")
    spread = jnp.broadcast_to(weight[None], (filts,) + weight.shape)
    by_filt = lax.all_to_all(spread, "filt", 0, 0, tiled=True)
    both = gather_blocks(by_filt[None], "chan", 0)
    c_loc, m_loc = weight.shape[2:]
    whole = jnp.transpose(both, (2, 3, 0, 4, 1, 5))
    return whole.reshape(3, 3, chans * c_loc, filts * m_loc)


def sub_block(chan, filt, filts):
    return jnp.where(chan % 2 == 0, filt, filts - 1 - filt)


def sub_block_of(c, f, filts):
    return f if c % 2 == 0 else filts - 1 - f


def forward(volume, weight, depth_weight):
    chans = lax.axis_size("chan")
    filts = lax.axis_size("filt")
    chan = lax.axis_index("chan")
    filt = lax.axis_index("filt")
    rows = volume.shape[2] // (chans * filts)
    padded = jnp.pad(volume, ((0, 0), (0, 0), (1, 1), (0, 0)))
    window = lambda c: lax.dynamic_slice_in_dim(padded, (c * filts + sub_block(c, filt, filts)) * rows, rows + 2, 2)
    pieces = [window(chan)]
    for k in range(1, chans):
        pieces.append(lax.ppermute(window((chan + k) % chans), "chan", shift_pairs(chans, k)))
    all_channels = order_blocks(pieces, chan, 0)
    mid = plane_conv(all_channels, weight, "HWIO").astype(jnp.bfloat16)
    deep = halo(mid, "slab", 1)
    out = depth_conv(deep, depth_weight, "DHWOI").astype(jnp.bfloat16)
    got = lax.all_to_all(out, "filt", 0, 2, tiled=True)
    split = got.reshape(got.shape[:2] + (filts, rows) + got.shape[3:])
    flipped = jnp.where(chan % 2 == 0, split, split[:, :, ::-1])
    return flipped.reshape(got.shape)


def backward(grad_out, weight, depth_weight):
    chans = lax.axis_size("chan")
    filts = lax.axis_size("filt")
    chan = lax.axis_index("chan")
    filt = lax.axis_index("filt")
    rows = grad_out.shape[2] // filts
    blocks = jnp.stack(
        [lax.dynamic_slice_in_dim(grad_out, sub_block(chan, t, filts) * rows, rows, 2) for t in range(filts)]
    )
    all_filters = lax.all_to_all(blocks, "filt", 0, 0, tiled=True)
    all_filters = all_filters.reshape((-1,) + all_filters.shape[2:])
    deep = halo(all_filters, "slab", 1)
    grad_mid = depth_conv(deep, depth_weight[::-1], "DHWIO").astype(jnp.bfloat16)
    place = lambda g: (g // filts) * filts + sub_block_of(g // filts, g % filts, filts)
    rimmed = halo(grad_mid, ROWS, 2, place)
    grad_in = plane_conv(rimmed, weight[::-1, ::-1], "HWOI").astype(jnp.bfloat16)
    group = chan * filts + sub_block(chan, filt, filts)
    c_loc = grad_in.shape[0] // chans
    pieces = []
    for j in range(chans):
        pairs = []
        for c in range(chans):
            for f in range(filts):
                g = c * filts + sub_block_of(c, f, filts)
                pairs.append((c * filts + f, ((g + j) % chans) * filts + g // chans))
        block = lax.dynamic_slice_in_dim(grad_in, ((group + j) % chans) * c_loc, c_loc, 0)
        pieces.append(lax.ppermute(block, ROWS, pairs))
    return order_blocks(pieces, chan, 2)


def local(volume, plane_weight, depth_weight, grad_out):
    weight = gather_weight(plane_weight)
    output = forward(volume, weight, depth_weight)
    grad_in = backward(grad_out, weight, depth_weight)
    return (output, grad_in)


def solution(mesh):
    placed = (
        P("chan", "slab", None, None),
        P(None, None, "chan", "filt"),
        P(),
        P("filt", "slab", "chan", None),
    )
    return jax.shard_map(
        local,
        mesh=mesh,
        in_specs=placed,
        out_specs=(P("filt", "slab", "chan", None), P("chan", "slab", "filt", None)),
        check_vma=False,
    )
```

```python
import jax
import jax.numpy as jnp
from jax import lax
from jax.sharding import PartitionSpec as P

ROWS = ("chan", "filt")


def shift_pairs(n, k):
    return [(i, (i + k) % n) for i in range(n)]


def order_blocks(pieces, me, dim):
    n = len(pieces)
    if n == 1:
        return pieces[0]
    block = pieces[0].shape[dim]
    stacked = jnp.concatenate(pieces[::-1], axis=dim)
    return jnp.roll(stacked, (me + 1) * block, axis=dim)


def gather_blocks(x, axis, dim):
    n = lax.axis_size(axis)
    me = lax.axis_index(axis)
    pieces = [x] + [lax.ppermute(x, axis, shift_pairs(n, k)) for k in range(1, n)]
    return order_blocks(pieces, me, dim)


def scatter_blocks(x, axis, dim, gather_dim):
    n = lax.axis_size(axis)
    me = lax.axis_index(axis)
    size = x.shape[dim] // n
    take = lambda t: lax.dynamic_slice_in_dim(x, t * size, size, dim)
    pieces = [take(me)]
    for k in range(1, n):
        pieces.append(lax.ppermute(take((me + k) % n), axis, shift_pairs(n, k)))
    return order_blocks(pieces, me, gather_dim)


def halo(x, axis, dim, place=None):
    n = lax.axis_size(axis)
    place = place or (lambda i: i)
    up = [(place(i), place(i + 1)) for i in range(n - 1)]
    down = [(place(i + 1), place(i)) for i in range(n - 1)]
    length = x.shape[dim]
    before = lax.ppermute(lax.slice_in_dim(x, length - 1, length, axis=dim), axis, up)
    after = lax.ppermute(lax.slice_in_dim(x, 0, 1, axis=dim), axis, down)
    return jnp.concatenate([before, x, after], axis=dim)


def plane_conv(rows, weight, spec):
    return lax.conv_general_dilated(
        rows,
        weight,
        window_strides=(1, 1),
        padding=((0, 0), (1, 1)),
        dimension_numbers=("CNHW", spec, "CNHW"),
        preferred_element_type=jnp.float32,
    )


def depth_conv(padded, weight, spec):
    out = lax.conv_general_dilated(
        padded[None],
        weight[:, None, None],
        window_strides=(1, 1, 1),
        padding=((0, 0), (0, 0), (0, 0)),
        dimension_numbers=("NCDHW", spec, "NCDHW"),
        preferred_element_type=jnp.float32,
    )
    return out[0]


def gather_weight(weight):
    filts = lax.axis_size("filt")
    chans = lax.axis_size("chan")
    spread = jnp.broadcast_to(weight[None], (filts,) + weight.shape)
    by_filt = lax.all_to_all(spread, "filt", 0, 0, tiled=True)
    both = gather_blocks(by_filt[None], "chan", 0)
    c_loc, m_loc = weight.shape[2:]
    whole = jnp.transpose(both, (2, 3, 0, 4, 1, 5))
    return whole.reshape(3, 3, chans * c_loc, filts * m_loc)


def sub_block(chan, filt, filts):
    return jnp.where(chan % 2 == 0, filt, filts - 1 - filt)


def sub_block_of(c, f, filts):
    return f if c % 2 == 0 else filts - 1 - f


def forward(volume, weight, depth_weight):
    chans = lax.axis_size("chan")
    filts = lax.axis_size("filt")
    chan = lax.axis_index("chan")
    filt = lax.axis_index("filt")
    rows = volume.shape[2] // (chans * filts)
    padded = jnp.pad(volume, ((0, 0), (0, 0), (1, 1), (0, 0)))
    window = lambda c: lax.dynamic_slice_in_dim(padded, (c * filts + sub_block(c, filt, filts)) * rows, rows + 2, 2)
    pieces = [window(chan)]
    for k in range(1, chans):
        pieces.append(lax.ppermute(window((chan + k) % chans), "chan", shift_pairs(chans, k)))
    all_channels = order_blocks(pieces, chan, 0)
    mid = plane_conv(all_channels, weight, "HWIO").astype(jnp.bfloat16)
    deep = halo(mid, "slab", 1)
    out = depth_conv(deep, depth_weight, "DHWOI").astype(jnp.bfloat16)
    got = lax.all_to_all(out, "filt", 0, 2, tiled=True)
    split = got.reshape(got.shape[:2] + (filts, rows) + got.shape[3:])
    flipped = jnp.where(chan % 2 == 0, split, split[:, :, ::-1])
    return flipped.reshape(got.shape)


def backward(grad_out, weight, depth_weight):
    chans = lax.axis_size("chan")
    filts = lax.axis_size("filt")
    chan = lax.axis_index("chan")
    filt = lax.axis_index("filt")
    rows = grad_out.shape[2] // filts
    turn = lambda f, r: r if f % 2 == 0 else chans - 1 - r
    place = lambda g: turn(g // chans, g % chans) * filts + g // chans
    group = filt * chans + jnp.where(filt % 2 == 0, chan, chans - 1 - chan)
    pieces = []
    for k in range(filts):
        pairs = [(c * filts + f, place(c * filts + (f + k) % filts)) for f in range(filts) for c in range(chans)]
        block = lax.dynamic_slice_in_dim(grad_out, ((filt + k) % filts) * rows, rows, 2)
        pieces.append(lax.ppermute(block, ROWS, pairs))
    all_filters = order_blocks(pieces, group % filts, 0)
    deep = halo(all_filters, "slab", 1)
    grad_mid = depth_conv(deep, depth_weight[::-1], "DHWIO").astype(jnp.bfloat16)
    rimmed = halo(grad_mid, ROWS, 2, place)
    grad_in = plane_conv(rimmed, weight[::-1, ::-1], "HWOI").astype(jnp.bfloat16)
    got = lax.all_to_all(grad_in, "chan", 0, 2, tiled=True)
    split = got.reshape(got.shape[:2] + (chans, rows) + got.shape[3:])
    flipped = jnp.where(filt % 2 == 0, split, split[:, :, ::-1])
    return flipped.reshape(got.shape)


def local(volume, plane_weight, depth_weight, grad_out):
    weight = gather_weight(plane_weight)
    output = forward(volume, weight, depth_weight)
    grad_in = backward(grad_out, weight, depth_weight)
    return (output, grad_in)


def solution(mesh):
    placed = (
        P("chan", "slab", None, None),
        P(None, None, "chan", "filt"),
        P(),
        P("filt", "slab", "chan", None),
    )
    return jax.shard_map(
        local,
        mesh=mesh,
        in_specs=placed,
        out_specs=(P("filt", "slab", "chan", None), P("chan", "slab", "filt", None)),
        check_vma=False,
    )
```

```python
import jax
import jax.numpy as jnp
from jax import lax
from jax.sharding import PartitionSpec as P

ROWS = ("chan", "filt")


def shift_pairs(n, k):
    return [(i, (i + k) % n) for i in range(n)]


def order_blocks(pieces, me, dim):
    n = len(pieces)
    if n == 1:
        return pieces[0]
    block = pieces[0].shape[dim]
    stacked = jnp.concatenate(pieces[::-1], axis=dim)
    return jnp.roll(stacked, (me + 1) * block, axis=dim)


def gather_blocks(x, axis, dim):
    n = lax.axis_size(axis)
    me = lax.axis_index(axis)
    pieces = [x] + [lax.ppermute(x, axis, shift_pairs(n, k)) for k in range(1, n)]
    return order_blocks(pieces, me, dim)


def scatter_blocks(x, axis, dim, gather_dim):
    n = lax.axis_size(axis)
    me = lax.axis_index(axis)
    size = x.shape[dim] // n
    take = lambda t: lax.dynamic_slice_in_dim(x, t * size, size, dim)
    pieces = [take(me)]
    for k in range(1, n):
        pieces.append(lax.ppermute(take((me + k) % n), axis, shift_pairs(n, k)))
    return order_blocks(pieces, me, gather_dim)


def halo(x, axis, dim, place=None):
    n = lax.axis_size(axis)
    place = place or (lambda i: i)
    up = [(place(i), place(i + 1)) for i in range(n - 1)]
    down = [(place(i + 1), place(i)) for i in range(n - 1)]
    length = x.shape[dim]
    before = lax.ppermute(lax.slice_in_dim(x, length - 1, length, axis=dim), axis, up)
    after = lax.ppermute(lax.slice_in_dim(x, 0, 1, axis=dim), axis, down)
    return jnp.concatenate([before, x, after], axis=dim)


def plane_conv(rows, weight, spec):
    return lax.conv_general_dilated(
        rows,
        weight,
        window_strides=(1, 1),
        padding=((0, 0), (1, 1)),
        dimension_numbers=("CNHW", spec, "CNHW"),
        preferred_element_type=jnp.float32,
    )


def depth_conv(padded, weight, spec):
    out = lax.conv_general_dilated(
        padded[None],
        weight[:, None, None],
        window_strides=(1, 1, 1),
        padding=((0, 0), (0, 0), (0, 0)),
        dimension_numbers=("NCDHW", spec, "NCDHW"),
        preferred_element_type=jnp.float32,
    )
    return out[0]


def gather_weight(weight):
    filts = lax.axis_size("filt")
    chans = lax.axis_size("chan")
    spread = jnp.broadcast_to(weight[None], (filts,) + weight.shape)
    by_filt = lax.all_to_all(spread, "filt", 0, 0, tiled=True)
    both = gather_blocks(by_filt[None], "chan", 0)
    c_loc, m_loc = weight.shape[2:]
    whole = jnp.transpose(both, (2, 3, 0, 4, 1, 5))
    return whole.reshape(3, 3, chans * c_loc, filts * m_loc)


def sub_block(chan, filt, filts):
    return jnp.where(chan % 2 == 0, filt, filts - 1 - filt)


def sub_block_of(c, f, filts):
    return f if c % 2 == 0 else filts - 1 - f


def forward(volume, weight, depth_weight):
    chans = lax.axis_size("chan")
    filts = lax.axis_size("filt")
    chan = lax.axis_index("chan")
    filt = lax.axis_index("filt")
    rows = volume.shape[2] // (chans * filts)
    padded = jnp.pad(volume, ((0, 0), (0, 0), (1, 1), (0, 0)))
    window = lambda c: lax.dynamic_slice_in_dim(padded, (c * filts + sub_block(c, filt, filts)) * rows, rows + 2, 2)
    pieces = [window(chan)]
    for k in range(1, chans):
        pieces.append(lax.ppermute(window((chan + k) % chans), "chan", shift_pairs(chans, k)))
    all_channels = order_blocks(pieces, chan, 0)
    mid = plane_conv(all_channels, weight, "HWIO").astype(jnp.bfloat16)
    deep = halo(mid, "slab", 1)
    out = depth_conv(deep, depth_weight, "DHWOI").astype(jnp.bfloat16)
    got = lax.all_to_all(out, "filt", 0, 2, tiled=True)
    split = got.reshape(got.shape[:2] + (filts, rows) + got.shape[3:])
    flipped = jnp.where(chan % 2 == 0, split, split[:, :, ::-1])
    return flipped.reshape(got.shape)


def backward(grad_out, weight, depth_weight):
    chans = lax.axis_size("chan")
    filts = lax.axis_size("filt")
    chan = lax.axis_index("chan")
    filt = lax.axis_index("filt")
    rows = grad_out.shape[2] // filts
    turn = lambda f, r: r if f % 2 == 0 else chans - 1 - r
    place = lambda g: turn(g // chans, g % chans) * filts + g // chans
    group_of = lambda c, f: f * chans + turn(f, c)
    need = [[[f for f in range(filts) if group_of(t, f) // filts == r] for r in range(chans)] for t in range(chans)]
    per = max(len(need[t][r]) for t in range(chans) for r in range(chans))
    pick = lambda t, r: [group_of(t, f) % filts for f in need[t][r]] + [0] * (per - len(need[t][r]))
    received = []
    for k in range(chans):
        table = jnp.array([pick((r + k) % chans, r) for r in range(chans)], jnp.int32)[chan]
        send = jnp.stack([lax.dynamic_slice_in_dim(grad_out, table[q] * rows, rows, 2) for q in range(per)])
        received.append(send if k == 0 else lax.ppermute(send, "chan", shift_pairs(chans, k)))
    received = jnp.concatenate(received)
    slot = [[0] * filts for _ in range(chans)]
    for t in range(chans):
        for k in range(chans):
            r = (t - k) % chans
            for q, f in enumerate(need[t][r]):
                slot[t][f] = k * per + q
    blocks = jnp.take(received, jnp.array(slot, jnp.int32)[chan], axis=0)
    all_filters = lax.all_to_all(blocks, "filt", 0, 0, tiled=True)
    all_filters = all_filters.reshape((-1,) + all_filters.shape[2:])
    deep = halo(all_filters, "slab", 1)
    grad_mid = depth_conv(deep, depth_weight[::-1], "DHWIO").astype(jnp.bfloat16)
    rimmed = halo(grad_mid, ROWS, 2, place)
    grad_in = plane_conv(rimmed, weight[::-1, ::-1], "HWOI").astype(jnp.bfloat16)
    got = lax.all_to_all(grad_in, "chan", 0, 2, tiled=True)
    split = got.reshape(got.shape[:2] + (chans, rows) + got.shape[3:])
    flipped = jnp.where(filt % 2 == 0, split, split[:, :, ::-1])
    return flipped.reshape(got.shape)


def local(volume, plane_weight, depth_weight, grad_out):
    weight = gather_weight(plane_weight)
    output = forward(volume, weight, depth_weight)
    grad_in = backward(grad_out, weight, depth_weight)
    return (output, grad_in)


def solution(mesh):
    placed = (
        P("chan", "slab", None, None),
        P(None, None, "chan", "filt"),
        P(),
        P("filt", "slab", "chan", None),
    )
    return jax.shard_map(
        local,
        mesh=mesh,
        in_specs=placed,
        out_specs=(P("filt", "slab", "chan", None), P("chan", "slab", "filt", None)),
        check_vma=False,
    )
```

```python
import jax
import jax.numpy as jnp
from jax import lax
from jax.sharding import PartitionSpec as P

ROWS = ("chan", "filt")


def shift_pairs(n, k):
    return [(i, (i + k) % n) for i in range(n)]


def order_blocks(pieces, me, dim):
    n = len(pieces)
    if n == 1:
        return pieces[0]
    block = pieces[0].shape[dim]
    stacked = jnp.concatenate(pieces[::-1], axis=dim)
    return jnp.roll(stacked, (me + 1) * block, axis=dim)


def gather_blocks(x, axis, dim):
    n = lax.axis_size(axis)
    me = lax.axis_index(axis)
    pieces = [x] + [lax.ppermute(x, axis, shift_pairs(n, k)) for k in range(1, n)]
    return order_blocks(pieces, me, dim)


def scatter_blocks(x, axis, dim, gather_dim):
    n = lax.axis_size(axis)
    me = lax.axis_index(axis)
    size = x.shape[dim] // n
    take = lambda t: lax.dynamic_slice_in_dim(x, t * size, size, dim)
    pieces = [take(me)]
    for k in range(1, n):
        pieces.append(lax.ppermute(take((me + k) % n), axis, shift_pairs(n, k)))
    return order_blocks(pieces, me, gather_dim)


def halo(x, axis, dim, place=None):
    n = lax.axis_size(axis)
    place = place or (lambda i: i)
    up = [(place(i), place(i + 1)) for i in range(n - 1)]
    down = [(place(i + 1), place(i)) for i in range(n - 1)]
    length = x.shape[dim]
    before = lax.ppermute(lax.slice_in_dim(x, length - 1, length, axis=dim), axis, up)
    after = lax.ppermute(lax.slice_in_dim(x, 0, 1, axis=dim), axis, down)
    return jnp.concatenate([before, x, after], axis=dim)


def plane_conv(rows, weight, spec):
    return lax.conv_general_dilated(
        rows,
        weight,
        window_strides=(1, 1),
        padding=((0, 0), (1, 1)),
        dimension_numbers=("CNHW", spec, "CNHW"),
        preferred_element_type=jnp.float32,
    )


def depth_conv(padded, weight, spec):
    out = lax.conv_general_dilated(
        padded[None],
        weight[:, None, None],
        window_strides=(1, 1, 1),
        padding=((0, 0), (0, 0), (0, 0)),
        dimension_numbers=("NCDHW", spec, "NCDHW"),
        preferred_element_type=jnp.float32,
    )
    return out[0]


def relay_gather(x, axis):
    n = lax.axis_size(axis)
    me = lax.axis_index(axis)
    right = [(i, i + 1) for i in range(n - 1)]
    left = [(i + 1, i) for i in range(n - 1)]
    from_left, from_right = [x], [x]
    for _ in range(n - 1):
        from_left.append(lax.ppermute(from_left[-1], axis, right))
        from_right.append(lax.ppermute(from_right[-1], axis, left))
    blocks = []
    for position in range(n):
        block = jnp.zeros_like(x)
        for k in range(n):
            block = jnp.where(me - position == k, from_left[k], block)
            block = jnp.where(position - me == k, from_right[k], block)
        blocks.append(block)
    return jnp.stack(blocks)


def gather_weight(weight):
    filts = lax.axis_size("filt")
    chans = lax.axis_size("chan")
    slabs = lax.axis_size("slab")
    core = lax.axis_index("slab") % 2
    c_loc, m_loc = weight.shape[2:]
    half = c_loc // 2
    mine = lax.dynamic_slice_in_dim(weight, core * half, half, 2)
    by_filt = relay_gather(mine, "filt")
    both = gather_blocks(by_filt[None], "chan", 0)
    other = lax.ppermute(both, "slab", [(i, i ^ 1) for i in range(slabs)])
    halves = jnp.roll(jnp.stack([both, other]), core, axis=0)
    whole = jnp.transpose(halves, (3, 4, 1, 0, 5, 2, 6))
    return whole.reshape(3, 3, chans * c_loc, filts * m_loc)


def sub_block(chan, filt, filts):
    return jnp.where(chan % 2 == 0, filt, filts - 1 - filt)


def sub_block_of(c, f, filts):
    return f if c % 2 == 0 else filts - 1 - f


def forward(volume, weight, depth_weight):
    chans = lax.axis_size("chan")
    filts = lax.axis_size("filt")
    chan = lax.axis_index("chan")
    filt = lax.axis_index("filt")
    rows = volume.shape[2] // (chans * filts)
    padded = jnp.pad(volume, ((0, 0), (0, 0), (1, 1), (0, 0)))
    window = lambda c: lax.dynamic_slice_in_dim(padded, (c * filts + sub_block(c, filt, filts)) * rows, rows + 2, 2)
    pieces = [window(chan)]
    for k in range(1, chans):
        pieces.append(lax.ppermute(window((chan + k) % chans), "chan", shift_pairs(chans, k)))
    all_channels = order_blocks(pieces, chan, 0)
    mid = plane_conv(all_channels, weight, "HWIO").astype(jnp.bfloat16)
    deep = halo(mid, "slab", 1)
    out = depth_conv(deep, depth_weight, "DHWOI").astype(jnp.bfloat16)
    got = lax.all_to_all(out, "filt", 0, 2, tiled=True)
    split = got.reshape(got.shape[:2] + (filts, rows) + got.shape[3:])
    flipped = jnp.where(chan % 2 == 0, split, split[:, :, ::-1])
    return flipped.reshape(got.shape)


def backward(grad_out, weight, depth_weight):
    chans = lax.axis_size("chan")
    filts = lax.axis_size("filt")
    chan = lax.axis_index("chan")
    filt = lax.axis_index("filt")
    rows = grad_out.shape[2] // filts
    turn = lambda f, r: r if f % 2 == 0 else chans - 1 - r
    place = lambda g: turn(g // chans, g % chans) * filts + g // chans
    group_of = lambda c, f: f * chans + turn(f, c)
    need = [[[f for f in range(filts) if group_of(t, f) // filts == r] for r in range(chans)] for t in range(chans)]
    per = max(len(need[t][r]) for t in range(chans) for r in range(chans))
    pick = lambda t, r: [group_of(t, f) % filts for f in need[t][r]] + [0] * (per - len(need[t][r]))
    received = []
    for k in range(chans):
        table = jnp.array([pick((r + k) % chans, r) for r in range(chans)], jnp.int32)[chan]
        send = jnp.stack([lax.dynamic_slice_in_dim(grad_out, table[q] * rows, rows, 2) for q in range(per)])
        received.append(send if k == 0 else lax.ppermute(send, "chan", shift_pairs(chans, k)))
    received = jnp.concatenate(received)
    slot = [[0] * filts for _ in range(chans)]
    for t in range(chans):
        for k in range(chans):
            r = (t - k) % chans
            for q, f in enumerate(need[t][r]):
                slot[t][f] = k * per + q
    blocks = jnp.take(received, jnp.array(slot, jnp.int32)[chan], axis=0)
    all_filters = lax.all_to_all(blocks, "filt", 0, 0, tiled=True)
    all_filters = all_filters.reshape((-1,) + all_filters.shape[2:])
    deep = halo(all_filters, "slab", 1)
    grad_mid = depth_conv(deep, depth_weight[::-1], "DHWIO").astype(jnp.bfloat16)
    rimmed = halo(grad_mid, ROWS, 2, place)
    grad_in = plane_conv(rimmed, weight[::-1, ::-1], "HWOI").astype(jnp.bfloat16)
    got = lax.all_to_all(grad_in, "chan", 0, 2, tiled=True)
    split = got.reshape(got.shape[:2] + (chans, rows) + got.shape[3:])
    flipped = jnp.where(filt % 2 == 0, split, split[:, :, ::-1])
    return flipped.reshape(got.shape)


def local(volume, plane_weight, depth_weight, grad_out):
    weight = gather_weight(plane_weight)
    output = forward(volume, weight, depth_weight)
    grad_in = backward(grad_out, weight, depth_weight)
    return (output, grad_in)


def solution(mesh):
    placed = (
        P("chan", "slab", None, None),
        P(None, None, "chan", "filt"),
        P(),
        P("filt", "slab", "chan", None),
    )
    return jax.shard_map(
        local,
        mesh=mesh,
        in_specs=placed,
        out_specs=(P("filt", "slab", "chan", None), P("chan", "slab", "filt", None)),
        check_vma=False,
    )
```

```python
import jax
import jax.numpy as jnp
from jax import lax
from jax.sharding import PartitionSpec as P

ROWS = ("chan", "filt")


def shift_pairs(n, k):
    return [(i, (i + k) % n) for i in range(n)]


def order_blocks(pieces, me, dim):
    n = len(pieces)
    if n == 1:
        return pieces[0]
    block = pieces[0].shape[dim]
    stacked = jnp.concatenate(pieces[::-1], axis=dim)
    return jnp.roll(stacked, (me + 1) * block, axis=dim)


def gather_blocks(x, axis, dim):
    n = lax.axis_size(axis)
    me = lax.axis_index(axis)
    pieces = [x] + [lax.ppermute(x, axis, shift_pairs(n, k)) for k in range(1, n)]
    return order_blocks(pieces, me, dim)


def scatter_blocks(x, axis, dim, gather_dim):
    n = lax.axis_size(axis)
    me = lax.axis_index(axis)
    size = x.shape[dim] // n
    take = lambda t: lax.dynamic_slice_in_dim(x, t * size, size, dim)
    pieces = [take(me)]
    for k in range(1, n):
        pieces.append(lax.ppermute(take((me + k) % n), axis, shift_pairs(n, k)))
    return order_blocks(pieces, me, gather_dim)


def halo(x, axis, dim, place=None):
    n = lax.axis_size(axis)
    place = place or (lambda i: i)
    up = [(place(i), place(i + 1)) for i in range(n - 1)]
    down = [(place(i + 1), place(i)) for i in range(n - 1)]
    length = x.shape[dim]
    before = lax.ppermute(lax.slice_in_dim(x, length - 1, length, axis=dim), axis, up)
    after = lax.ppermute(lax.slice_in_dim(x, 0, 1, axis=dim), axis, down)
    return jnp.concatenate([before, x, after], axis=dim)


def plane_conv(rows, weight, spec):
    return lax.conv_general_dilated(
        rows,
        weight,
        window_strides=(1, 1),
        padding=((0, 0), (1, 1)),
        dimension_numbers=("CNHW", spec, "CNHW"),
        preferred_element_type=jnp.float32,
    )


def depth_conv(padded, weight, spec):
    out = lax.conv_general_dilated(
        padded[None],
        weight[:, None, None],
        window_strides=(1, 1, 1),
        padding=((0, 0), (0, 0), (0, 0)),
        dimension_numbers=("NCDHW", spec, "NCDHW"),
        preferred_element_type=jnp.float32,
    )
    return out[0]


def gather_weight(weight):
    filts = lax.axis_size("filt")
    chans = lax.axis_size("chan")
    spread = jnp.broadcast_to(weight[None], (filts,) + weight.shape)
    by_filt = lax.all_to_all(spread, "filt", 0, 0, tiled=True)
    both = gather_blocks(by_filt[None], "chan", 0)
    c_loc, m_loc = weight.shape[2:]
    whole = jnp.transpose(both, (2, 3, 0, 4, 1, 5))
    return whole.reshape(3, 3, chans * c_loc, filts * m_loc)


def sub_block(chan, filt, filts):
    return jnp.where(chan % 2 == 0, filt, filts - 1 - filt)


def sub_block_of(c, f, filts):
    return f if c % 2 == 0 else filts - 1 - f


def forward(volume, weight, depth_weight):
    chans = lax.axis_size("chan")
    filts = lax.axis_size("filt")
    chan = lax.axis_index("chan")
    filt = lax.axis_index("filt")
    rows = volume.shape[2] // (chans * filts)
    padded = jnp.pad(volume, ((0, 0), (0, 0), (1, 1), (0, 0)))
    window = lambda c: lax.dynamic_slice_in_dim(padded, (c * filts + sub_block(c, filt, filts)) * rows, rows + 2, 2)
    pieces = [window(chan)]
    for k in range(1, chans):
        pieces.append(lax.ppermute(window((chan + k) % chans), "chan", shift_pairs(chans, k)))
    all_channels = order_blocks(pieces, chan, 0)
    return plane_conv(all_channels, weight, "HWIO").astype(jnp.bfloat16)


def forward_out(deep, depth_weight):
    chans = lax.axis_size("chan")
    filts = lax.axis_size("filt")
    chan = lax.axis_index("chan")
    rows = deep.shape[2]
    out = depth_conv(deep, depth_weight, "DHWOI").astype(jnp.bfloat16)
    got = lax.all_to_all(out, "filt", 0, 2, tiled=True)
    split = got.reshape(got.shape[:2] + (filts, rows) + got.shape[3:])
    flipped = jnp.where(chan % 2 == 0, split, split[:, :, ::-1])
    return flipped.reshape(got.shape)


def backward(grad_out, weight, depth_weight):
    chans = lax.axis_size("chan")
    filts = lax.axis_size("filt")
    chan = lax.axis_index("chan")
    filt = lax.axis_index("filt")
    rows = grad_out.shape[2] // filts
    turn = lambda f, r: r if f % 2 == 0 else chans - 1 - r
    place = lambda g: turn(g // chans, g % chans) * filts + g // chans
    group_of = lambda c, f: f * chans + turn(f, c)
    need = [[[f for f in range(filts) if group_of(t, f) // filts == r] for r in range(chans)] for t in range(chans)]
    per = max(len(need[t][r]) for t in range(chans) for r in range(chans))
    pick = lambda t, r: [group_of(t, f) % filts for f in need[t][r]] + [0] * (per - len(need[t][r]))
    received = []
    for k in range(chans):
        table = jnp.array([pick((r + k) % chans, r) for r in range(chans)], jnp.int32)[chan]
        send = jnp.stack([lax.dynamic_slice_in_dim(grad_out, table[q] * rows, rows, 2) for q in range(per)])
        received.append(send if k == 0 else lax.ppermute(send, "chan", shift_pairs(chans, k)))
    received = jnp.concatenate(received)
    slot = [[0] * filts for _ in range(chans)]
    for t in range(chans):
        for k in range(chans):
            r = (t - k) % chans
            for q, f in enumerate(need[t][r]):
                slot[t][f] = k * per + q
    blocks = jnp.take(received, jnp.array(slot, jnp.int32)[chan], axis=0)
    all_filters = lax.all_to_all(blocks, "filt", 0, 0, tiled=True)
    return all_filters.reshape((-1,) + all_filters.shape[2:])


def backward_in(deep, weight, depth_weight):
    chans = lax.axis_size("chan")
    filts = lax.axis_size("filt")
    filt = lax.axis_index("filt")
    rows = deep.shape[2]
    turn = lambda f, r: r if f % 2 == 0 else chans - 1 - r
    place = lambda g: turn(g // chans, g % chans) * filts + g // chans
    grad_mid = depth_conv(deep, depth_weight[::-1], "DHWIO").astype(jnp.bfloat16)
    rimmed = halo(grad_mid, ROWS, 2, place)
    grad_in = plane_conv(rimmed, weight[::-1, ::-1], "HWOI").astype(jnp.bfloat16)
    got = scatter_blocks(grad_in, "chan", 0, 2)
    split = got.reshape(got.shape[:2] + (chans, rows) + got.shape[3:])
    flipped = jnp.where(filt % 2 == 0, split, split[:, :, ::-1])
    return flipped.reshape(got.shape)


def local(volume, plane_weight, depth_weight, grad_out):
    weight = gather_weight(plane_weight)
    mid = forward(volume, weight, depth_weight)
    all_filters = backward(grad_out, weight, depth_weight)
    deep = halo(jnp.concatenate([mid, all_filters]), "slab", 1)
    output = forward_out(deep[: mid.shape[0]], depth_weight)
    grad_in = backward_in(deep[mid.shape[0] :], weight, depth_weight)
    return (output, grad_in)


def solution(mesh):
    placed = (
        P("chan", "slab", None, None),
        P(None, None, "chan", "filt"),
        P(),
        P("filt", "slab", "chan", None),
    )
    return jax.shard_map(
        local,
        mesh=mesh,
        in_specs=placed,
        out_specs=(P("filt", "slab", "chan", None), P("chan", "slab", "filt", None)),
        check_vma=False,
    )
```

```python
import jax
import jax.numpy as jnp
from jax import lax
from jax.sharding import PartitionSpec as P

ROWS = ("chan", "filt")


def shift_pairs(n, k):
    return [(i, (i + k) % n) for i in range(n)]


def order_blocks(pieces, me, dim):
    n = len(pieces)
    if n == 1:
        return pieces[0]
    block = pieces[0].shape[dim]
    stacked = jnp.concatenate(pieces[::-1], axis=dim)
    return jnp.roll(stacked, (me + 1) * block, axis=dim)


def gather_blocks(x, axis, dim):
    n = lax.axis_size(axis)
    me = lax.axis_index(axis)
    pieces = [x] + [lax.ppermute(x, axis, shift_pairs(n, k)) for k in range(1, n)]
    return order_blocks(pieces, me, dim)


def scatter_blocks(x, axis, dim, gather_dim):
    n = lax.axis_size(axis)
    me = lax.axis_index(axis)
    size = x.shape[dim] // n
    take = lambda t: lax.dynamic_slice_in_dim(x, t * size, size, dim)
    pieces = [take(me)]
    for k in range(1, n):
        pieces.append(lax.ppermute(take((me + k) % n), axis, shift_pairs(n, k)))
    return order_blocks(pieces, me, gather_dim)


def halo(x, axis, dim, place=None):
    n = lax.axis_size(axis)
    place = place or (lambda i: i)
    up = [(place(i), place(i + 1)) for i in range(n - 1)]
    down = [(place(i + 1), place(i)) for i in range(n - 1)]
    length = x.shape[dim]
    before = lax.ppermute(lax.slice_in_dim(x, length - 1, length, axis=dim), axis, up)
    after = lax.ppermute(lax.slice_in_dim(x, 0, 1, axis=dim), axis, down)
    return jnp.concatenate([before, x, after], axis=dim)


def plane_conv(rows, weight, spec):
    return lax.conv_general_dilated(
        rows,
        weight,
        window_strides=(1, 1),
        padding=((0, 0), (1, 1)),
        dimension_numbers=("CNHW", spec, "CNHW"),
        preferred_element_type=jnp.float32,
    )


def depth_conv(padded, weight, spec):
    out = lax.conv_general_dilated(
        padded[None],
        weight[:, None, None],
        window_strides=(1, 1, 1),
        padding=((0, 0), (0, 0), (0, 0)),
        dimension_numbers=("NCDHW", spec, "NCDHW"),
        preferred_element_type=jnp.float32,
    )
    return out[0]


def gather_weight(weight):
    filts = lax.axis_size("filt")
    chans = lax.axis_size("chan")
    spread = jnp.broadcast_to(weight[None], (filts,) + weight.shape)
    by_filt = lax.all_to_all(spread, "filt", 0, 0, tiled=True)
    both = gather_blocks(by_filt[None], "chan", 0)
    c_loc, m_loc = weight.shape[2:]
    whole = jnp.transpose(both, (2, 3, 0, 4, 1, 5))
    return whole.reshape(3, 3, chans * c_loc, filts * m_loc)


def sub_block(chan, filt, filts):
    return jnp.where(chan % 2 == 0, filt, filts - 1 - filt)


def sub_block_of(c, f, filts):
    return f if c % 2 == 0 else filts - 1 - f


def volume_sends(volume):
    chans = lax.axis_size("chan")
    filts = lax.axis_size("filt")
    chan = lax.axis_index("chan")
    filt = lax.axis_index("filt")
    rows = volume.shape[2] // (chans * filts)
    padded = jnp.pad(volume, ((0, 0), (0, 0), (1, 1), (0, 0)))
    window = lambda c: lax.dynamic_slice_in_dim(padded, (c * filts + sub_block(c, filt, filts)) * rows, rows + 2, 2)
    return [window((chan + k) % chans) for k in range(chans)]


def forward(pieces, weight):
    all_channels = order_blocks(pieces, lax.axis_index("chan"), 0)
    return plane_conv(all_channels, weight, "HWIO").astype(jnp.bfloat16)


def forward_out(deep, depth_weight):
    chans = lax.axis_size("chan")
    filts = lax.axis_size("filt")
    chan = lax.axis_index("chan")
    rows = deep.shape[2]
    out = depth_conv(deep, depth_weight, "DHWOI").astype(jnp.bfloat16)
    got = lax.all_to_all(out, "filt", 0, 2, tiled=True)
    split = got.reshape(got.shape[:2] + (filts, rows) + got.shape[3:])
    flipped = jnp.where(chan % 2 == 0, split, split[:, :, ::-1])
    return flipped.reshape(got.shape)


def grad_sends(grad_out):
    chans = lax.axis_size("chan")
    filts = lax.axis_size("filt")
    chan = lax.axis_index("chan")
    filt = lax.axis_index("filt")
    rows = grad_out.shape[2] // filts
    turn = lambda f, r: r if f % 2 == 0 else chans - 1 - r
    place = lambda g: turn(g // chans, g % chans) * filts + g // chans
    group_of = lambda c, f: f * chans + turn(f, c)
    need = [[[f for f in range(filts) if group_of(t, f) // filts == r] for r in range(chans)] for t in range(chans)]
    per = max(len(need[t][r]) for t in range(chans) for r in range(chans))
    pick = lambda t, r: [group_of(t, f) % filts for f in need[t][r]] + [0] * (per - len(need[t][r]))
    sends = []
    for k in range(chans):
        table = jnp.array([pick((r + k) % chans, r) for r in range(chans)], jnp.int32)[chan]
        sends.append(jnp.stack([lax.dynamic_slice_in_dim(grad_out, table[q] * rows, rows, 2) for q in range(per)]))
    return sends


def grad_blocks(received):
    chans = lax.axis_size("chan")
    filts = lax.axis_size("filt")
    chan = lax.axis_index("chan")
    turn = lambda f, r: r if f % 2 == 0 else chans - 1 - r
    group_of = lambda c, f: f * chans + turn(f, c)
    need = [[[f for f in range(filts) if group_of(t, f) // filts == r] for r in range(chans)] for t in range(chans)]
    per = received[0].shape[0]
    received = jnp.concatenate(received)
    slot = [[0] * filts for _ in range(chans)]
    for t in range(chans):
        for k in range(chans):
            r = (t - k) % chans
            for q, f in enumerate(need[t][r]):
                slot[t][f] = k * per + q
    blocks = jnp.take(received, jnp.array(slot, jnp.int32)[chan], axis=0)
    all_filters = lax.all_to_all(blocks, "filt", 0, 0, tiled=True)
    return all_filters.reshape((-1,) + all_filters.shape[2:])


def backward_in(deep, weight, depth_weight):
    chans = lax.axis_size("chan")
    filts = lax.axis_size("filt")
    filt = lax.axis_index("filt")
    rows = deep.shape[2]
    turn = lambda f, r: r if f % 2 == 0 else chans - 1 - r
    place = lambda g: turn(g // chans, g % chans) * filts + g // chans
    grad_mid = depth_conv(deep, depth_weight[::-1], "DHWIO").astype(jnp.bfloat16)
    rimmed = halo(grad_mid, ROWS, 2, place)
    grad_in = plane_conv(rimmed, weight[::-1, ::-1], "HWOI").astype(jnp.bfloat16)
    got = scatter_blocks(grad_in, "chan", 0, 2)
    split = got.reshape(got.shape[:2] + (chans, rows) + got.shape[3:])
    flipped = jnp.where(filt % 2 == 0, split, split[:, :, ::-1])
    return flipped.reshape(got.shape)


def local(volume, plane_weight, depth_weight, grad_out):
    weight = gather_weight(plane_weight)
    chans = lax.axis_size("chan")
    vol_sends, grad_send = volume_sends(volume), grad_sends(grad_out)
    vol_got, grad_got = [vol_sends[0]], [grad_send[0]]
    for k in range(1, chans):
        a, b = vol_sends[k], grad_send[k]
        lead, depth, width = a.shape[0], a.shape[1], a.shape[3]
        if b.size % (lead * depth * width) == 0:
            both = jnp.concatenate([a, b.reshape(lead, depth, -1, width)], axis=2)
            both = lax.ppermute(both, "chan", shift_pairs(chans, k))
            vol_got.append(both[:, :, : a.shape[2]])
            grad_got.append(both[:, :, a.shape[2] :].reshape(b.shape))
        else:
            vol_got.append(lax.ppermute(a, "chan", shift_pairs(chans, k)))
            grad_got.append(lax.ppermute(b, "chan", shift_pairs(chans, k)))
    mid = forward(vol_got, weight)
    all_filters = grad_blocks(grad_got)
    deep = halo(jnp.concatenate([mid, all_filters]), "slab", 1)
    output = forward_out(deep[: mid.shape[0]], depth_weight)
    grad_in = backward_in(deep[mid.shape[0] :], weight, depth_weight)
    return (output, grad_in)


def solution(mesh):
    placed = (
        P("chan", "slab", None, None),
        P(None, None, "chan", "filt"),
        P(),
        P("filt", "slab", "chan", None),
    )
    return jax.shard_map(
        local,
        mesh=mesh,
        in_specs=placed,
        out_specs=(P("filt", "slab", "chan", None), P("chan", "slab", "filt", None)),
        check_vma=False,
    )
```

```python
import jax
import jax.numpy as jnp
from jax import lax
from jax.sharding import PartitionSpec as P

ROWS = ("chan", "filt")


def shift_pairs(n, k):
    return [(i, (i + k) % n) for i in range(n)]


def order_blocks(pieces, me, dim):
    n = len(pieces)
    if n == 1:
        return pieces[0]
    block = pieces[0].shape[dim]
    stacked = jnp.concatenate(pieces[::-1], axis=dim)
    return jnp.roll(stacked, (me + 1) * block, axis=dim)


def gather_blocks(x, axis, dim):
    n = lax.axis_size(axis)
    me = lax.axis_index(axis)
    pieces = [x] + [lax.ppermute(x, axis, shift_pairs(n, k)) for k in range(1, n)]
    return order_blocks(pieces, me, dim)


def scatter_blocks(x, axis, dim, gather_dim):
    n = lax.axis_size(axis)
    me = lax.axis_index(axis)
    size = x.shape[dim] // n
    take = lambda t: lax.dynamic_slice_in_dim(x, t * size, size, dim)
    pieces = [take(me)]
    for k in range(1, n):
        pieces.append(lax.ppermute(take((me + k) % n), axis, shift_pairs(n, k)))
    return order_blocks(pieces, me, gather_dim)


def halo(x, axis, dim, place=None):
    n = lax.axis_size(axis)
    place = place or (lambda i: i)
    up = [(place(i), place(i + 1)) for i in range(n - 1)]
    down = [(place(i + 1), place(i)) for i in range(n - 1)]
    length = x.shape[dim]
    before = lax.ppermute(lax.slice_in_dim(x, length - 1, length, axis=dim), axis, up)
    after = lax.ppermute(lax.slice_in_dim(x, 0, 1, axis=dim), axis, down)
    return jnp.concatenate([before, x, after], axis=dim)


def plane_conv(rows, weight, spec):
    return lax.conv_general_dilated(
        rows,
        weight,
        window_strides=(1, 1),
        padding=((0, 0), (1, 1)),
        dimension_numbers=("CNHW", spec, "CNHW"),
        preferred_element_type=jnp.float32,
    )


def depth_conv(padded, weight, spec):
    out = lax.conv_general_dilated(
        padded[None],
        weight[:, None, None],
        window_strides=(1, 1, 1),
        padding=((0, 0), (0, 0), (0, 0)),
        dimension_numbers=("NCDHW", spec, "NCDHW"),
        preferred_element_type=jnp.float32,
    )
    return out[0]


def gather_weight(weight):
    filts = lax.axis_size("filt")
    chans = lax.axis_size("chan")
    spread = jnp.broadcast_to(weight[None], (filts,) + weight.shape)
    by_filt = lax.all_to_all(spread, "filt", 0, 0, tiled=True)
    both = gather_blocks(by_filt[None], "chan", 0)
    c_loc, m_loc = weight.shape[2:]
    whole = jnp.transpose(both, (2, 3, 0, 4, 1, 5))
    return whole.reshape(3, 3, chans * c_loc, filts * m_loc)


def sub_block(chan, filt, filts):
    return jnp.where(chan % 2 == 0, filt, filts - 1 - filt)


def sub_block_of(c, f, filts):
    return f if c % 2 == 0 else filts - 1 - f


def forward(volume, weight, depth_weight):
    chans = lax.axis_size("chan")
    filts = lax.axis_size("filt")
    chan = lax.axis_index("chan")
    filt = lax.axis_index("filt")
    rows = volume.shape[2] // (chans * filts)
    padded = jnp.pad(volume, ((0, 0), (0, 0), (1, 1), (0, 0)))
    window = lambda c: lax.dynamic_slice_in_dim(padded, (c * filts + filt) * rows, rows + 2, 2)
    pieces = [window(chan)]
    for k in range(1, chans):
        pieces.append(lax.ppermute(window((chan + k) % chans), "chan", shift_pairs(chans, k)))
    all_channels = order_blocks(pieces, chan, 0)
    return plane_conv(all_channels, weight, "HWIO").astype(jnp.bfloat16)


def forward_out(deep, depth_weight):
    chans = lax.axis_size("chan")
    filts = lax.axis_size("filt")
    chan = lax.axis_index("chan")
    rows = deep.shape[2]
    out = depth_conv(deep, depth_weight, "DHWOI").astype(jnp.bfloat16)
    return lax.all_to_all(out, "filt", 0, 2, tiled=True)


def backward(grad_out, weight, depth_weight):
    chans = lax.axis_size("chan")
    filts = lax.axis_size("filt")
    chan = lax.axis_index("chan")
    filt = lax.axis_index("filt")
    rows = grad_out.shape[2] // filts
    turn = lambda f, r: r if f % 2 == 0 else chans - 1 - r
    place = lambda g: turn(g // chans, g % chans) * filts + g // chans
    group_of = lambda c, f: f * chans + turn(f, c)
    need = [[[f for f in range(filts) if group_of(t, f) // filts == r] for r in range(chans)] for t in range(chans)]
    per = max(len(need[t][r]) for t in range(chans) for r in range(chans))
    pick = lambda t, r: [group_of(t, f) % filts for f in need[t][r]] + [0] * (per - len(need[t][r]))
    received = []
    for k in range(chans):
        table = jnp.array([pick((r + k) % chans, r) for r in range(chans)], jnp.int32)[chan]
        send = jnp.stack([lax.dynamic_slice_in_dim(grad_out, table[q] * rows, rows, 2) for q in range(per)])
        received.append(send if k == 0 else lax.ppermute(send, "chan", shift_pairs(chans, k)))
    received = jnp.concatenate(received)
    slot = [[0] * filts for _ in range(chans)]
    for t in range(chans):
        for k in range(chans):
            r = (t - k) % chans
            for q, f in enumerate(need[t][r]):
                slot[t][f] = k * per + q
    blocks = jnp.take(received, jnp.array(slot, jnp.int32)[chan], axis=0)
    all_filters = lax.all_to_all(blocks, "filt", 0, 0, tiled=True)
    return all_filters.reshape((-1,) + all_filters.shape[2:])


def backward_in(deep, weight, depth_weight):
    chans = lax.axis_size("chan")
    filts = lax.axis_size("filt")
    filt = lax.axis_index("filt")
    rows = deep.shape[2]
    turn = lambda f, r: r if f % 2 == 0 else chans - 1 - r
    place = lambda g: turn(g // chans, g % chans) * filts + g // chans
    grad_mid = depth_conv(deep, depth_weight[::-1], "DHWIO").astype(jnp.bfloat16)
    rimmed = halo(grad_mid, ROWS, 2, place)
    grad_in = plane_conv(rimmed, weight[::-1, ::-1], "HWOI").astype(jnp.bfloat16)
    chan = lax.axis_index("chan")
    c_loc = grad_in.shape[0] // chans
    even = filt % 2 == 0
    pieces = [lax.dynamic_slice_in_dim(grad_in, chan * c_loc, c_loc, 0)]
    for k in range(1, chans):
        target = jnp.where(even, (chan + k) % chans, (chan - k) % chans)
        pairs = [(c * filts + f, (((c + k) if f % 2 == 0 else (c - k)) % chans) * filts + f)
                 for c in range(chans) for f in range(filts)]
        pieces.append(lax.ppermute(lax.dynamic_slice_in_dim(grad_in, target * c_loc, c_loc, 0), ROWS, pairs))
    return order_blocks(pieces, jnp.where(even, chan, chans - 1 - chan), 2)


def local(volume, plane_weight, depth_weight, grad_out):
    weight = gather_weight(plane_weight)
    mid = forward(volume, weight, depth_weight)
    all_filters = backward(grad_out, weight, depth_weight)
    deep = halo(jnp.concatenate([mid, all_filters]), "slab", 1)
    output = forward_out(deep[: mid.shape[0]], depth_weight)
    grad_in = backward_in(deep[mid.shape[0] :], weight, depth_weight)
    return (output, grad_in)


def solution(mesh):
    placed = (
        P("chan", "slab", None, None),
        P(None, None, "chan", "filt"),
        P(),
        P("filt", "slab", "chan", None),
    )
    return jax.shard_map(
        local,
        mesh=mesh,
        in_specs=placed,
        out_specs=(P("filt", "slab", "chan", None), P("chan", "slab", "filt", None)),
        check_vma=False,
    )
```

```python
import jax
import jax.numpy as jnp
from jax import lax
from jax.sharding import PartitionSpec as P

ROWS = ("chan", "filt")


def shift_pairs(n, k):
    return [(i, (i + k) % n) for i in range(n)]


def order_blocks(pieces, me, dim):
    n = len(pieces)
    if n == 1:
        return pieces[0]
    block = pieces[0].shape[dim]
    stacked = jnp.concatenate(pieces[::-1], axis=dim)
    return jnp.roll(stacked, (me + 1) * block, axis=dim)


def gather_blocks(x, axis, dim):
    n = lax.axis_size(axis)
    me = lax.axis_index(axis)
    pieces = [x] + [lax.ppermute(x, axis, shift_pairs(n, k)) for k in range(1, n)]
    return order_blocks(pieces, me, dim)


def scatter_blocks(x, axis, dim, gather_dim):
    n = lax.axis_size(axis)
    me = lax.axis_index(axis)
    size = x.shape[dim] // n
    take = lambda t: lax.dynamic_slice_in_dim(x, t * size, size, dim)
    pieces = [take(me)]
    for k in range(1, n):
        pieces.append(lax.ppermute(take((me + k) % n), axis, shift_pairs(n, k)))
    return order_blocks(pieces, me, gather_dim)


def halo(x, axis, dim, place=None):
    n = lax.axis_size(axis)
    place = place or (lambda i: i)
    up = [(place(i), place(i + 1)) for i in range(n - 1)]
    down = [(place(i + 1), place(i)) for i in range(n - 1)]
    length = x.shape[dim]
    before = lax.ppermute(lax.slice_in_dim(x, length - 1, length, axis=dim), axis, up)
    after = lax.ppermute(lax.slice_in_dim(x, 0, 1, axis=dim), axis, down)
    return jnp.concatenate([before, x, after], axis=dim)


def plane_conv(rows, weight, spec):
    return lax.conv_general_dilated(
        rows,
        weight,
        window_strides=(1, 1),
        padding=((0, 0), (1, 1)),
        dimension_numbers=("CNHW", spec, "CNHW"),
        preferred_element_type=jnp.float32,
    )


def depth_conv(padded, weight, spec):
    out = lax.conv_general_dilated(
        padded[None],
        weight[:, None, None],
        window_strides=(1, 1, 1),
        padding=((0, 0), (0, 0), (0, 0)),
        dimension_numbers=("NCDHW", spec, "NCDHW"),
        preferred_element_type=jnp.float32,
    )
    return out[0]


def gather_weight(weight):
    filts = lax.axis_size("filt")
    chans = lax.axis_size("chan")
    spread = jnp.broadcast_to(weight[None], (filts,) + weight.shape)
    by_filt = lax.all_to_all(spread, "filt", 0, 0, tiled=True)
    both = gather_blocks(by_filt[None], "chan", 0)
    c_loc, m_loc = weight.shape[2:]
    whole = jnp.transpose(both, (2, 3, 0, 4, 1, 5))
    return whole.reshape(3, 3, chans * c_loc, filts * m_loc)


def sub_block(chan, filt, filts):
    return jnp.where(chan % 2 == 0, filt, filts - 1 - filt)


def sub_block_of(c, f, filts):
    return f if c % 2 == 0 else filts - 1 - f


def forward(volume, weight, depth_weight):
    chans = lax.axis_size("chan")
    filts = lax.axis_size("filt")
    chan = lax.axis_index("chan")
    filt = lax.axis_index("filt")
    rows = volume.shape[2] // (chans * filts)
    padded = jnp.pad(volume, ((0, 0), (0, 0), (1, 1), (0, 0)))
    window = lambda c: lax.dynamic_slice_in_dim(padded, (c * filts + filt) * rows, rows + 2, 2)
    pieces = [window(chan)]
    for k in range(1, chans):
        pieces.append(lax.ppermute(window((chan + k) % chans), "chan", shift_pairs(chans, k)))
    all_channels = order_blocks(pieces, chan, 0)
    return plane_conv(all_channels, weight, "HWIO").astype(jnp.bfloat16)


def forward_out(deep, depth_weight):
    chans = lax.axis_size("chan")
    filts = lax.axis_size("filt")
    chan = lax.axis_index("chan")
    rows = deep.shape[2]
    return depth_conv(deep, depth_weight, "DHWOI").astype(jnp.bfloat16)


def send_out(out):
    return lax.all_to_all(out, "filt", 0, 2, tiled=True)


def backward(grad_out, weight, depth_weight):
    chans = lax.axis_size("chan")
    filts = lax.axis_size("filt")
    chan = lax.axis_index("chan")
    filt = lax.axis_index("filt")
    rows = grad_out.shape[2] // filts
    turn = lambda f, r: r if f % 2 == 0 else chans - 1 - r
    place = lambda g: turn(g // chans, g % chans) * filts + g // chans
    group_of = lambda c, f: f * chans + turn(f, c)
    need = [[[f for f in range(filts) if group_of(t, f) // filts == r] for r in range(chans)] for t in range(chans)]
    per = max(len(need[t][r]) for t in range(chans) for r in range(chans))
    pick = lambda t, r: [group_of(t, f) % filts for f in need[t][r]] + [0] * (per - len(need[t][r]))
    received = []
    for k in range(chans):
        table = jnp.array([pick((r + k) % chans, r) for r in range(chans)], jnp.int32)[chan]
        send = jnp.stack([lax.dynamic_slice_in_dim(grad_out, table[q] * rows, rows, 2) for q in range(per)])
        received.append(send if k == 0 else lax.ppermute(send, "chan", shift_pairs(chans, k)))
    received = jnp.concatenate(received)
    slot = [[0] * filts for _ in range(chans)]
    for t in range(chans):
        for k in range(chans):
            r = (t - k) % chans
            for q, f in enumerate(need[t][r]):
                slot[t][f] = k * per + q
    blocks = jnp.take(received, jnp.array(slot, jnp.int32)[chan], axis=0)
    all_filters = lax.all_to_all(blocks, "filt", 0, 0, tiled=True)
    return all_filters.reshape((-1,) + all_filters.shape[2:])


def backward_in(deep, weight, depth_weight):
    chans = lax.axis_size("chan")
    filts = lax.axis_size("filt")
    filt = lax.axis_index("filt")
    rows = deep.shape[2]
    turn = lambda f, r: r if f % 2 == 0 else chans - 1 - r
    place = lambda g: turn(g // chans, g % chans) * filts + g // chans
    grad_mid = depth_conv(deep, depth_weight[::-1], "DHWIO").astype(jnp.bfloat16)
    rimmed = halo(grad_mid, ROWS, 2, place)
    return plane_conv(rimmed, weight[::-1, ::-1], "HWOI").astype(jnp.bfloat16)


def send_grad_in(grad_in):
    chans = lax.axis_size("chan")
    filts = lax.axis_size("filt")
    filt = lax.axis_index("filt")
    chan = lax.axis_index("chan")
    c_loc = grad_in.shape[0] // chans
    even = filt % 2 == 0
    pieces = [lax.dynamic_slice_in_dim(grad_in, chan * c_loc, c_loc, 0)]
    for k in range(1, chans):
        target = jnp.where(even, (chan + k) % chans, (chan - k) % chans)
        pairs = [(c * filts + f, (((c + k) if f % 2 == 0 else (c - k)) % chans) * filts + f)
                 for c in range(chans) for f in range(filts)]
        pieces.append(lax.ppermute(lax.dynamic_slice_in_dim(grad_in, target * c_loc, c_loc, 0), ROWS, pairs))
    return order_blocks(pieces, jnp.where(even, chan, chans - 1 - chan), 2)


def local(volume, plane_weight, depth_weight, grad_out):
    weight = gather_weight(plane_weight)
    mid = forward(volume, weight, depth_weight)
    all_filters = backward(grad_out, weight, depth_weight)
    deep = halo(jnp.concatenate([mid, all_filters]), "slab", 1)
    output = forward_out(deep[: mid.shape[0]], depth_weight)
    grad_in = backward_in(deep[mid.shape[0] :], weight, depth_weight)
    output, grad_in = lax.optimization_barrier((output, grad_in))
    return (send_out(output), send_grad_in(grad_in))


def solution(mesh):
    placed = (
        P("chan", "slab", None, None),
        P(None, None, "chan", "filt"),
        P(),
        P("filt", "slab", "chan", None),
    )
    return jax.shard_map(
        local,
        mesh=mesh,
        in_specs=placed,
        out_specs=(P("filt", "slab", "chan", None), P("chan", "slab", "filt", None)),
        check_vma=False,
    )
```

```python
import jax
import jax.numpy as jnp
from jax import lax
from jax.sharding import PartitionSpec as P

ROWS = ("chan", "filt")


def shift_pairs(n, k):
    return [(i, (i + k) % n) for i in range(n)]


def order_blocks(pieces, me, dim):
    n = len(pieces)
    if n == 1:
        return pieces[0]
    block = pieces[0].shape[dim]
    stacked = jnp.concatenate(pieces[::-1], axis=dim)
    return jnp.roll(stacked, (me + 1) * block, axis=dim)


def gather_blocks(x, axis, dim):
    n = lax.axis_size(axis)
    me = lax.axis_index(axis)
    pieces = [x] + [lax.ppermute(x, axis, shift_pairs(n, k)) for k in range(1, n)]
    return order_blocks(pieces, me, dim)


def scatter_blocks(x, axis, dim, gather_dim):
    n = lax.axis_size(axis)
    me = lax.axis_index(axis)
    size = x.shape[dim] // n
    take = lambda t: lax.dynamic_slice_in_dim(x, t * size, size, dim)
    pieces = [take(me)]
    for k in range(1, n):
        pieces.append(lax.ppermute(take((me + k) % n), axis, shift_pairs(n, k)))
    return order_blocks(pieces, me, gather_dim)


def halo(x, axis, dim, place=None):
    n = lax.axis_size(axis)
    place = place or (lambda i: i)
    up = [(place(i), place(i + 1)) for i in range(n - 1)]
    down = [(place(i + 1), place(i)) for i in range(n - 1)]
    length = x.shape[dim]
    before = lax.ppermute(lax.slice_in_dim(x, length - 1, length, axis=dim), axis, up)
    after = lax.ppermute(lax.slice_in_dim(x, 0, 1, axis=dim), axis, down)
    return jnp.concatenate([before, x, after], axis=dim)


def plane_conv(rows, weight, spec):
    return lax.conv_general_dilated(
        rows,
        weight,
        window_strides=(1, 1),
        padding=((0, 0), (1, 1)),
        dimension_numbers=("CNHW", spec, "CNHW"),
        preferred_element_type=jnp.float32,
    )


def depth_conv(padded, weight, spec):
    out = lax.conv_general_dilated(
        padded[None],
        weight[:, None, None],
        window_strides=(1, 1, 1),
        padding=((0, 0), (0, 0), (0, 0)),
        dimension_numbers=("NCDHW", spec, "NCDHW"),
        preferred_element_type=jnp.float32,
    )
    return out[0]


def gather_weight(weight):
    filts = lax.axis_size("filt")
    spread = jnp.broadcast_to(weight[None], (filts,) + weight.shape)
    by_filt = lax.all_to_all(spread, "filt", 0, 4, tiled=True)[0]
    return gather_blocks(by_filt, "chan", 2)


def sub_block(chan, filt, filts):
    return jnp.where(chan % 2 == 0, filt, filts - 1 - filt)


def sub_block_of(c, f, filts):
    return f if c % 2 == 0 else filts - 1 - f


def forward(volume, weight, depth_weight):
    chans = lax.axis_size("chan")
    filts = lax.axis_size("filt")
    chan = lax.axis_index("chan")
    filt = lax.axis_index("filt")
    rows = volume.shape[2] // (chans * filts)
    padded = jnp.pad(volume, ((0, 0), (0, 0), (1, 1), (0, 0)))
    window = lambda c: lax.dynamic_slice_in_dim(padded, (c * filts + filt) * rows, rows + 2, 2)
    pieces = [window(chan)]
    for k in range(1, chans):
        pieces.append(lax.ppermute(window((chan + k) % chans), "chan", shift_pairs(chans, k)))
    all_channels = order_blocks(pieces, chan, 0)
    return plane_conv(all_channels, weight, "HWIO").astype(jnp.bfloat16)


def forward_out(deep, depth_weight):
    chans = lax.axis_size("chan")
    filts = lax.axis_size("filt")
    chan = lax.axis_index("chan")
    rows = deep.shape[2]
    out = depth_conv(deep, depth_weight, "DHWOI").astype(jnp.bfloat16)
    return lax.all_to_all(out, "filt", 0, 2, tiled=True)


def backward(grad_out, weight, depth_weight):
    chans = lax.axis_size("chan")
    filts = lax.axis_size("filt")
    chan = lax.axis_index("chan")
    filt = lax.axis_index("filt")
    rows = grad_out.shape[2] // filts
    turn = lambda f, r: r if f % 2 == 0 else chans - 1 - r
    place = lambda g: turn(g // chans, g % chans) * filts + g // chans
    group_of = lambda c, f: f * chans + turn(f, c)
    need = [[[f for f in range(filts) if group_of(t, f) // filts == r] for r in range(chans)] for t in range(chans)]
    per = max(len(need[t][r]) for t in range(chans) for r in range(chans))
    pick = lambda t, r: [group_of(t, f) % filts for f in need[t][r]] + [0] * (per - len(need[t][r]))
    received = []
    for k in range(chans):
        table = jnp.array([pick((r + k) % chans, r) for r in range(chans)], jnp.int32)[chan]
        send = jnp.stack([lax.dynamic_slice_in_dim(grad_out, table[q] * rows, rows, 2) for q in range(per)])
        received.append(send if k == 0 else lax.ppermute(send, "chan", shift_pairs(chans, k)))
    received = jnp.concatenate(received)
    slot = [[0] * filts for _ in range(chans)]
    for t in range(chans):
        for k in range(chans):
            r = (t - k) % chans
            for q, f in enumerate(need[t][r]):
                slot[t][f] = k * per + q
    blocks = jnp.take(received, jnp.array(slot, jnp.int32)[chan], axis=0)
    all_filters = lax.all_to_all(blocks, "filt", 0, 0, tiled=True)
    return all_filters.reshape((-1,) + all_filters.shape[2:])


def backward_in(deep, weight, depth_weight):
    chans = lax.axis_size("chan")
    filts = lax.axis_size("filt")
    filt = lax.axis_index("filt")
    rows = deep.shape[2]
    turn = lambda f, r: r if f % 2 == 0 else chans - 1 - r
    place = lambda g: turn(g // chans, g % chans) * filts + g // chans
    grad_mid = depth_conv(deep, depth_weight[::-1], "DHWIO").astype(jnp.bfloat16)
    rimmed = halo(grad_mid, ROWS, 2, place)
    grad_in = plane_conv(rimmed, weight[::-1, ::-1], "HWOI").astype(jnp.bfloat16)
    chan = lax.axis_index("chan")
    c_loc = grad_in.shape[0] // chans
    even = filt % 2 == 0
    pieces = [lax.dynamic_slice_in_dim(grad_in, chan * c_loc, c_loc, 0)]
    for k in range(1, chans):
        target = jnp.where(even, (chan + k) % chans, (chan - k) % chans)
        pairs = [(c * filts + f, (((c + k) if f % 2 == 0 else (c - k)) % chans) * filts + f)
                 for c in range(chans) for f in range(filts)]
        pieces.append(lax.ppermute(lax.dynamic_slice_in_dim(grad_in, target * c_loc, c_loc, 0), ROWS, pairs))
    return order_blocks(pieces, jnp.where(even, chan, chans - 1 - chan), 2)


def local(volume, plane_weight, depth_weight, grad_out):
    weight = gather_weight(plane_weight)
    mid = forward(volume, weight, depth_weight)
    all_filters = backward(grad_out, weight, depth_weight)
    deep = halo(jnp.concatenate([mid, all_filters]), "slab", 1)
    output = forward_out(deep[: mid.shape[0]], depth_weight)
    grad_in = backward_in(deep[mid.shape[0] :], weight, depth_weight)
    return (output, grad_in)


def solution(mesh):
    placed = (
        P("chan", "slab", None, None),
        P(None, None, "chan", "filt"),
        P(),
        P("filt", "slab", "chan", None),
    )
    return jax.shard_map(
        local,
        mesh=mesh,
        in_specs=placed,
        out_specs=(P("filt", "slab", "chan", None), P("chan", "slab", "filt", None)),
        check_vma=False,
    )
```

```python
import jax
import jax.numpy as jnp
from jax import lax
from jax.sharding import PartitionSpec as P

ROWS = ("chan", "filt")


def shift_pairs(n, k):
    return [(i, (i + k) % n) for i in range(n)]


def order_blocks(pieces, me, dim):
    n = len(pieces)
    if n == 1:
        return pieces[0]
    block = pieces[0].shape[dim]
    stacked = jnp.concatenate(pieces[::-1], axis=dim)
    return jnp.roll(stacked, (me + 1) * block, axis=dim)


def gather_blocks(x, axis, dim):
    n = lax.axis_size(axis)
    me = lax.axis_index(axis)
    pieces = [x] + [lax.ppermute(x, axis, shift_pairs(n, k)) for k in range(1, n)]
    return order_blocks(pieces, me, dim)


def scatter_blocks(x, axis, dim, gather_dim):
    n = lax.axis_size(axis)
    me = lax.axis_index(axis)
    size = x.shape[dim] // n
    take = lambda t: lax.dynamic_slice_in_dim(x, t * size, size, dim)
    pieces = [take(me)]
    for k in range(1, n):
        pieces.append(lax.ppermute(take((me + k) % n), axis, shift_pairs(n, k)))
    return order_blocks(pieces, me, gather_dim)


def halo(x, axis, dim, place=None):
    n = lax.axis_size(axis)
    place = place or (lambda i: i)
    up = [(place(i), place(i + 1)) for i in range(n - 1)]
    down = [(place(i + 1), place(i)) for i in range(n - 1)]
    length = x.shape[dim]
    before = lax.ppermute(lax.slice_in_dim(x, length - 1, length, axis=dim), axis, up)
    after = lax.ppermute(lax.slice_in_dim(x, 0, 1, axis=dim), axis, down)
    return jnp.concatenate([before, x, after], axis=dim)


def plane_conv(rows, weight, spec):
    return lax.conv_general_dilated(
        rows,
        weight,
        window_strides=(1, 1),
        padding=((0, 0), (1, 1)),
        dimension_numbers=("CNHW", spec, "CNHW"),
        preferred_element_type=jnp.float32,
    )


def depth_conv(padded, weight, spec):
    out = lax.conv_general_dilated(
        padded[None],
        weight[:, None, None],
        window_strides=(1, 1, 1),
        padding=((0, 0), (0, 0), (0, 0)),
        dimension_numbers=("NCDHW", spec, "NCDHW"),
        preferred_element_type=jnp.float32,
    )
    return out[0]


def gather_weight(weight):
    filts = lax.axis_size("filt")
    spread = jnp.broadcast_to(weight[None], (filts,) + weight.shape)
    by_filt = lax.all_to_all(spread, "filt", 0, 4, tiled=True)[0]
    chans = lax.axis_size("chan")
    pieces = [by_filt] + [lax.ppermute(by_filt, "chan", shift_pairs(chans, k)) for k in range(1, chans)]
    return jnp.concatenate(pieces, axis=2)


def sub_block(chan, filt, filts):
    return jnp.where(chan % 2 == 0, filt, filts - 1 - filt)


def sub_block_of(c, f, filts):
    return f if c % 2 == 0 else filts - 1 - f


def forward(volume, weight, depth_weight):
    chans = lax.axis_size("chan")
    filts = lax.axis_size("filt")
    chan = lax.axis_index("chan")
    filt = lax.axis_index("filt")
    rows = volume.shape[2] // (chans * filts)
    padded = jnp.pad(volume, ((0, 0), (0, 0), (1, 1), (0, 0)))
    window = lambda c: lax.dynamic_slice_in_dim(padded, (c * filts + filt) * rows, rows + 2, 2)
    pieces = [window(chan)]
    for k in range(1, chans):
        pieces.append(lax.ppermute(window((chan + k) % chans), "chan", shift_pairs(chans, k)))
    all_channels = jnp.concatenate(pieces, axis=0)
    return plane_conv(all_channels, weight, "HWIO").astype(jnp.bfloat16)


def forward_out(deep, depth_weight):
    chans = lax.axis_size("chan")
    filts = lax.axis_size("filt")
    chan = lax.axis_index("chan")
    rows = deep.shape[2]
    out = depth_conv(deep, depth_weight, "DHWOI").astype(jnp.bfloat16)
    return lax.all_to_all(out, "filt", 0, 2, tiled=True)


def backward(grad_out, weight, depth_weight):
    chans = lax.axis_size("chan")
    filts = lax.axis_size("filt")
    chan = lax.axis_index("chan")
    filt = lax.axis_index("filt")
    rows = grad_out.shape[2] // filts
    turn = lambda f, r: r if f % 2 == 0 else chans - 1 - r
    place = lambda g: turn(g // chans, g % chans) * filts + g // chans
    group_of = lambda c, f: f * chans + turn(f, c)
    need = [[[f for f in range(filts) if group_of(t, f) // filts == r] for r in range(chans)] for t in range(chans)]
    per = max(len(need[t][r]) for t in range(chans) for r in range(chans))
    pick = lambda t, r: [group_of(t, f) % filts for f in need[t][r]] + [0] * (per - len(need[t][r]))
    received = []
    for k in range(chans):
        table = jnp.array([pick((r + k) % chans, r) for r in range(chans)], jnp.int32)[chan]
        send = jnp.stack([lax.dynamic_slice_in_dim(grad_out, table[q] * rows, rows, 2) for q in range(per)])
        received.append(send if k == 0 else lax.ppermute(send, "chan", shift_pairs(chans, k)))
    received = jnp.concatenate(received)
    slot = [[0] * filts for _ in range(chans)]
    for t in range(chans):
        for k in range(chans):
            r = (t - k) % chans
            for q, f in enumerate(need[t][r]):
                slot[t][f] = k * per + q
    blocks = jnp.take(received, jnp.array(slot, jnp.int32)[chan], axis=0)
    all_filters = lax.all_to_all(blocks, "filt", 0, 0, tiled=True)
    return all_filters.reshape((-1,) + all_filters.shape[2:])


def backward_in(deep, weight, depth_weight):
    chans = lax.axis_size("chan")
    filts = lax.axis_size("filt")
    filt = lax.axis_index("filt")
    rows = deep.shape[2]
    turn = lambda f, r: r if f % 2 == 0 else chans - 1 - r
    place = lambda g: turn(g // chans, g % chans) * filts + g // chans
    grad_mid = depth_conv(deep, depth_weight[::-1], "DHWIO").astype(jnp.bfloat16)
    rimmed = halo(grad_mid, ROWS, 2, place)
    grad_in = plane_conv(rimmed, weight[::-1, ::-1], "HWOI").astype(jnp.bfloat16)
    chan = lax.axis_index("chan")
    c_loc = grad_in.shape[0] // chans
    even = filt % 2 == 0
    pieces = [grad_in[:c_loc]]
    for k in range(1, chans):
        target = jnp.where(even, (chan + k) % chans, (chan - k) % chans)
        pairs = [(c * filts + f, (((c + k) if f % 2 == 0 else (c - k)) % chans) * filts + f)
                 for c in range(chans) for f in range(filts)]
        at = (chan - target) % chans
        pieces.append(lax.ppermute(lax.dynamic_slice_in_dim(grad_in, at * c_loc, c_loc, 0), ROWS, pairs))
    return order_blocks(pieces, jnp.where(even, chan, chans - 1 - chan), 2)


def local(volume, plane_weight, depth_weight, grad_out):
    weight = gather_weight(plane_weight)
    mid = forward(volume, weight, depth_weight)
    all_filters = backward(grad_out, weight, depth_weight)
    deep = halo(jnp.concatenate([mid, all_filters]), "slab", 1)
    output = forward_out(deep[: mid.shape[0]], depth_weight)
    grad_in = backward_in(deep[mid.shape[0] :], weight, depth_weight)
    return (output, grad_in)


def solution(mesh):
    placed = (
        P("chan", "slab", None, None),
        P(None, None, "chan", "filt"),
        P(),
        P("filt", "slab", "chan", None),
    )
    return jax.shard_map(
        local,
        mesh=mesh,
        in_specs=placed,
        out_specs=(P("filt", "slab", "chan", None), P("chan", "slab", "filt", None)),
        check_vma=False,
    )
```

```python
import jax
import jax.numpy as jnp
from jax import lax
from jax.sharding import PartitionSpec as P

ROWS = ("chan", "filt")


def shift_pairs(n, k):
    return [(i, (i + k) % n) for i in range(n)]


def order_blocks(pieces, me, dim):
    n = len(pieces)
    if n == 1:
        return pieces[0]
    block = pieces[0].shape[dim]
    stacked = jnp.concatenate(pieces[::-1], axis=dim)
    return jnp.roll(stacked, (me + 1) * block, axis=dim)


def gather_blocks(x, axis, dim):
    n = lax.axis_size(axis)
    me = lax.axis_index(axis)
    pieces = [x] + [lax.ppermute(x, axis, shift_pairs(n, k)) for k in range(1, n)]
    return order_blocks(pieces, me, dim)


def scatter_blocks(x, axis, dim, gather_dim):
    n = lax.axis_size(axis)
    me = lax.axis_index(axis)
    size = x.shape[dim] // n
    take = lambda t: lax.dynamic_slice_in_dim(x, t * size, size, dim)
    pieces = [take(me)]
    for k in range(1, n):
        pieces.append(lax.ppermute(take((me + k) % n), axis, shift_pairs(n, k)))
    return order_blocks(pieces, me, gather_dim)


def halo(x, axis, dim, place=None):
    n = lax.axis_size(axis)
    place = place or (lambda i: i)
    up = [(place(i), place(i + 1)) for i in range(n - 1)]
    down = [(place(i + 1), place(i)) for i in range(n - 1)]
    length = x.shape[dim]
    before = lax.ppermute(lax.slice_in_dim(x, length - 1, length, axis=dim), axis, up)
    after = lax.ppermute(lax.slice_in_dim(x, 0, 1, axis=dim), axis, down)
    return jnp.concatenate([before, x, after], axis=dim)


def plane_conv(rows, weight, spec):
    return lax.conv_general_dilated(
        rows,
        weight,
        window_strides=(1, 1),
        padding=((0, 0), (1, 1)),
        dimension_numbers=("CNHW", spec, "CNHW"),
        preferred_element_type=jnp.float32,
    )


def depth_conv(padded, weight, spec):
    out = lax.conv_general_dilated(
        padded[None],
        weight[:, None, None],
        window_strides=(1, 1, 1),
        padding=((0, 0), (0, 0), (0, 0)),
        dimension_numbers=("NCDHW", spec, "NCDHW"),
        preferred_element_type=jnp.float32,
    )
    return out[0]


def gather_weight(weight):
    filts = lax.axis_size("filt")
    spread = jnp.broadcast_to(weight[None], (filts,) + weight.shape)
    by_filt = lax.all_to_all(spread, "filt", 0, 4, tiled=True)[0]
    return gather_blocks(by_filt, "chan", 2)


def sub_block(chan, filt, filts):
    return jnp.where(chan % 2 == 0, filt, filts - 1 - filt)


def sub_block_of(c, f, filts):
    return f if c % 2 == 0 else filts - 1 - f


def forward(volume, weight, depth_weight):
    chans = lax.axis_size("chan")
    filts = lax.axis_size("filt")
    chan = lax.axis_index("chan")
    filt = lax.axis_index("filt")
    rows = volume.shape[2] // (chans * filts)
    padded = jnp.pad(volume, ((0, 0), (0, 0), (1, 1), (0, 0)))
    window = lambda c: lax.dynamic_slice_in_dim(padded, (c * filts + filt) * rows, rows + 2, 2)
    pieces = [window(chan)]
    for k in range(1, chans):
        pieces.append(lax.ppermute(window((chan + k) % chans), "chan", shift_pairs(chans, k)))
    all_channels = order_blocks(pieces, chan, 0)
    return plane_conv(all_channels, weight, "HWIO").astype(jnp.bfloat16)


def forward_out(deep, depth_weight):
    chans = lax.axis_size("chan")
    filts = lax.axis_size("filt")
    chan = lax.axis_index("chan")
    rows = deep.shape[2]
    out = depth_conv(deep, depth_weight, "DHWOI").astype(jnp.bfloat16)
    return lax.all_to_all(out, "filt", 0, 2, tiled=True)


def grad_rows(grad_out):
    chans = lax.axis_size("chan")
    filts = lax.axis_size("filt")
    chan = lax.axis_index("chan")
    filt = lax.axis_index("filt")
    rows = grad_out.shape[2] // filts
    turn = lambda f, r: r if f % 2 == 0 else chans - 1 - r
    place = lambda g: turn(g // chans, g % chans) * filts + g // chans
    group_of = lambda c, f: f * chans + turn(f, c)
    need = [[[f for f in range(filts) if group_of(t, f) // filts == r] for r in range(chans)] for t in range(chans)]
    per = max(len(need[t][r]) for t in range(chans) for r in range(chans))
    pick = lambda t, r: [group_of(t, f) % filts for f in need[t][r]] + [0] * (per - len(need[t][r]))
    received = []
    for k in range(chans):
        table = jnp.array([pick((r + k) % chans, r) for r in range(chans)], jnp.int32)[chan]
        send = jnp.stack([lax.dynamic_slice_in_dim(grad_out, table[q] * rows, rows, 2) for q in range(per)])
        received.append(send if k == 0 else lax.ppermute(send, "chan", shift_pairs(chans, k)))
    return received


def grad_blocks(received):
    chans = lax.axis_size("chan")
    filts = lax.axis_size("filt")
    chan = lax.axis_index("chan")
    turn = lambda f, r: r if f % 2 == 0 else chans - 1 - r
    group_of = lambda c, f: f * chans + turn(f, c)
    need = [[[f for f in range(filts) if group_of(t, f) // filts == r] for r in range(chans)] for t in range(chans)]
    per = received[0].shape[0]
    received = jnp.concatenate(received)
    slot = [[0] * filts for _ in range(chans)]
    for t in range(chans):
        for k in range(chans):
            r = (t - k) % chans
            for q, f in enumerate(need[t][r]):
                slot[t][f] = k * per + q
    blocks = jnp.take(received, jnp.array(slot, jnp.int32)[chan], axis=0)
    all_filters = lax.all_to_all(blocks, "filt", 0, 0, tiled=True)
    return all_filters.reshape((-1,) + all_filters.shape[2:])


def backward_in(deep, weight, depth_weight):
    chans = lax.axis_size("chan")
    filts = lax.axis_size("filt")
    filt = lax.axis_index("filt")
    rows = deep.shape[2]
    turn = lambda f, r: r if f % 2 == 0 else chans - 1 - r
    place = lambda g: turn(g // chans, g % chans) * filts + g // chans
    grad_mid = depth_conv(deep, depth_weight[::-1], "DHWIO").astype(jnp.bfloat16)
    rimmed = halo(grad_mid, ROWS, 2, place)
    grad_in = plane_conv(rimmed, weight[::-1, ::-1], "HWOI").astype(jnp.bfloat16)
    chan = lax.axis_index("chan")
    c_loc = grad_in.shape[0] // chans
    even = filt % 2 == 0
    pieces = [lax.dynamic_slice_in_dim(grad_in, chan * c_loc, c_loc, 0)]
    for k in range(1, chans):
        target = jnp.where(even, (chan + k) % chans, (chan - k) % chans)
        pairs = [(c * filts + f, (((c + k) if f % 2 == 0 else (c - k)) % chans) * filts + f)
                 for c in range(chans) for f in range(filts)]
        pieces.append(lax.ppermute(lax.dynamic_slice_in_dim(grad_in, target * c_loc, c_loc, 0), ROWS, pairs))
    return order_blocks(pieces, jnp.where(even, chan, chans - 1 - chan), 2)


def local(volume, plane_weight, depth_weight, grad_out):
    weight = gather_weight(plane_weight)
    received = grad_rows(grad_out)
    volume, received = lax.optimization_barrier((volume, received))
    mid = forward(volume, weight, depth_weight)
    all_filters = grad_blocks(received)
    deep = halo(jnp.concatenate([mid, all_filters]), "slab", 1)
    output = forward_out(deep[: mid.shape[0]], depth_weight)
    grad_in = backward_in(deep[mid.shape[0] :], weight, depth_weight)
    return (output, grad_in)


def solution(mesh):
    placed = (
        P("chan", "slab", None, None),
        P(None, None, "chan", "filt"),
        P(),
        P("filt", "slab", "chan", None),
    )
    return jax.shard_map(
        local,
        mesh=mesh,
        in_specs=placed,
        out_specs=(P("filt", "slab", "chan", None), P("chan", "slab", "filt", None)),
        check_vma=False,
    )
```

```python
import jax
import jax.numpy as jnp
from jax import lax
from jax.sharding import PartitionSpec as P

ROWS = ("chan", "filt")


def shift_pairs(n, k):
    return [(i, (i + k) % n) for i in range(n)]


def order_blocks(pieces, me, dim):
    n = len(pieces)
    if n == 1:
        return pieces[0]
    block = pieces[0].shape[dim]
    stacked = jnp.concatenate(pieces[::-1], axis=dim)
    return jnp.roll(stacked, (me + 1) * block, axis=dim)


def gather_blocks(x, axis, dim):
    n = lax.axis_size(axis)
    me = lax.axis_index(axis)
    pieces = [x] + [lax.ppermute(x, axis, shift_pairs(n, k)) for k in range(1, n)]
    return order_blocks(pieces, me, dim)


def scatter_blocks(x, axis, dim, gather_dim):
    n = lax.axis_size(axis)
    me = lax.axis_index(axis)
    size = x.shape[dim] // n
    take = lambda t: lax.dynamic_slice_in_dim(x, t * size, size, dim)
    pieces = [take(me)]
    for k in range(1, n):
        pieces.append(lax.ppermute(take((me + k) % n), axis, shift_pairs(n, k)))
    return order_blocks(pieces, me, gather_dim)


def halo(x, axis, dim, place=None):
    n = lax.axis_size(axis)
    place = place or (lambda i: i)
    up = [(place(i), place(i + 1)) for i in range(n - 1)]
    down = [(place(i + 1), place(i)) for i in range(n - 1)]
    length = x.shape[dim]
    before = lax.ppermute(lax.slice_in_dim(x, length - 1, length, axis=dim), axis, up)
    after = lax.ppermute(lax.slice_in_dim(x, 0, 1, axis=dim), axis, down)
    return jnp.concatenate([before, x, after], axis=dim)


def plane_conv(rows, weight, spec):
    return lax.conv_general_dilated(
        rows,
        weight,
        window_strides=(1, 1),
        padding=((0, 0), (1, 1)),
        dimension_numbers=("CNHW", spec, "CNHW"),
        preferred_element_type=jnp.float32,
    )


def depth_conv(padded, weight, spec):
    out = lax.conv_general_dilated(
        padded[None],
        weight[:, None, None],
        window_strides=(1, 1, 1),
        padding=((0, 0), (0, 0), (0, 0)),
        dimension_numbers=("NCDHW", spec, "NCDHW"),
        preferred_element_type=jnp.float32,
    )
    return out[0]


def gather_weight(weight):
    filts = lax.axis_size("filt")
    chans = lax.axis_size("chan")
    slabs = lax.axis_size("slab")
    core = lax.axis_index("slab") % 2
    c_loc = weight.shape[2]
    half = c_loc // 2
    mine = lax.dynamic_slice_in_dim(weight, core * half, half, 2)
    spread = jnp.broadcast_to(mine[None], (filts,) + mine.shape)
    by_filt = gather_blocks(lax.all_to_all(spread, "filt", 0, 4, tiled=True)[0], "chan", 2)
    other = lax.ppermute(by_filt, "slab", [(i, i ^ 1) for i in range(slabs)])
    first = jnp.where(core == 0, by_filt, other)
    second = jnp.where(core == 0, other, by_filt)
    split = lambda w: w.reshape(3, 3, chans, 1, half, w.shape[-1])
    whole = jnp.concatenate([split(first), split(second)], axis=3)
    return whole.reshape(3, 3, chans * c_loc, whole.shape[-1])


def sub_block(chan, filt, filts):
    return jnp.where(chan % 2 == 0, filt, filts - 1 - filt)


def sub_block_of(c, f, filts):
    return f if c % 2 == 0 else filts - 1 - f


def forward(volume, weight, depth_weight):
    chans = lax.axis_size("chan")
    filts = lax.axis_size("filt")
    chan = lax.axis_index("chan")
    filt = lax.axis_index("filt")
    rows = volume.shape[2] // (chans * filts)
    padded = jnp.pad(volume, ((0, 0), (0, 0), (1, 1), (0, 0)))
    window = lambda c: lax.dynamic_slice_in_dim(padded, (c * filts + filt) * rows, rows + 2, 2)
    pieces = [window(chan)]
    for k in range(1, chans):
        pieces.append(lax.ppermute(window((chan + k) % chans), "chan", shift_pairs(chans, k)))
    all_channels = order_blocks(pieces, chan, 0)
    return plane_conv(all_channels, weight, "HWIO").astype(jnp.bfloat16)


def forward_out(deep, depth_weight):
    chans = lax.axis_size("chan")
    filts = lax.axis_size("filt")
    chan = lax.axis_index("chan")
    rows = deep.shape[2]
    out = depth_conv(deep, depth_weight, "DHWOI").astype(jnp.bfloat16)
    return lax.all_to_all(out, "filt", 0, 2, tiled=True)


def backward(grad_out, weight, depth_weight):
    chans = lax.axis_size("chan")
    filts = lax.axis_size("filt")
    chan = lax.axis_index("chan")
    filt = lax.axis_index("filt")
    rows = grad_out.shape[2] // filts
    turn = lambda f, r: r if f % 2 == 0 else chans - 1 - r
    place = lambda g: turn(g // chans, g % chans) * filts + g // chans
    group_of = lambda c, f: f * chans + turn(f, c)
    need = [[[f for f in range(filts) if group_of(t, f) // filts == r] for r in range(chans)] for t in range(chans)]
    per = max(len(need[t][r]) for t in range(chans) for r in range(chans))
    pick = lambda t, r: [group_of(t, f) % filts for f in need[t][r]] + [0] * (per - len(need[t][r]))
    received = []
    for k in range(chans):
        table = jnp.array([pick((r + k) % chans, r) for r in range(chans)], jnp.int32)[chan]
        send = jnp.stack([lax.dynamic_slice_in_dim(grad_out, table[q] * rows, rows, 2) for q in range(per)])
        received.append(send if k == 0 else lax.ppermute(send, "chan", shift_pairs(chans, k)))
    received = jnp.concatenate(received)
    slot = [[0] * filts for _ in range(chans)]
    for t in range(chans):
        for k in range(chans):
            r = (t - k) % chans
            for q, f in enumerate(need[t][r]):
                slot[t][f] = k * per + q
    blocks = jnp.take(received, jnp.array(slot, jnp.int32)[chan], axis=0)
    all_filters = lax.all_to_all(blocks, "filt", 0, 0, tiled=True)
    return all_filters.reshape((-1,) + all_filters.shape[2:])


def backward_in(deep, weight, depth_weight):
    chans = lax.axis_size("chan")
    filts = lax.axis_size("filt")
    filt = lax.axis_index("filt")
    rows = deep.shape[2]
    turn = lambda f, r: r if f % 2 == 0 else chans - 1 - r
    place = lambda g: turn(g // chans, g % chans) * filts + g // chans
    grad_mid = depth_conv(deep, depth_weight[::-1], "DHWIO").astype(jnp.bfloat16)
    rimmed = halo(grad_mid, ROWS, 2, place)
    grad_in = plane_conv(rimmed, weight[::-1, ::-1], "HWOI").astype(jnp.bfloat16)
    chan = lax.axis_index("chan")
    c_loc = grad_in.shape[0] // chans
    even = filt % 2 == 0
    pieces = [lax.dynamic_slice_in_dim(grad_in, chan * c_loc, c_loc, 0)]
    for k in range(1, chans):
        target = jnp.where(even, (chan + k) % chans, (chan - k) % chans)
        pairs = [(c * filts + f, (((c + k) if f % 2 == 0 else (c - k)) % chans) * filts + f)
                 for c in range(chans) for f in range(filts)]
        pieces.append(lax.ppermute(lax.dynamic_slice_in_dim(grad_in, target * c_loc, c_loc, 0), ROWS, pairs))
    return order_blocks(pieces, jnp.where(even, chan, chans - 1 - chan), 2)


def local(volume, plane_weight, depth_weight, grad_out):
    weight = gather_weight(plane_weight)
    mid = forward(volume, weight, depth_weight)
    all_filters = backward(grad_out, weight, depth_weight)
    deep = halo(jnp.concatenate([mid, all_filters]), "slab", 1)
    output = forward_out(deep[: mid.shape[0]], depth_weight)
    grad_in = backward_in(deep[mid.shape[0] :], weight, depth_weight)
    return (output, grad_in)


def solution(mesh):
    placed = (
        P("chan", "slab", None, None),
        P(None, None, "chan", "filt"),
        P(),
        P("filt", "slab", "chan", None),
    )
    return jax.shard_map(
        local,
        mesh=mesh,
        in_specs=placed,
        out_specs=(P("filt", "slab", "chan", None), P("chan", "slab", "filt", None)),
        check_vma=False,
    )
```

```python
import jax
import jax.numpy as jnp
from jax import lax
from jax.sharding import PartitionSpec as P

ROWS = ("chan", "filt")


def shift_pairs(n, k):
    return [(i, (i + k) % n) for i in range(n)]


def order_blocks(pieces, me, dim):
    n = len(pieces)
    if n == 1:
        return pieces[0]
    block = pieces[0].shape[dim]
    stacked = jnp.concatenate(pieces[::-1], axis=dim)
    return jnp.roll(stacked, (me + 1) * block, axis=dim)


def gather_blocks(x, axis, dim):
    n = lax.axis_size(axis)
    me = lax.axis_index(axis)
    pieces = [x] + [lax.ppermute(x, axis, shift_pairs(n, k)) for k in range(1, n)]
    return order_blocks(pieces, me, dim)


def scatter_blocks(x, axis, dim, gather_dim):
    n = lax.axis_size(axis)
    me = lax.axis_index(axis)
    size = x.shape[dim] // n
    take = lambda t: lax.dynamic_slice_in_dim(x, t * size, size, dim)
    pieces = [take(me)]
    for k in range(1, n):
        pieces.append(lax.ppermute(take((me + k) % n), axis, shift_pairs(n, k)))
    return order_blocks(pieces, me, gather_dim)


def halo(x, axis, dim, place=None):
    n = lax.axis_size(axis)
    place = place or (lambda i: i)
    up = [(place(i), place(i + 1)) for i in range(n - 1)]
    down = [(place(i + 1), place(i)) for i in range(n - 1)]
    length = x.shape[dim]
    before = lax.ppermute(lax.slice_in_dim(x, length - 1, length, axis=dim), axis, up)
    after = lax.ppermute(lax.slice_in_dim(x, 0, 1, axis=dim), axis, down)
    return jnp.concatenate([before, x, after], axis=dim)


def plane_conv(rows, weight, spec):
    return lax.conv_general_dilated(
        rows,
        weight,
        window_strides=(1, 1),
        padding=((0, 0), (1, 1)),
        dimension_numbers=("CNHW", spec, "CNHW"),
        preferred_element_type=jnp.float32,
    )


def depth_conv(padded, weight, spec):
    out = lax.conv_general_dilated(
        padded[None],
        weight[:, None, None],
        window_strides=(1, 1, 1),
        padding=((0, 0), (0, 0), (0, 0)),
        dimension_numbers=("NCDHW", spec, "NCDHW"),
        preferred_element_type=jnp.float32,
    )
    return out[0]


def gather_weight(weight):
    filts = lax.axis_size("filt")
    chans = lax.axis_size("chan")
    slabs = lax.axis_size("slab")
    core = lax.axis_index("slab") % 2
    c_loc = weight.shape[2]
    half = c_loc // 2
    mine = lax.dynamic_slice_in_dim(weight, core * half, half, 2)
    spread = jnp.broadcast_to(mine[None], (filts,) + mine.shape)
    by_filt = gather_blocks(lax.all_to_all(spread, "filt", 0, 4, tiled=True)[0], "chan", 2)
    other = lax.ppermute(by_filt, "slab", [(i, i ^ 1) for i in range(slabs)])
    first = jnp.where(core == 0, by_filt, other)
    second = jnp.where(core == 0, other, by_filt)
    split = lambda w: w.reshape(3, 3, chans, 1, half, w.shape[-1])
    whole = jnp.concatenate([split(first), split(second)], axis=3)
    return whole.reshape(3, 3, chans * c_loc, whole.shape[-1])


def sub_block(chan, filt, filts):
    return jnp.where(chan % 2 == 0, filt, filts - 1 - filt)


def sub_block_of(c, f, filts):
    return f if c % 2 == 0 else filts - 1 - f


def forward(volume, weight, depth_weight):
    chans = lax.axis_size("chan")
    filts = lax.axis_size("filt")
    chan = lax.axis_index("chan")
    filt = lax.axis_index("filt")
    rows = volume.shape[2] // (chans * filts)
    padded = jnp.pad(volume, ((0, 0), (0, 0), (1, 1), (0, 0)))
    window = lambda c: lax.dynamic_slice_in_dim(padded, (c * filts + filt) * rows, rows + 2, 2)
    pieces = [window(chan)]
    for k in range(1, chans):
        pieces.append(lax.ppermute(window((chan + k) % chans), "chan", shift_pairs(chans, k)))
    all_channels = order_blocks(pieces, chan, 0)
    return plane_conv(all_channels, weight, "HWIO").astype(jnp.bfloat16)


def forward_out(deep, depth_weight):
    chans = lax.axis_size("chan")
    filts = lax.axis_size("filt")
    chan = lax.axis_index("chan")
    rows = deep.shape[2]
    out = depth_conv(deep, depth_weight, "DHWOI").astype(jnp.bfloat16)
    return lax.all_to_all(out, "filt", 0, 2, tiled=True)


def grad_rows(grad_out):
    chans = lax.axis_size("chan")
    filts = lax.axis_size("filt")
    chan = lax.axis_index("chan")
    filt = lax.axis_index("filt")
    rows = grad_out.shape[2] // filts
    turn = lambda f, r: r if f % 2 == 0 else chans - 1 - r
    place = lambda g: turn(g // chans, g % chans) * filts + g // chans
    group_of = lambda c, f: f * chans + turn(f, c)
    need = [[[f for f in range(filts) if group_of(t, f) // filts == r] for r in range(chans)] for t in range(chans)]
    per = max(len(need[t][r]) for t in range(chans) for r in range(chans))
    pick = lambda t, r: [group_of(t, f) % filts for f in need[t][r]] + [0] * (per - len(need[t][r]))
    received = []
    for k in range(chans):
        table = jnp.array([pick((r + k) % chans, r) for r in range(chans)], jnp.int32)[chan]
        send = jnp.stack([lax.dynamic_slice_in_dim(grad_out, table[q] * rows, rows, 2) for q in range(per)])
        received.append(send if k == 0 else lax.ppermute(send, "chan", shift_pairs(chans, k)))
    return received


def grad_blocks(received):
    chans = lax.axis_size("chan")
    filts = lax.axis_size("filt")
    chan = lax.axis_index("chan")
    turn = lambda f, r: r if f % 2 == 0 else chans - 1 - r
    group_of = lambda c, f: f * chans + turn(f, c)
    need = [[[f for f in range(filts) if group_of(t, f) // filts == r] for r in range(chans)] for t in range(chans)]
    per = received[0].shape[0]
    received = jnp.concatenate(received)
    slot = [[0] * filts for _ in range(chans)]
    for t in range(chans):
        for k in range(chans):
            r = (t - k) % chans
            for q, f in enumerate(need[t][r]):
                slot[t][f] = k * per + q
    blocks = jnp.take(received, jnp.array(slot, jnp.int32)[chan], axis=0)
    all_filters = lax.all_to_all(blocks, "filt", 0, 0, tiled=True)
    return all_filters.reshape((-1,) + all_filters.shape[2:])


def backward_in(deep, weight, depth_weight):
    chans = lax.axis_size("chan")
    filts = lax.axis_size("filt")
    filt = lax.axis_index("filt")
    rows = deep.shape[2]
    turn = lambda f, r: r if f % 2 == 0 else chans - 1 - r
    place = lambda g: turn(g // chans, g % chans) * filts + g // chans
    grad_mid = depth_conv(deep, depth_weight[::-1], "DHWIO").astype(jnp.bfloat16)
    rimmed = halo(grad_mid, ROWS, 2, place)
    grad_in = plane_conv(rimmed, weight[::-1, ::-1], "HWOI").astype(jnp.bfloat16)
    chan = lax.axis_index("chan")
    c_loc = grad_in.shape[0] // chans
    even = filt % 2 == 0
    pieces = [lax.dynamic_slice_in_dim(grad_in, chan * c_loc, c_loc, 0)]
    for k in range(1, chans):
        target = jnp.where(even, (chan + k) % chans, (chan - k) % chans)
        pairs = [(c * filts + f, (((c + k) if f % 2 == 0 else (c - k)) % chans) * filts + f)
                 for c in range(chans) for f in range(filts)]
        pieces.append(lax.ppermute(lax.dynamic_slice_in_dim(grad_in, target * c_loc, c_loc, 0), ROWS, pairs))
    return order_blocks(pieces, jnp.where(even, chan, chans - 1 - chan), 2)


def local(volume, plane_weight, depth_weight, grad_out):
    received = grad_rows(grad_out)
    volume, received = lax.optimization_barrier((volume, received))
    all_filters = grad_blocks(received)
    plane_weight, all_filters = lax.optimization_barrier((plane_weight, all_filters))
    weight = gather_weight(plane_weight)
    mid = forward(volume, weight, depth_weight)
    deep = halo(jnp.concatenate([mid, all_filters]), "slab", 1)
    output = forward_out(deep[: mid.shape[0]], depth_weight)
    grad_in = backward_in(deep[mid.shape[0] :], weight, depth_weight)
    return (output, grad_in)


def solution(mesh):
    placed = (
        P("chan", "slab", None, None),
        P(None, None, "chan", "filt"),
        P(),
        P("filt", "slab", "chan", None),
    )
    return jax.shard_map(
        local,
        mesh=mesh,
        in_specs=placed,
        out_specs=(P("filt", "slab", "chan", None), P("chan", "slab", "filt", None)),
        check_vma=False,
    )
```

```python
import jax
import jax.numpy as jnp
from jax import lax
from jax.sharding import PartitionSpec as P

ROWS = ("chan", "filt")


def shift_pairs(n, k):
    return [(i, (i + k) % n) for i in range(n)]


def order_blocks(pieces, me, dim):
    n = len(pieces)
    if n == 1:
        return pieces[0]
    block = pieces[0].shape[dim]
    stacked = jnp.concatenate(pieces[::-1], axis=dim)
    return jnp.roll(stacked, (me + 1) * block, axis=dim)


def gather_blocks(x, axis, dim):
    n = lax.axis_size(axis)
    me = lax.axis_index(axis)
    pieces = [x] + [lax.ppermute(x, axis, shift_pairs(n, k)) for k in range(1, n)]
    return order_blocks(pieces, me, dim)


def scatter_blocks(x, axis, dim, gather_dim):
    n = lax.axis_size(axis)
    me = lax.axis_index(axis)
    size = x.shape[dim] // n
    take = lambda t: lax.dynamic_slice_in_dim(x, t * size, size, dim)
    pieces = [take(me)]
    for k in range(1, n):
        pieces.append(lax.ppermute(take((me + k) % n), axis, shift_pairs(n, k)))
    return order_blocks(pieces, me, gather_dim)


def halo(x, axis, dim, place=None):
    n = lax.axis_size(axis)
    place = place or (lambda i: i)
    up = [(place(i), place(i + 1)) for i in range(n - 1)]
    down = [(place(i + 1), place(i)) for i in range(n - 1)]
    length = x.shape[dim]
    before = lax.ppermute(lax.slice_in_dim(x, length - 1, length, axis=dim), axis, up)
    after = lax.ppermute(lax.slice_in_dim(x, 0, 1, axis=dim), axis, down)
    return jnp.concatenate([before, x, after], axis=dim)


def plane_conv(rows, weight, spec):
    return lax.conv_general_dilated(
        rows,
        weight,
        window_strides=(1, 1),
        padding=((0, 0), (1, 1)),
        dimension_numbers=("CNHW", spec, "CNHW"),
        preferred_element_type=jnp.float32,
    )


def depth_conv(padded, weight, spec):
    out = lax.conv_general_dilated(
        padded[None],
        weight[:, None, None],
        window_strides=(1, 1, 1),
        padding=((0, 0), (0, 0), (0, 0)),
        dimension_numbers=("NCDHW", spec, "NCDHW"),
        preferred_element_type=jnp.float32,
    )
    return out[0]


def gather_weight(weight):
    filts = lax.axis_size("filt")
    chans = lax.axis_size("chan")
    slabs = lax.axis_size("slab")
    core = lax.axis_index("slab") % 2
    c_loc = weight.shape[2]
    half = c_loc // 2
    mine = lax.dynamic_slice_in_dim(weight, core * half, half, 2)
    spread = jnp.broadcast_to(mine[None], (filts,) + mine.shape)
    by_filt = gather_blocks(lax.all_to_all(spread, "filt", 0, 4, tiled=True)[0], "chan", 2)
    other = lax.ppermute(by_filt, "slab", [(i, i ^ 1) for i in range(slabs)])
    first = jnp.where(core == 0, by_filt, other)
    second = jnp.where(core == 0, other, by_filt)
    split = lambda w: w.reshape(3, 3, chans, 1, half, w.shape[-1])
    whole = jnp.concatenate([split(first), split(second)], axis=3)
    return whole.reshape(3, 3, chans * c_loc, whole.shape[-1])


def sub_block(chan, filt, filts):
    return jnp.where(chan % 2 == 0, filt, filts - 1 - filt)


def sub_block_of(c, f, filts):
    return f if c % 2 == 0 else filts - 1 - f


def forward(volume, weight, depth_weight):
    chans = lax.axis_size("chan")
    filts = lax.axis_size("filt")
    chan = lax.axis_index("chan")
    filt = lax.axis_index("filt")
    rows = volume.shape[2] // (chans * filts)
    padded = jnp.pad(volume, ((0, 0), (0, 0), (1, 1), (0, 0)))
    window = lambda c: lax.dynamic_slice_in_dim(padded, (c * filts + filt) * rows, rows + 2, 2)
    pieces = [window(chan)]
    for k in range(1, chans):
        pieces.append(lax.ppermute(window((chan + k) % chans), "chan", shift_pairs(chans, k)))
    all_channels = order_blocks(pieces, chan, 0)
    return plane_conv(all_channels, weight, "HWIO").astype(jnp.bfloat16)


def forward_out(deep, depth_weight):
    chans = lax.axis_size("chan")
    filts = lax.axis_size("filt")
    chan = lax.axis_index("chan")
    rows = deep.shape[2]
    out = depth_conv(deep, depth_weight, "DHWOI").astype(jnp.bfloat16)
    return lax.all_to_all(out, "filt", 0, 2, tiled=True)


def backward(grad_out, weight, depth_weight):
    chans = lax.axis_size("chan")
    filts = lax.axis_size("filt")
    chan = lax.axis_index("chan")
    filt = lax.axis_index("filt")
    rows = grad_out.shape[2] // filts
    turn = lambda f, r: r if f % 2 == 0 else chans - 1 - r
    place = lambda g: turn(g // chans, g % chans) * filts + g // chans
    group_of = lambda c, f: f * chans + turn(f, c)
    need = [[[f for f in range(filts) if group_of(t, f) // filts == r] for r in range(chans)] for t in range(chans)]
    per = max(len(need[t][r]) for t in range(chans) for r in range(chans))
    pick = lambda t, r: [group_of(t, f) % filts for f in need[t][r]] + [0] * (per - len(need[t][r]))
    received = []
    for k in range(chans):
        table = jnp.array([pick((r + k) % chans, r) for r in range(chans)], jnp.int32)[chan]
        send = jnp.stack([lax.dynamic_slice_in_dim(grad_out, table[q] * rows, rows, 2) for q in range(per)])
        received.append(send if k == 0 else lax.ppermute(send, "chan", shift_pairs(chans, k)))
    received = jnp.concatenate(received)
    slot = [[0] * filts for _ in range(chans)]
    for t in range(chans):
        for k in range(chans):
            r = (t - k) % chans
            for q, f in enumerate(need[t][r]):
                slot[t][f] = k * per + q
    blocks = jnp.take(received, jnp.array(slot, jnp.int32)[chan], axis=0)
    all_filters = lax.all_to_all(blocks, "filt", 0, 0, tiled=True)
    return all_filters.reshape((-1,) + all_filters.shape[2:])


def backward_in(deep, weight, depth_weight):
    chans = lax.axis_size("chan")
    filts = lax.axis_size("filt")
    filt = lax.axis_index("filt")
    rows = deep.shape[2]
    turn = lambda f, r: r if f % 2 == 0 else chans - 1 - r
    place = lambda g: turn(g // chans, g % chans) * filts + g // chans
    grad_mid = depth_conv(deep, depth_weight[::-1], "DHWIO").astype(jnp.bfloat16)
    rimmed = halo(grad_mid, ROWS, 2, place)
    grad_in = plane_conv(rimmed, weight[::-1, ::-1], "HWOI").astype(jnp.bfloat16)
    chan = lax.axis_index("chan")
    c_loc = grad_in.shape[0] // chans
    even = filt % 2 == 0
    pieces = [lax.dynamic_slice_in_dim(grad_in, chan * c_loc, c_loc, 0)]
    for k in range(1, chans):
        target = jnp.where(even, (chan + k) % chans, (chan - k) % chans)
        pairs = [(c * filts + f, (((c + k) if f % 2 == 0 else (c - k)) % chans) * filts + f)
                 for c in range(chans) for f in range(filts)]
        pieces.append(lax.ppermute(lax.dynamic_slice_in_dim(grad_in, target * c_loc, c_loc, 0), ROWS, pairs))
    return order_blocks(pieces, jnp.where(even, chan, chans - 1 - chan), 2)


def local(volume, plane_weight, depth_weight, grad_out):
    weight = gather_weight(plane_weight)
    mid = forward(volume, weight, depth_weight)
    all_filters = backward(grad_out, weight, depth_weight)
    output = forward_out(halo(mid, "slab", 1), depth_weight)
    grad_in = backward_in(halo(all_filters, "slab", 1), weight, depth_weight)
    return (output, grad_in)


def solution(mesh):
    placed = (
        P("chan", "slab", None, None),
        P(None, None, "chan", "filt"),
        P(),
        P("filt", "slab", "chan", None),
    )
    return jax.shard_map(
        local,
        mesh=mesh,
        in_specs=placed,
        out_specs=(P("filt", "slab", "chan", None), P("chan", "slab", "filt", None)),
        check_vma=False,
    )
```

```python
import jax
import jax.numpy as jnp
from jax import lax
from jax.sharding import PartitionSpec as P

ROWS = ("chan", "filt")


def shift_pairs(n, k):
    return [(i, (i + k) % n) for i in range(n)]


def order_blocks(pieces, me, dim):
    n = len(pieces)
    if n == 1:
        return pieces[0]
    block = pieces[0].shape[dim]
    stacked = jnp.concatenate(pieces[::-1], axis=dim)
    return jnp.roll(stacked, (me + 1) * block, axis=dim)


def gather_blocks(x, axis, dim):
    n = lax.axis_size(axis)
    me = lax.axis_index(axis)
    pieces = [x] + [lax.ppermute(x, axis, shift_pairs(n, k)) for k in range(1, n)]
    return order_blocks(pieces, me, dim)


def scatter_blocks(x, axis, dim, gather_dim):
    n = lax.axis_size(axis)
    me = lax.axis_index(axis)
    size = x.shape[dim] // n
    take = lambda t: lax.dynamic_slice_in_dim(x, t * size, size, dim)
    pieces = [take(me)]
    for k in range(1, n):
        pieces.append(lax.ppermute(take((me + k) % n), axis, shift_pairs(n, k)))
    return order_blocks(pieces, me, gather_dim)


def halo(x, axis, dim, place=None):
    n = lax.axis_size(axis)
    place = place or (lambda i: i)
    up = [(place(i), place(i + 1)) for i in range(n - 1)]
    down = [(place(i + 1), place(i)) for i in range(n - 1)]
    length = x.shape[dim]
    before = lax.ppermute(lax.slice_in_dim(x, length - 1, length, axis=dim), axis, up)
    after = lax.ppermute(lax.slice_in_dim(x, 0, 1, axis=dim), axis, down)
    return jnp.concatenate([before, x, after], axis=dim)


def plane_conv(rows, weight, spec):
    return lax.conv_general_dilated(
        rows,
        weight,
        window_strides=(1, 1),
        padding=((0, 0), (1, 1)),
        dimension_numbers=("CNHW", spec, "CNHW"),
        preferred_element_type=jnp.float32,
    )


def depth_conv(padded, weight, spec):
    out = lax.conv_general_dilated(
        padded[None],
        weight[:, None, None],
        window_strides=(1, 1, 1),
        padding=((0, 0), (0, 0), (0, 0)),
        dimension_numbers=("NCDHW", spec, "NCDHW"),
        preferred_element_type=jnp.float32,
    )
    return out[0]


def gather_weight(weight):
    filts = lax.axis_size("filt")
    chans = lax.axis_size("chan")
    slabs = lax.axis_size("slab")
    core = lax.axis_index("slab") % 2
    c_loc = weight.shape[2]
    half = c_loc // 2
    mine = lax.dynamic_slice_in_dim(weight, core * half, half, 2)
    spread = jnp.broadcast_to(mine[None], (filts,) + mine.shape)
    by_filt = lax.all_to_all(spread, "filt", 0, 4, tiled=True)[0]
    other = lax.ppermute(by_filt, "slab", [(i, i ^ 1) for i in range(slabs)])
    first = jnp.where(core == 0, by_filt, other)
    second = jnp.where(core == 0, other, by_filt)
    return jnp.concatenate([first, second], axis=2)


def sub_block(chan, filt, filts):
    return jnp.where(chan % 2 == 0, filt, filts - 1 - filt)


def sub_block_of(c, f, filts):
    return f if c % 2 == 0 else filts - 1 - f


def forward(volume, local_weight):
    chans = lax.axis_size("chan")
    filts = lax.axis_size("filt")
    chan = lax.axis_index("chan")
    filt = lax.axis_index("filt")
    rows = volume.shape[2] // (chans * filts)
    padded = jnp.pad(volume, ((0, 0), (0, 0), (1, 1), (0, 0)))
    window = lambda c: lax.dynamic_slice_in_dim(padded, (c * filts + filt) * rows, rows + 2, 2)
    pieces, kernels = [window(chan)], [local_weight]
    for k in range(1, chans):
        a = window((chan + k) % chans)
        tile = a[0].size
        if local_weight.size % tile == 0:
            both = jnp.concatenate([a, local_weight.reshape((-1,) + a.shape[1:])], axis=0)
            both = lax.ppermute(both, "chan", shift_pairs(chans, k))
            pieces.append(both[: a.shape[0]])
            kernels.append(both[a.shape[0] :].reshape(local_weight.shape))
        else:
            pieces.append(lax.ppermute(a, "chan", shift_pairs(chans, k)))
            kernels.append(lax.ppermute(local_weight, "chan", shift_pairs(chans, k)))
    weight = order_blocks(kernels, chan, 2)
    all_channels = order_blocks(pieces, chan, 0)
    return plane_conv(all_channels, weight, "HWIO").astype(jnp.bfloat16), weight


def forward_out(deep, depth_weight):
    chans = lax.axis_size("chan")
    filts = lax.axis_size("filt")
    chan = lax.axis_index("chan")
    rows = deep.shape[2]
    out = depth_conv(deep, depth_weight, "DHWOI").astype(jnp.bfloat16)
    return lax.all_to_all(out, "filt", 0, 2, tiled=True)


def backward(grad_out, weight, depth_weight):
    chans = lax.axis_size("chan")
    filts = lax.axis_size("filt")
    chan = lax.axis_index("chan")
    filt = lax.axis_index("filt")
    rows = grad_out.shape[2] // filts
    turn = lambda f, r: r if f % 2 == 0 else chans - 1 - r
    place = lambda g: turn(g // chans, g % chans) * filts + g // chans
    group_of = lambda c, f: f * chans + turn(f, c)
    need = [[[f for f in range(filts) if group_of(t, f) // filts == r] for r in range(chans)] for t in range(chans)]
    per = max(len(need[t][r]) for t in range(chans) for r in range(chans))
    pick = lambda t, r: [group_of(t, f) % filts for f in need[t][r]] + [0] * (per - len(need[t][r]))
    received = []
    for k in range(chans):
        table = jnp.array([pick((r + k) % chans, r) for r in range(chans)], jnp.int32)[chan]
        send = jnp.stack([lax.dynamic_slice_in_dim(grad_out, table[q] * rows, rows, 2) for q in range(per)])
        received.append(send if k == 0 else lax.ppermute(send, "chan", shift_pairs(chans, k)))
    received = jnp.concatenate(received)
    slot = [[0] * filts for _ in range(chans)]
    for t in range(chans):
        for k in range(chans):
            r = (t - k) % chans
            for q, f in enumerate(need[t][r]):
                slot[t][f] = k * per + q
    blocks = jnp.take(received, jnp.array(slot, jnp.int32)[chan], axis=0)
    all_filters = lax.all_to_all(blocks, "filt", 0, 0, tiled=True)
    return all_filters.reshape((-1,) + all_filters.shape[2:])


def backward_in(deep, weight, depth_weight):
    chans = lax.axis_size("chan")
    filts = lax.axis_size("filt")
    filt = lax.axis_index("filt")
    rows = deep.shape[2]
    turn = lambda f, r: r if f % 2 == 0 else chans - 1 - r
    place = lambda g: turn(g // chans, g % chans) * filts + g // chans
    grad_mid = depth_conv(deep, depth_weight[::-1], "DHWIO").astype(jnp.bfloat16)
    rimmed = halo(grad_mid, ROWS, 2, place)
    grad_in = plane_conv(rimmed, weight[::-1, ::-1], "HWOI").astype(jnp.bfloat16)
    chan = lax.axis_index("chan")
    c_loc = grad_in.shape[0] // chans
    even = filt % 2 == 0
    pieces = [lax.dynamic_slice_in_dim(grad_in, chan * c_loc, c_loc, 0)]
    for k in range(1, chans):
        target = jnp.where(even, (chan + k) % chans, (chan - k) % chans)
        pairs = [(c * filts + f, (((c + k) if f % 2 == 0 else (c - k)) % chans) * filts + f)
                 for c in range(chans) for f in range(filts)]
        pieces.append(lax.ppermute(lax.dynamic_slice_in_dim(grad_in, target * c_loc, c_loc, 0), ROWS, pairs))
    return order_blocks(pieces, jnp.where(even, chan, chans - 1 - chan), 2)


def local(volume, plane_weight, depth_weight, grad_out):
    weight = gather_weight(plane_weight)
    mid, weight = forward(volume, weight)
    all_filters = backward(grad_out, weight, depth_weight)
    deep = halo(jnp.concatenate([mid, all_filters]), "slab", 1)
    output = forward_out(deep[: mid.shape[0]], depth_weight)
    grad_in = backward_in(deep[mid.shape[0] :], weight, depth_weight)
    return (output, grad_in)


def solution(mesh):
    placed = (
        P("chan", "slab", None, None),
        P(None, None, "chan", "filt"),
        P(),
        P("filt", "slab", "chan", None),
    )
    return jax.shard_map(
        local,
        mesh=mesh,
        in_specs=placed,
        out_specs=(P("filt", "slab", "chan", None), P("chan", "slab", "filt", None)),
        check_vma=False,
    )
```

```python
import jax
import jax.numpy as jnp
from jax import lax
from jax.sharding import PartitionSpec as P

ROWS = ("chan", "filt")


def shift_pairs(n, k):
    return [(i, (i + k) % n) for i in range(n)]


def order_blocks(pieces, me, dim):
    n = len(pieces)
    if n == 1:
        return pieces[0]
    block = pieces[0].shape[dim]
    stacked = jnp.concatenate(pieces[::-1], axis=dim)
    return jnp.roll(stacked, (me + 1) * block, axis=dim)


def gather_blocks(x, axis, dim):
    n = lax.axis_size(axis)
    me = lax.axis_index(axis)
    pieces = [x] + [lax.ppermute(x, axis, shift_pairs(n, k)) for k in range(1, n)]
    return order_blocks(pieces, me, dim)


def scatter_blocks(x, axis, dim, gather_dim):
    n = lax.axis_size(axis)
    me = lax.axis_index(axis)
    size = x.shape[dim] // n
    take = lambda t: lax.dynamic_slice_in_dim(x, t * size, size, dim)
    pieces = [take(me)]
    for k in range(1, n):
        pieces.append(lax.ppermute(take((me + k) % n), axis, shift_pairs(n, k)))
    return order_blocks(pieces, me, gather_dim)


def halo(x, axis, dim, place=None):
    n = lax.axis_size(axis)
    place = place or (lambda i: i)
    up = [(place(i), place(i + 1)) for i in range(n - 1)]
    down = [(place(i + 1), place(i)) for i in range(n - 1)]
    length = x.shape[dim]
    before = lax.ppermute(lax.slice_in_dim(x, length - 1, length, axis=dim), axis, up)
    after = lax.ppermute(lax.slice_in_dim(x, 0, 1, axis=dim), axis, down)
    return jnp.concatenate([before, x, after], axis=dim)


def plane_conv(rows, weight, spec):
    return lax.conv_general_dilated(
        rows,
        weight,
        window_strides=(1, 1),
        padding=((0, 0), (1, 1)),
        dimension_numbers=("CNHW", spec, "CNHW"),
        preferred_element_type=jnp.float32,
    )


def depth_conv(padded, weight, spec):
    out = lax.conv_general_dilated(
        padded[None],
        weight[:, None, None],
        window_strides=(1, 1, 1),
        padding=((0, 0), (0, 0), (0, 0)),
        dimension_numbers=("NCDHW", spec, "NCDHW"),
        preferred_element_type=jnp.float32,
    )
    return out[0]


def finish_weight(weight):
    filts = lax.axis_size("filt")
    chans = lax.axis_size("chan")
    slabs = lax.axis_size("slab")
    core = lax.axis_index("slab") % 2
    half = weight.shape[2]
    c_loc = 2 * half
    by_filt = gather_blocks(weight, "chan", 2)
    other = lax.ppermute(by_filt, "slab", [(i, i ^ 1) for i in range(slabs)])
    first = jnp.where(core == 0, by_filt, other)
    second = jnp.where(core == 0, other, by_filt)
    split = lambda w: w.reshape(3, 3, chans, 1, half, w.shape[-1])
    whole = jnp.concatenate([split(first), split(second)], axis=3)
    return whole.reshape(3, 3, chans * c_loc, whole.shape[-1])


def sub_block(chan, filt, filts):
    return jnp.where(chan % 2 == 0, filt, filts - 1 - filt)


def sub_block_of(c, f, filts):
    return f if c % 2 == 0 else filts - 1 - f


def forward(volume, weight, depth_weight):
    chans = lax.axis_size("chan")
    filts = lax.axis_size("filt")
    chan = lax.axis_index("chan")
    filt = lax.axis_index("filt")
    rows = volume.shape[2] // (chans * filts)
    padded = jnp.pad(volume, ((0, 0), (0, 0), (1, 1), (0, 0)))
    window = lambda c: lax.dynamic_slice_in_dim(padded, (c * filts + filt) * rows, rows + 2, 2)
    pieces = [window(chan)]
    for k in range(1, chans):
        pieces.append(lax.ppermute(window((chan + k) % chans), "chan", shift_pairs(chans, k)))
    all_channels = order_blocks(pieces, chan, 0)
    return plane_conv(all_channels, weight, "HWIO").astype(jnp.bfloat16)


def forward_out(deep, depth_weight):
    chans = lax.axis_size("chan")
    filts = lax.axis_size("filt")
    chan = lax.axis_index("chan")
    rows = deep.shape[2]
    out = depth_conv(deep, depth_weight, "DHWOI").astype(jnp.bfloat16)
    return lax.all_to_all(out, "filt", 0, 2, tiled=True)


def backward(grad_out, weight, depth_weight):
    chans = lax.axis_size("chan")
    filts = lax.axis_size("filt")
    chan = lax.axis_index("chan")
    filt = lax.axis_index("filt")
    rows = grad_out.shape[2] // filts
    turn = lambda f, r: r if f % 2 == 0 else chans - 1 - r
    place = lambda g: turn(g // chans, g % chans) * filts + g // chans
    group_of = lambda c, f: f * chans + turn(f, c)
    need = [[[f for f in range(filts) if group_of(t, f) // filts == r] for r in range(chans)] for t in range(chans)]
    per = max(len(need[t][r]) for t in range(chans) for r in range(chans))
    pick = lambda t, r: [group_of(t, f) % filts for f in need[t][r]] + [0] * (per - len(need[t][r]))
    received = []
    for k in range(chans):
        table = jnp.array([pick((r + k) % chans, r) for r in range(chans)], jnp.int32)[chan]
        send = jnp.stack([lax.dynamic_slice_in_dim(grad_out, table[q] * rows, rows, 2) for q in range(per)])
        received.append(send if k == 0 else lax.ppermute(send, "chan", shift_pairs(chans, k)))
    received = jnp.concatenate(received)
    slot = [[0] * filts for _ in range(chans)]
    for t in range(chans):
        for k in range(chans):
            r = (t - k) % chans
            for q, f in enumerate(need[t][r]):
                slot[t][f] = k * per + q
    blocks = jnp.take(received, jnp.array(slot, jnp.int32)[chan], axis=0)
    core = lax.axis_index("slab") % 2
    half = weight.shape[2] // 2
    mine = lax.dynamic_slice_in_dim(weight, core * half, half, 2)
    tile = blocks[0, 0].size
    if mine.size % tile == 0:
        extra = mine.reshape((-1,) + blocks.shape[2:])
        both = jnp.concatenate([blocks, jnp.broadcast_to(extra[None], (filts,) + extra.shape)], axis=1)
        both = lax.all_to_all(both, "filt", 0, 0, tiled=True)
        all_filters = both[:, : blocks.shape[1]]
        got = both[:, blocks.shape[1] :].reshape((filts,) + mine.shape)
        kernel = jnp.transpose(got, (1, 2, 3, 0, 4)).reshape(mine.shape[:3] + (-1,))
    else:
        all_filters = lax.all_to_all(blocks, "filt", 0, 0, tiled=True)
        spread = jnp.broadcast_to(mine[None], (filts,) + mine.shape)
        kernel = lax.all_to_all(spread, "filt", 0, 4, tiled=True)[0]
    return all_filters.reshape((-1,) + all_filters.shape[2:]), kernel


def backward_in(deep, weight, depth_weight):
    chans = lax.axis_size("chan")
    filts = lax.axis_size("filt")
    filt = lax.axis_index("filt")
    rows = deep.shape[2]
    turn = lambda f, r: r if f % 2 == 0 else chans - 1 - r
    place = lambda g: turn(g // chans, g % chans) * filts + g // chans
    grad_mid = depth_conv(deep, depth_weight[::-1], "DHWIO").astype(jnp.bfloat16)
    rimmed = halo(grad_mid, ROWS, 2, place)
    grad_in = plane_conv(rimmed, weight[::-1, ::-1], "HWOI").astype(jnp.bfloat16)
    chan = lax.axis_index("chan")
    c_loc = grad_in.shape[0] // chans
    even = filt % 2 == 0
    pieces = [lax.dynamic_slice_in_dim(grad_in, chan * c_loc, c_loc, 0)]
    for k in range(1, chans):
        target = jnp.where(even, (chan + k) % chans, (chan - k) % chans)
        pairs = [(c * filts + f, (((c + k) if f % 2 == 0 else (c - k)) % chans) * filts + f)
                 for c in range(chans) for f in range(filts)]
        pieces.append(lax.ppermute(lax.dynamic_slice_in_dim(grad_in, target * c_loc, c_loc, 0), ROWS, pairs))
    return order_blocks(pieces, jnp.where(even, chan, chans - 1 - chan), 2)


def local(volume, plane_weight, depth_weight, grad_out):
    all_filters, kernel = backward(grad_out, plane_weight, depth_weight)
    weight = finish_weight(kernel)
    mid = forward(volume, weight, depth_weight)
    deep = halo(jnp.concatenate([mid, all_filters]), "slab", 1)
    output = forward_out(deep[: mid.shape[0]], depth_weight)
    grad_in = backward_in(deep[mid.shape[0] :], weight, depth_weight)
    return (output, grad_in)


def solution(mesh):
    placed = (
        P("chan", "slab", None, None),
        P(None, None, "chan", "filt"),
        P(),
        P("filt", "slab", "chan", None),
    )
    return jax.shard_map(
        local,
        mesh=mesh,
        in_specs=placed,
        out_specs=(P("filt", "slab", "chan", None), P("chan", "slab", "filt", None)),
        check_vma=False,
    )
```

```python
import jax
import jax.numpy as jnp
from jax import lax
from jax.sharding import PartitionSpec as P

ROWS = ("chan", "filt")


def shift_pairs(n, k):
    return [(i, (i + k) % n) for i in range(n)]


def order_blocks(pieces, me, dim):
    n = len(pieces)
    if n == 1:
        return pieces[0]
    if n == 2:
        return jnp.where(me % 2 == 0, jnp.concatenate(pieces, axis=dim), jnp.concatenate(pieces[::-1], axis=dim))
    block = pieces[0].shape[dim]
    stacked = jnp.concatenate(pieces[::-1], axis=dim)
    return jnp.roll(stacked, (me + 1) * block, axis=dim)


def gather_blocks(x, axis, dim):
    n = lax.axis_size(axis)
    me = lax.axis_index(axis)
    pieces = [x] + [lax.ppermute(x, axis, shift_pairs(n, k)) for k in range(1, n)]
    return order_blocks(pieces, me, dim)


def scatter_blocks(x, axis, dim, gather_dim):
    n = lax.axis_size(axis)
    me = lax.axis_index(axis)
    size = x.shape[dim] // n
    take = lambda t: lax.dynamic_slice_in_dim(x, t * size, size, dim)
    pieces = [take(me)]
    for k in range(1, n):
        pieces.append(lax.ppermute(take((me + k) % n), axis, shift_pairs(n, k)))
    return order_blocks(pieces, me, gather_dim)


def halo(x, axis, dim, place=None):
    n = lax.axis_size(axis)
    place = place or (lambda i: i)
    up = [(place(i), place(i + 1)) for i in range(n - 1)]
    down = [(place(i + 1), place(i)) for i in range(n - 1)]
    length = x.shape[dim]
    before = lax.ppermute(lax.slice_in_dim(x, length - 1, length, axis=dim), axis, up)
    after = lax.ppermute(lax.slice_in_dim(x, 0, 1, axis=dim), axis, down)
    return jnp.concatenate([before, x, after], axis=dim)


def plane_conv(rows, weight, spec):
    return lax.conv_general_dilated(
        rows,
        weight,
        window_strides=(1, 1),
        padding=((0, 0), (1, 1)),
        dimension_numbers=("CNHW", spec, "CNHW"),
        preferred_element_type=jnp.float32,
    )


def depth_conv(padded, weight, spec):
    out = lax.conv_general_dilated(
        padded[None],
        weight[:, None, None],
        window_strides=(1, 1, 1),
        padding=((0, 0), (0, 0), (0, 0)),
        dimension_numbers=("NCDHW", spec, "NCDHW"),
        preferred_element_type=jnp.float32,
    )
    return out[0]


def gather_weight(weight):
    filts = lax.axis_size("filt")
    chans = lax.axis_size("chan")
    slabs = lax.axis_size("slab")
    core = lax.axis_index("slab") % 2
    c_loc = weight.shape[2]
    half = c_loc // 2
    mine = lax.dynamic_slice_in_dim(weight, core * half, half, 2)
    spread = jnp.broadcast_to(mine[None], (filts,) + mine.shape)
    by_filt = gather_blocks(lax.all_to_all(spread, "filt", 0, 4, tiled=True)[0], "chan", 2)
    other = lax.ppermute(by_filt, "slab", [(i, i ^ 1) for i in range(slabs)])
    first = jnp.where(core == 0, by_filt, other)
    second = jnp.where(core == 0, other, by_filt)
    split = lambda w: w.reshape(3, 3, chans, 1, half, w.shape[-1])
    whole = jnp.concatenate([split(first), split(second)], axis=3)
    return whole.reshape(3, 3, chans * c_loc, whole.shape[-1])


def sub_block(chan, filt, filts):
    return jnp.where(chan % 2 == 0, filt, filts - 1 - filt)


def sub_block_of(c, f, filts):
    return f if c % 2 == 0 else filts - 1 - f


def forward(volume, weight, depth_weight):
    chans = lax.axis_size("chan")
    filts = lax.axis_size("filt")
    chan = lax.axis_index("chan")
    filt = lax.axis_index("filt")
    rows = volume.shape[2] // (chans * filts)
    padded = jnp.pad(volume, ((0, 0), (0, 0), (1, 1), (0, 0)))
    window = lambda c: lax.dynamic_slice_in_dim(padded, (c * filts + filt) * rows, rows + 2, 2)
    pieces = [window(chan)]
    for k in range(1, chans):
        pieces.append(lax.ppermute(window((chan + k) % chans), "chan", shift_pairs(chans, k)))
    all_channels = order_blocks(pieces, chan, 0)
    return plane_conv(all_channels, weight, "HWIO").astype(jnp.bfloat16)


def forward_out(deep, depth_weight):
    chans = lax.axis_size("chan")
    filts = lax.axis_size("filt")
    chan = lax.axis_index("chan")
    rows = deep.shape[2]
    out = depth_conv(deep, depth_weight, "DHWOI").astype(jnp.bfloat16)
    return lax.all_to_all(out, "filt", 0, 2, tiled=True)


def backward(grad_out, weight, depth_weight):
    chans = lax.axis_size("chan")
    filts = lax.axis_size("filt")
    chan = lax.axis_index("chan")
    filt = lax.axis_index("filt")
    rows = grad_out.shape[2] // filts
    turn = lambda f, r: r if f % 2 == 0 else chans - 1 - r
    place = lambda g: turn(g // chans, g % chans) * filts + g // chans
    group_of = lambda c, f: f * chans + turn(f, c)
    need = [[[f for f in range(filts) if group_of(t, f) // filts == r] for r in range(chans)] for t in range(chans)]
    per = max(len(need[t][r]) for t in range(chans) for r in range(chans))
    pick = lambda t, r: [group_of(t, f) % filts for f in need[t][r]] + [0] * (per - len(need[t][r]))
    received = []
    for k in range(chans):
        table = jnp.array([pick((r + k) % chans, r) for r in range(chans)], jnp.int32)[chan]
        send = jnp.stack([lax.dynamic_slice_in_dim(grad_out, table[q] * rows, rows, 2) for q in range(per)])
        received.append(send if k == 0 else lax.ppermute(send, "chan", shift_pairs(chans, k)))
    received = jnp.concatenate(received)
    slot = [[0] * filts for _ in range(chans)]
    for t in range(chans):
        for k in range(chans):
            r = (t - k) % chans
            for q, f in enumerate(need[t][r]):
                slot[t][f] = k * per + q
    blocks = jnp.take(received, jnp.array(slot, jnp.int32)[chan], axis=0)
    all_filters = lax.all_to_all(blocks, "filt", 0, 0, tiled=True)
    return all_filters.reshape((-1,) + all_filters.shape[2:])


def backward_in(deep, weight, depth_weight):
    chans = lax.axis_size("chan")
    filts = lax.axis_size("filt")
    filt = lax.axis_index("filt")
    rows = deep.shape[2]
    turn = lambda f, r: r if f % 2 == 0 else chans - 1 - r
    place = lambda g: turn(g // chans, g % chans) * filts + g // chans
    grad_mid = depth_conv(deep, depth_weight[::-1], "DHWIO").astype(jnp.bfloat16)
    rimmed = halo(grad_mid, ROWS, 2, place)
    grad_in = plane_conv(rimmed, weight[::-1, ::-1], "HWOI").astype(jnp.bfloat16)
    chan = lax.axis_index("chan")
    c_loc = grad_in.shape[0] // chans
    even = filt % 2 == 0
    pieces = [lax.dynamic_slice_in_dim(grad_in, chan * c_loc, c_loc, 0)]
    for k in range(1, chans):
        target = jnp.where(even, (chan + k) % chans, (chan - k) % chans)
        pairs = [(c * filts + f, (((c + k) if f % 2 == 0 else (c - k)) % chans) * filts + f)
                 for c in range(chans) for f in range(filts)]
        pieces.append(lax.ppermute(lax.dynamic_slice_in_dim(grad_in, target * c_loc, c_loc, 0), ROWS, pairs))
    return order_blocks(pieces, jnp.where(even, chan, chans - 1 - chan), 2)


def local(volume, plane_weight, depth_weight, grad_out):
    weight = gather_weight(plane_weight)
    mid = forward(volume, weight, depth_weight)
    all_filters = backward(grad_out, weight, depth_weight)
    deep = halo(jnp.concatenate([mid, all_filters]), "slab", 1)
    output = forward_out(deep[: mid.shape[0]], depth_weight)
    grad_in = backward_in(deep[mid.shape[0] :], weight, depth_weight)
    return (output, grad_in)


def solution(mesh):
    placed = (
        P("chan", "slab", None, None),
        P(None, None, "chan", "filt"),
        P(),
        P("filt", "slab", "chan", None),
    )
    return jax.shard_map(
        local,
        mesh=mesh,
        in_specs=placed,
        out_specs=(P("filt", "slab", "chan", None), P("chan", "slab", "filt", None)),
        check_vma=False,
    )
```

```python
import jax
import jax.numpy as jnp
from jax import lax
from jax.sharding import PartitionSpec as P

ROWS = ("chan", "filt")


def shift_pairs(n, k):
    return [(i, (i + k) % n) for i in range(n)]


def order_blocks(pieces, me, dim):
    n = len(pieces)
    if n == 1:
        return pieces[0]
    if n == 2:
        return jnp.where(me % 2 == 0, jnp.concatenate(pieces, axis=dim), jnp.concatenate(pieces[::-1], axis=dim))
    block = pieces[0].shape[dim]
    stacked = jnp.concatenate(pieces[::-1], axis=dim)
    return jnp.roll(stacked, (me + 1) * block, axis=dim)


def gather_blocks(x, axis, dim):
    n = lax.axis_size(axis)
    me = lax.axis_index(axis)
    pieces = [x] + [lax.ppermute(x, axis, shift_pairs(n, k)) for k in range(1, n)]
    return order_blocks(pieces, me, dim)


def scatter_blocks(x, axis, dim, gather_dim):
    n = lax.axis_size(axis)
    me = lax.axis_index(axis)
    size = x.shape[dim] // n
    take = lambda t: lax.dynamic_slice_in_dim(x, t * size, size, dim)
    pieces = [take(me)]
    for k in range(1, n):
        pieces.append(lax.ppermute(take((me + k) % n), axis, shift_pairs(n, k)))
    return order_blocks(pieces, me, gather_dim)


def halo(x, axis, dim, place=None):
    n = lax.axis_size(axis)
    place = place or (lambda i: i)
    up = [(place(i), place(i + 1)) for i in range(n - 1)]
    down = [(place(i + 1), place(i)) for i in range(n - 1)]
    length = x.shape[dim]
    before = lax.ppermute(lax.slice_in_dim(x, length - 1, length, axis=dim), axis, up)
    after = lax.ppermute(lax.slice_in_dim(x, 0, 1, axis=dim), axis, down)
    return jnp.concatenate([before, x, after], axis=dim)


def plane_conv(rows, weight, spec):
    return lax.conv_general_dilated(
        rows,
        weight,
        window_strides=(1, 1),
        padding=((0, 0), (1, 1)),
        dimension_numbers=("CNHW", spec, "CNHW"),
        preferred_element_type=jnp.float32,
    )


def depth_conv(padded, weight, spec):
    out = lax.conv_general_dilated(
        padded[None],
        weight[:, None, None],
        window_strides=(1, 1, 1),
        padding=((0, 0), (0, 0), (0, 0)),
        dimension_numbers=("NCDHW", spec, "NCDHW"),
        preferred_element_type=jnp.float32,
    )
    return out[0]


def gather_weight(weight):
    filts = lax.axis_size("filt")
    chans = lax.axis_size("chan")
    slabs = lax.axis_size("slab")
    core = lax.axis_index("slab") % 2
    c_loc = weight.shape[2]
    half = c_loc // 2
    mine = lax.dynamic_slice_in_dim(weight, core * half, half, 2)
    spread = jnp.broadcast_to(mine[None], (filts,) + mine.shape)
    by_filt = gather_blocks(lax.all_to_all(spread, "filt", 0, 4, tiled=True)[0], "chan", 2)
    other = lax.ppermute(by_filt, "slab", [(i, i ^ 1) for i in range(slabs)])
    first = jnp.where(core == 0, by_filt, other)
    second = jnp.where(core == 0, other, by_filt)
    split = lambda w: w.reshape(3, 3, chans, 1, half, w.shape[-1])
    whole = jnp.concatenate([split(first), split(second)], axis=3)
    return whole.reshape(3, 3, chans * c_loc, whole.shape[-1])


def sub_block(chan, filt, filts):
    return jnp.where(chan % 2 == 0, filt, filts - 1 - filt)


def sub_block_of(c, f, filts):
    return f if c % 2 == 0 else filts - 1 - f


def forward(volume, weight, depth_weight):
    chans = lax.axis_size("chan")
    filts = lax.axis_size("filt")
    chan = lax.axis_index("chan")
    filt = lax.axis_index("filt")
    rows = volume.shape[2] // (chans * filts)
    padded = jnp.pad(volume, ((0, 0), (0, 0), (1, 1), (0, 0)))
    window = lambda c: lax.dynamic_slice_in_dim(padded, (c * filts + filt) * rows, rows + 2, 2)
    pieces = [window(chan)]
    for k in range(1, chans):
        pieces.append(lax.ppermute(window((chan + k) % chans), "chan", shift_pairs(chans, k)))
    all_channels = order_blocks(pieces, chan, 0)
    return plane_conv(all_channels, weight, "HWIO").astype(jnp.bfloat16)


def forward_out(deep, depth_weight):
    chans = lax.axis_size("chan")
    filts = lax.axis_size("filt")
    chan = lax.axis_index("chan")
    rows = deep.shape[2]
    out = depth_conv(deep, depth_weight, "DHWOI").astype(jnp.bfloat16)
    return lax.all_to_all(out, "filt", 0, 2, tiled=True)


def backward(grad_out, weight, depth_weight):
    chans = lax.axis_size("chan")
    filts = lax.axis_size("filt")
    chan = lax.axis_index("chan")
    filt = lax.axis_index("filt")
    rows = grad_out.shape[2] // filts
    turn = lambda f, r: r if f % 2 == 0 else chans - 1 - r
    place = lambda g: turn(g // chans, g % chans) * filts + g // chans
    group_of = lambda c, f: f * chans + turn(f, c)
    need = [[[f for f in range(filts) if group_of(t, f) // filts == r] for r in range(chans)] for t in range(chans)]
    per = max(len(need[t][r]) for t in range(chans) for r in range(chans))
    pick = lambda t, r: [group_of(t, f) % filts for f in need[t][r]] + [0] * (per - len(need[t][r]))
    received = []
    for k in range(chans):
        table = jnp.array([pick((r + k) % chans, r) for r in range(chans)], jnp.int32)[chan]
        send = jnp.stack([lax.dynamic_slice_in_dim(grad_out, table[q] * rows, rows, 2) for q in range(per)])
        received.append(send if k == 0 else lax.ppermute(send, "chan", shift_pairs(chans, k)))
    received = jnp.concatenate(received)
    slot = [[0] * filts for _ in range(chans)]
    for t in range(chans):
        for k in range(chans):
            r = (t - k) % chans
            for q, f in enumerate(need[t][r]):
                slot[t][f] = k * per + q
    if chans == 2:
        order = lambda t: jnp.stack([received[slot[t][f]] for f in range(filts)])
        blocks = jnp.where(chan == 0, order(0), order(1))
    else:
        blocks = jnp.take(received, jnp.array(slot, jnp.int32)[chan], axis=0)
    all_filters = lax.all_to_all(blocks, "filt", 0, 0, tiled=True)
    return all_filters.reshape((-1,) + all_filters.shape[2:])


def backward_in(deep, weight, depth_weight):
    chans = lax.axis_size("chan")
    filts = lax.axis_size("filt")
    filt = lax.axis_index("filt")
    rows = deep.shape[2]
    turn = lambda f, r: r if f % 2 == 0 else chans - 1 - r
    place = lambda g: turn(g // chans, g % chans) * filts + g // chans
    grad_mid = depth_conv(deep, depth_weight[::-1], "DHWIO").astype(jnp.bfloat16)
    rimmed = halo(grad_mid, ROWS, 2, place)
    grad_in = plane_conv(rimmed, weight[::-1, ::-1], "HWOI").astype(jnp.bfloat16)
    chan = lax.axis_index("chan")
    c_loc = grad_in.shape[0] // chans
    even = filt % 2 == 0
    pieces = [lax.dynamic_slice_in_dim(grad_in, chan * c_loc, c_loc, 0)]
    for k in range(1, chans):
        target = jnp.where(even, (chan + k) % chans, (chan - k) % chans)
        pairs = [(c * filts + f, (((c + k) if f % 2 == 0 else (c - k)) % chans) * filts + f)
                 for c in range(chans) for f in range(filts)]
        pieces.append(lax.ppermute(lax.dynamic_slice_in_dim(grad_in, target * c_loc, c_loc, 0), ROWS, pairs))
    return order_blocks(pieces, jnp.where(even, chan, chans - 1 - chan), 2)


def local(volume, plane_weight, depth_weight, grad_out):
    weight = gather_weight(plane_weight)
    mid = forward(volume, weight, depth_weight)
    all_filters = backward(grad_out, weight, depth_weight)
    deep = halo(jnp.concatenate([mid, all_filters]), "slab", 1)
    output = forward_out(deep[: mid.shape[0]], depth_weight)
    grad_in = backward_in(deep[mid.shape[0] :], weight, depth_weight)
    return (output, grad_in)


def solution(mesh):
    placed = (
        P("chan", "slab", None, None),
        P(None, None, "chan", "filt"),
        P(),
        P("filt", "slab", "chan", None),
    )
    return jax.shard_map(
        local,
        mesh=mesh,
        in_specs=placed,
        out_specs=(P("filt", "slab", "chan", None), P("chan", "slab", "filt", None)),
        check_vma=False,
    )
```

```python
import jax
import jax.numpy as jnp
from jax import lax
from jax.sharding import PartitionSpec as P

ROWS = ("chan", "filt")


def shift_pairs(n, k):
    return [(i, (i + k) % n) for i in range(n)]


def order_blocks(pieces, me, dim):
    n = len(pieces)
    if n == 1:
        return pieces[0]
    if n == 2:
        return jnp.where(me % 2 == 0, jnp.concatenate(pieces, axis=dim), jnp.concatenate(pieces[::-1], axis=dim))
    block = pieces[0].shape[dim]
    stacked = jnp.concatenate(pieces[::-1], axis=dim)
    return jnp.roll(stacked, (me + 1) * block, axis=dim)


def gather_blocks(x, axis, dim):
    n = lax.axis_size(axis)
    me = lax.axis_index(axis)
    pieces = [x] + [lax.ppermute(x, axis, shift_pairs(n, k)) for k in range(1, n)]
    return order_blocks(pieces, me, dim)


def scatter_blocks(x, axis, dim, gather_dim):
    n = lax.axis_size(axis)
    me = lax.axis_index(axis)
    size = x.shape[dim] // n
    take = lambda t: lax.dynamic_slice_in_dim(x, t * size, size, dim)
    pieces = [take(me)]
    for k in range(1, n):
        pieces.append(lax.ppermute(take((me + k) % n), axis, shift_pairs(n, k)))
    return order_blocks(pieces, me, gather_dim)


def halo(x, axis, dim, place=None):
    n = lax.axis_size(axis)
    place = place or (lambda i: i)
    up = [(place(i), place(i + 1)) for i in range(n - 1)]
    down = [(place(i + 1), place(i)) for i in range(n - 1)]
    length = x.shape[dim]
    before = lax.ppermute(lax.slice_in_dim(x, length - 1, length, axis=dim), axis, up)
    after = lax.ppermute(lax.slice_in_dim(x, 0, 1, axis=dim), axis, down)
    return jnp.concatenate([before, x, after], axis=dim)


def plane_conv(rows, weight, spec):
    return lax.conv_general_dilated(
        rows,
        weight,
        window_strides=(1, 1),
        padding=((0, 0), (1, 1)),
        dimension_numbers=("CNHW", spec, "CNHW"),
        preferred_element_type=jnp.float32,
    )


def depth_conv(padded, weight, spec):
    out = lax.conv_general_dilated(
        padded[None],
        weight[:, None, None],
        window_strides=(1, 1, 1),
        padding=((0, 0), (0, 0), (0, 0)),
        dimension_numbers=("NCDHW", spec, "NCDHW"),
        preferred_element_type=jnp.float32,
    )
    return out[0]


def gather_weight(weight):
    filts = lax.axis_size("filt")
    chans = lax.axis_size("chan")
    slabs = lax.axis_size("slab")
    core = lax.axis_index("slab") % 2
    c_loc = weight.shape[2]
    half = c_loc // 2
    mine = lax.dynamic_slice_in_dim(weight, core * half, half, 2)
    spread = jnp.broadcast_to(mine[None], (filts,) + mine.shape)
    by_filt = gather_blocks(lax.all_to_all(spread, "filt", 0, 4, tiled=True)[0], "chan", 2)
    other = lax.ppermute(by_filt, "slab", [(i, i ^ 1) for i in range(slabs)])
    first = jnp.where(core == 0, by_filt, other)
    second = jnp.where(core == 0, other, by_filt)
    split = lambda w: w.reshape(3, 3, chans, 1, half, w.shape[-1])
    whole = jnp.concatenate([split(first), split(second)], axis=3)
    return whole.reshape(3, 3, chans * c_loc, whole.shape[-1])


def sub_block(chan, filt, filts):
    return jnp.where(chan % 2 == 0, filt, filts - 1 - filt)


def sub_block_of(c, f, filts):
    return f if c % 2 == 0 else filts - 1 - f


def forward(volume, weight, depth_weight):
    chans = lax.axis_size("chan")
    filts = lax.axis_size("filt")
    chan = lax.axis_index("chan")
    filt = lax.axis_index("filt")
    rows = volume.shape[2] // (chans * filts)
    padded = jnp.pad(volume, ((0, 0), (0, 0), (1, 1), (0, 0)))
    window = lambda c: lax.dynamic_slice_in_dim(padded, (c * filts + filt) * rows, rows + 2, 2)
    pieces = [window(chan)]
    for k in range(1, chans):
        pieces.append(lax.ppermute(window((chan + k) % chans), "chan", shift_pairs(chans, k)))
    all_channels = order_blocks(pieces, chan, 0)
    return plane_conv(all_channels, weight, "HWIO").astype(jnp.bfloat16)


def forward_out(deep, depth_weight):
    chans = lax.axis_size("chan")
    filts = lax.axis_size("filt")
    chan = lax.axis_index("chan")
    rows = deep.shape[2]
    out = depth_conv(deep, depth_weight, "DHWOI").astype(jnp.bfloat16)
    return lax.all_to_all(out, "filt", 0, 2, tiled=True)


def backward(grad_out, weight, depth_weight):
    chans = lax.axis_size("chan")
    filts = lax.axis_size("filt")
    chan = lax.axis_index("chan")
    filt = lax.axis_index("filt")
    rows = grad_out.shape[2] // filts
    turn = lambda f, r: r if f % 2 == 0 else chans - 1 - r
    place = lambda g: turn(g // chans, g % chans) * filts + g // chans
    group_of = lambda c, f: f * chans + turn(f, c)
    need = [[[f for f in range(filts) if group_of(t, f) // filts == r] for r in range(chans)] for t in range(chans)]
    per = max(len(need[t][r]) for t in range(chans) for r in range(chans))
    pick = lambda t, r: [group_of(t, f) % filts for f in need[t][r]] + [0] * (per - len(need[t][r]))
    received = []
    for k in range(chans):
        table = jnp.array([pick((r + k) % chans, r) for r in range(chans)], jnp.int32)[chan]
        send = jnp.stack([lax.dynamic_slice_in_dim(grad_out, table[q] * rows, rows, 2) for q in range(per)])
        received.append(send if k == 0 else lax.ppermute(send, "chan", shift_pairs(chans, k)))
    received = jnp.concatenate(received)
    slot = [[0] * filts for _ in range(chans)]
    for t in range(chans):
        for k in range(chans):
            r = (t - k) % chans
            for q, f in enumerate(need[t][r]):
                slot[t][f] = k * per + q
    blocks = jnp.take(received, jnp.array(slot, jnp.int32)[chan], axis=0)
    all_filters = lax.all_to_all(blocks, "filt", 0, 0, tiled=True)
    return all_filters.reshape((-1,) + all_filters.shape[2:])


def backward_in(deep, weight, depth_weight):
    chans = lax.axis_size("chan")
    filts = lax.axis_size("filt")
    filt = lax.axis_index("filt")
    rows = deep.shape[2]
    turn = lambda f, r: r if f % 2 == 0 else chans - 1 - r
    place = lambda g: turn(g // chans, g % chans) * filts + g // chans
    taps = depth_weight.shape[0]
    flipped = jnp.concatenate([depth_weight[t : t + 1] for t in reversed(range(taps))])
    grad_mid = depth_conv(deep, flipped, "DHWIO").astype(jnp.bfloat16)
    rimmed = halo(grad_mid, ROWS, 2, place)
    grad_in = plane_conv(rimmed, weight[::-1, ::-1], "HWOI").astype(jnp.bfloat16)
    chan = lax.axis_index("chan")
    c_loc = grad_in.shape[0] // chans
    even = filt % 2 == 0
    pieces = [lax.dynamic_slice_in_dim(grad_in, chan * c_loc, c_loc, 0)]
    for k in range(1, chans):
        target = jnp.where(even, (chan + k) % chans, (chan - k) % chans)
        pairs = [(c * filts + f, (((c + k) if f % 2 == 0 else (c - k)) % chans) * filts + f)
                 for c in range(chans) for f in range(filts)]
        pieces.append(lax.ppermute(lax.dynamic_slice_in_dim(grad_in, target * c_loc, c_loc, 0), ROWS, pairs))
    return order_blocks(pieces, jnp.where(even, chan, chans - 1 - chan), 2)


def local(volume, plane_weight, depth_weight, grad_out):
    weight = gather_weight(plane_weight)
    mid = forward(volume, weight, depth_weight)
    all_filters = backward(grad_out, weight, depth_weight)
    deep = halo(jnp.concatenate([mid, all_filters]), "slab", 1)
    output = forward_out(deep[: mid.shape[0]], depth_weight)
    grad_in = backward_in(deep[mid.shape[0] :], weight, depth_weight)
    return (output, grad_in)


def solution(mesh):
    placed = (
        P("chan", "slab", None, None),
        P(None, None, "chan", "filt"),
        P(),
        P("filt", "slab", "chan", None),
    )
    return jax.shard_map(
        local,
        mesh=mesh,
        in_specs=placed,
        out_specs=(P("filt", "slab", "chan", None), P("chan", "slab", "filt", None)),
        check_vma=False,
    )
```

```python
import jax
import jax.numpy as jnp
from jax import lax
from jax.sharding import PartitionSpec as P

ROWS = ("chan", "filt")


def shift_pairs(n, k):
    return [(i, (i + k) % n) for i in range(n)]


def order_blocks(pieces, me, dim):
    n = len(pieces)
    if n == 1:
        return pieces[0]
    if n == 2:
        return jnp.where(me % 2 == 0, jnp.concatenate(pieces, axis=dim), jnp.concatenate(pieces[::-1], axis=dim))
    block = pieces[0].shape[dim]
    stacked = jnp.concatenate(pieces[::-1], axis=dim)
    return jnp.roll(stacked, (me + 1) * block, axis=dim)


def gather_blocks(x, axis, dim):
    n = lax.axis_size(axis)
    me = lax.axis_index(axis)
    pieces = [x] + [lax.ppermute(x, axis, shift_pairs(n, k)) for k in range(1, n)]
    return order_blocks(pieces, me, dim)


def scatter_blocks(x, axis, dim, gather_dim):
    n = lax.axis_size(axis)
    me = lax.axis_index(axis)
    size = x.shape[dim] // n
    take = lambda t: lax.dynamic_slice_in_dim(x, t * size, size, dim)
    pieces = [take(me)]
    for k in range(1, n):
        pieces.append(lax.ppermute(take((me + k) % n), axis, shift_pairs(n, k)))
    return order_blocks(pieces, me, gather_dim)


def halo(x, axis, dim, place=None):
    n = lax.axis_size(axis)
    place = place or (lambda i: i)
    up = [(place(i), place(i + 1)) for i in range(n - 1)]
    down = [(place(i + 1), place(i)) for i in range(n - 1)]
    length = x.shape[dim]
    before = lax.ppermute(lax.slice_in_dim(x, length - 1, length, axis=dim), axis, up)
    after = lax.ppermute(lax.slice_in_dim(x, 0, 1, axis=dim), axis, down)
    return jnp.concatenate([before, x, after], axis=dim)


def plane_conv(rows, weight, spec):
    return lax.conv_general_dilated(
        rows,
        weight,
        window_strides=(1, 1),
        padding=((0, 0), (1, 1)),
        dimension_numbers=("CNHW", spec, "CNHW"),
        preferred_element_type=jnp.float32,
    )


def depth_conv(padded, weight, spec):
    out = lax.conv_general_dilated(
        padded[None],
        weight[:, None, None],
        window_strides=(1, 1, 1),
        padding=((0, 0), (0, 0), (0, 0)),
        dimension_numbers=("NCDHW", spec, "NCDHW"),
        preferred_element_type=jnp.float32,
    )
    return out[0]


def gather_weight(weight):
    filts = lax.axis_size("filt")
    chans = lax.axis_size("chan")
    slabs = lax.axis_size("slab")
    core = lax.axis_index("slab") % 2
    c_loc = weight.shape[2]
    half = c_loc // 2
    mine = lax.dynamic_slice_in_dim(weight, core * half, half, 2)
    spread = jnp.broadcast_to(mine[None], (filts,) + mine.shape)
    got = lax.all_to_all(spread, "filt", 0, 4, tiled=True)[0]
    by_filt = jnp.concatenate([got] + [lax.ppermute(got, "chan", shift_pairs(chans, k)) for k in range(1, chans)], axis=2)
    other = lax.ppermute(by_filt, "slab", [(i, i ^ 1) for i in range(slabs)])
    first = jnp.where(core == 0, by_filt, other)
    second = jnp.where(core == 0, other, by_filt)
    split = lambda w: w.reshape(3, 3, chans, 1, half, w.shape[-1])
    whole = jnp.concatenate([split(first), split(second)], axis=3)
    return whole.reshape(3, 3, chans * c_loc, whole.shape[-1])


def sub_block(chan, filt, filts):
    return jnp.where(chan % 2 == 0, filt, filts - 1 - filt)


def sub_block_of(c, f, filts):
    return f if c % 2 == 0 else filts - 1 - f


def forward(volume, weight, depth_weight):
    chans = lax.axis_size("chan")
    filts = lax.axis_size("filt")
    chan = lax.axis_index("chan")
    filt = lax.axis_index("filt")
    rows = volume.shape[2] // (chans * filts)
    padded = jnp.pad(volume, ((0, 0), (0, 0), (1, 1), (0, 0)))
    window = lambda c: lax.dynamic_slice_in_dim(padded, (c * filts + filt) * rows, rows + 2, 2)
    pieces = [window(chan)]
    for k in range(1, chans):
        pieces.append(lax.ppermute(window((chan + k) % chans), "chan", shift_pairs(chans, k)))
    all_channels = jnp.concatenate(pieces, axis=0)
    return plane_conv(all_channels, weight, "HWIO").astype(jnp.bfloat16)


def forward_out(deep, depth_weight):
    chans = lax.axis_size("chan")
    filts = lax.axis_size("filt")
    chan = lax.axis_index("chan")
    rows = deep.shape[2]
    out = depth_conv(deep, depth_weight, "DHWOI").astype(jnp.bfloat16)
    return lax.all_to_all(out, "filt", 0, 2, tiled=True)


def backward(grad_out, weight, depth_weight):
    chans = lax.axis_size("chan")
    filts = lax.axis_size("filt")
    chan = lax.axis_index("chan")
    filt = lax.axis_index("filt")
    rows = grad_out.shape[2] // filts
    turn = lambda f, r: r if f % 2 == 0 else chans - 1 - r
    place = lambda g: turn(g // chans, g % chans) * filts + g // chans
    group_of = lambda c, f: f * chans + turn(f, c)
    need = [[[f for f in range(filts) if group_of(t, f) // filts == r] for r in range(chans)] for t in range(chans)]
    per = max(len(need[t][r]) for t in range(chans) for r in range(chans))
    pick = lambda t, r: [group_of(t, f) % filts for f in need[t][r]] + [0] * (per - len(need[t][r]))
    received = []
    for k in range(chans):
        table = jnp.array([pick((r + k) % chans, r) for r in range(chans)], jnp.int32)[chan]
        send = jnp.stack([lax.dynamic_slice_in_dim(grad_out, table[q] * rows, rows, 2) for q in range(per)])
        received.append(send if k == 0 else lax.ppermute(send, "chan", shift_pairs(chans, k)))
    received = jnp.concatenate(received)
    slot = [[0] * filts for _ in range(chans)]
    for t in range(chans):
        for k in range(chans):
            r = (t - k) % chans
            for q, f in enumerate(need[t][r]):
                slot[t][f] = k * per + q
    blocks = jnp.take(received, jnp.array(slot, jnp.int32)[chan], axis=0)
    all_filters = lax.all_to_all(blocks, "filt", 0, 0, tiled=True)
    return all_filters.reshape((-1,) + all_filters.shape[2:])


def backward_in(deep, weight, depth_weight):
    chans = lax.axis_size("chan")
    filts = lax.axis_size("filt")
    filt = lax.axis_index("filt")
    rows = deep.shape[2]
    turn = lambda f, r: r if f % 2 == 0 else chans - 1 - r
    place = lambda g: turn(g // chans, g % chans) * filts + g // chans
    grad_mid = depth_conv(deep, depth_weight[::-1], "DHWIO").astype(jnp.bfloat16)
    rimmed = halo(grad_mid, ROWS, 2, place)
    grad_in = plane_conv(rimmed, weight[::-1, ::-1], "HWOI").astype(jnp.bfloat16)
    chan = lax.axis_index("chan")
    c_loc = grad_in.shape[0] // chans
    even = filt % 2 == 0
    pieces = [grad_in[:c_loc]]
    for k in range(1, chans):
        target = jnp.where(even, (chan + k) % chans, (chan - k) % chans)
        pairs = [(c * filts + f, (((c + k) if f % 2 == 0 else (c - k)) % chans) * filts + f)
                 for c in range(chans) for f in range(filts)]
        at = (chan - target) % chans
        pieces.append(lax.ppermute(lax.dynamic_slice_in_dim(grad_in, at * c_loc, c_loc, 0), ROWS, pairs))
    return order_blocks(pieces, jnp.where(even, chan, chans - 1 - chan), 2)


def local(volume, plane_weight, depth_weight, grad_out):
    weight = gather_weight(plane_weight)
    mid = forward(volume, weight, depth_weight)
    all_filters = backward(grad_out, weight, depth_weight)
    deep = halo(jnp.concatenate([mid, all_filters]), "slab", 1)
    output = forward_out(deep[: mid.shape[0]], depth_weight)
    grad_in = backward_in(deep[mid.shape[0] :], weight, depth_weight)
    return (output, grad_in)


def solution(mesh):
    placed = (
        P("chan", "slab", None, None),
        P(None, None, "chan", "filt"),
        P(),
        P("filt", "slab", "chan", None),
    )
    return jax.shard_map(
        local,
        mesh=mesh,
        in_specs=placed,
        out_specs=(P("filt", "slab", "chan", None), P("chan", "slab", "filt", None)),
        check_vma=False,
    )
```

```python
import jax
import jax.numpy as jnp
from jax import lax
from jax.sharding import PartitionSpec as P

ROWS = ("chan", "filt")


def shift_pairs(n, k):
    return [(i, (i + k) % n) for i in range(n)]


def order_blocks(pieces, me, dim):
    n = len(pieces)
    if n == 1:
        return pieces[0]
    if n == 2:
        return jnp.where(me % 2 == 0, jnp.concatenate(pieces, axis=dim), jnp.concatenate(pieces[::-1], axis=dim))
    block = pieces[0].shape[dim]
    stacked = jnp.concatenate(pieces[::-1], axis=dim)
    return jnp.roll(stacked, (me + 1) * block, axis=dim)


def gather_blocks(x, axis, dim):
    n = lax.axis_size(axis)
    me = lax.axis_index(axis)
    pieces = [x] + [lax.ppermute(x, axis, shift_pairs(n, k)) for k in range(1, n)]
    return order_blocks(pieces, me, dim)


def scatter_blocks(x, axis, dim, gather_dim):
    n = lax.axis_size(axis)
    me = lax.axis_index(axis)
    size = x.shape[dim] // n
    take = lambda t: lax.dynamic_slice_in_dim(x, t * size, size, dim)
    pieces = [take(me)]
    for k in range(1, n):
        pieces.append(lax.ppermute(take((me + k) % n), axis, shift_pairs(n, k)))
    return order_blocks(pieces, me, gather_dim)


def halo(x, axis, dim, place=None):
    n = lax.axis_size(axis)
    place = place or (lambda i: i)
    up = [(place(i), place(i + 1)) for i in range(n - 1)]
    down = [(place(i + 1), place(i)) for i in range(n - 1)]
    length = x.shape[dim]
    before = lax.ppermute(lax.slice_in_dim(x, length - 1, length, axis=dim), axis, up)
    after = lax.ppermute(lax.slice_in_dim(x, 0, 1, axis=dim), axis, down)
    return jnp.concatenate([before, x, after], axis=dim)


def plane_conv(rows, weight, spec):
    return lax.conv_general_dilated(
        rows,
        weight,
        window_strides=(1, 1),
        padding=((0, 0), (1, 1)),
        dimension_numbers=("CNHW", spec, "CNHW"),
        preferred_element_type=jnp.float32,
    )


def depth_conv(padded, weight, spec):
    out = lax.conv_general_dilated(
        padded[None],
        weight[:, None, None],
        window_strides=(1, 1, 1),
        padding=((0, 0), (0, 0), (0, 0)),
        dimension_numbers=("NCDHW", spec, "NCDHW"),
        preferred_element_type=jnp.float32,
    )
    return out[0]


def gather_weight(weight):
    filts = lax.axis_size("filt")
    chans = lax.axis_size("chan")
    spread = jnp.broadcast_to(weight[None], (filts,) + weight.shape)
    got = lax.all_to_all(spread, "filt", 0, 4, tiled=True)[0]
    return jnp.concatenate([got] + [lax.ppermute(got, "chan", shift_pairs(chans, k)) for k in range(1, chans)], axis=2)


def sub_block(chan, filt, filts):
    return jnp.where(chan % 2 == 0, filt, filts - 1 - filt)


def sub_block_of(c, f, filts):
    return f if c % 2 == 0 else filts - 1 - f


def forward(volume, weight, depth_weight):
    chans = lax.axis_size("chan")
    filts = lax.axis_size("filt")
    chan = lax.axis_index("chan")
    filt = lax.axis_index("filt")
    rows = volume.shape[2] // (chans * filts)
    padded = jnp.pad(volume, ((0, 0), (0, 0), (1, 1), (0, 0)))
    window = lambda c: lax.dynamic_slice_in_dim(padded, (c * filts + filt) * rows, rows + 2, 2)
    pieces = [window(chan)]
    for k in range(1, chans):
        pieces.append(lax.ppermute(window((chan + k) % chans), "chan", shift_pairs(chans, k)))
    all_channels = jnp.concatenate(pieces, axis=0)
    return plane_conv(all_channels, weight, "HWIO").astype(jnp.bfloat16)


def forward_out(deep, depth_weight):
    chans = lax.axis_size("chan")
    filts = lax.axis_size("filt")
    chan = lax.axis_index("chan")
    rows = deep.shape[2]
    out = depth_conv(deep, depth_weight, "DHWOI").astype(jnp.bfloat16)
    return lax.all_to_all(out, "filt", 0, 2, tiled=True)


def backward(grad_out, weight, depth_weight):
    chans = lax.axis_size("chan")
    filts = lax.axis_size("filt")
    chan = lax.axis_index("chan")
    filt = lax.axis_index("filt")
    rows = grad_out.shape[2] // filts
    turn = lambda f, r: r if f % 2 == 0 else chans - 1 - r
    place = lambda g: turn(g // chans, g % chans) * filts + g // chans
    group_of = lambda c, f: f * chans + turn(f, c)
    need = [[[f for f in range(filts) if group_of(t, f) // filts == r] for r in range(chans)] for t in range(chans)]
    per = max(len(need[t][r]) for t in range(chans) for r in range(chans))
    pick = lambda t, r: [group_of(t, f) % filts for f in need[t][r]] + [0] * (per - len(need[t][r]))
    received = []
    for k in range(chans):
        table = jnp.array([pick((r + k) % chans, r) for r in range(chans)], jnp.int32)[chan]
        send = jnp.stack([lax.dynamic_slice_in_dim(grad_out, table[q] * rows, rows, 2) for q in range(per)])
        received.append(send if k == 0 else lax.ppermute(send, "chan", shift_pairs(chans, k)))
    received = jnp.concatenate(received)
    slot = [[0] * filts for _ in range(chans)]
    for t in range(chans):
        for k in range(chans):
            r = (t - k) % chans
            for q, f in enumerate(need[t][r]):
                slot[t][f] = k * per + q
    blocks = jnp.take(received, jnp.array(slot, jnp.int32)[chan], axis=0)
    all_filters = lax.all_to_all(blocks, "filt", 0, 0, tiled=True)
    return all_filters.reshape((-1,) + all_filters.shape[2:])


def backward_in(deep, weight, depth_weight):
    chans = lax.axis_size("chan")
    filts = lax.axis_size("filt")
    filt = lax.axis_index("filt")
    rows = deep.shape[2]
    turn = lambda f, r: r if f % 2 == 0 else chans - 1 - r
    place = lambda g: turn(g // chans, g % chans) * filts + g // chans
    grad_mid = depth_conv(deep, depth_weight[::-1], "DHWIO").astype(jnp.bfloat16)
    rimmed = halo(grad_mid, ROWS, 2, place)
    grad_in = plane_conv(rimmed, weight[::-1, ::-1], "HWOI").astype(jnp.bfloat16)
    chan = lax.axis_index("chan")
    c_loc = grad_in.shape[0] // chans
    even = filt % 2 == 0
    pieces = [grad_in[:c_loc]]
    for k in range(1, chans):
        target = jnp.where(even, (chan + k) % chans, (chan - k) % chans)
        pairs = [(c * filts + f, (((c + k) if f % 2 == 0 else (c - k)) % chans) * filts + f)
                 for c in range(chans) for f in range(filts)]
        at = (chan - target) % chans
        pieces.append(lax.ppermute(lax.dynamic_slice_in_dim(grad_in, at * c_loc, c_loc, 0), ROWS, pairs))
    return order_blocks(pieces, jnp.where(even, chan, chans - 1 - chan), 2)


def local(volume, plane_weight, depth_weight, grad_out):
    weight = gather_weight(plane_weight)
    mid = forward(volume, weight, depth_weight)
    all_filters = backward(grad_out, weight, depth_weight)
    deep = halo(jnp.concatenate([mid, all_filters]), "slab", 1)
    output = forward_out(deep[: mid.shape[0]], depth_weight)
    grad_in = backward_in(deep[mid.shape[0] :], weight, depth_weight)
    return (output, grad_in)


def solution(mesh):
    placed = (
        P("chan", "slab", None, None),
        P(None, None, "chan", "filt"),
        P(),
        P("filt", "slab", "chan", None),
    )
    return jax.shard_map(
        local,
        mesh=mesh,
        in_specs=placed,
        out_specs=(P("filt", "slab", "chan", None), P("chan", "slab", "filt", None)),
        check_vma=False,
    )
```

```python
import jax
import jax.numpy as jnp
from jax import lax
from jax.sharding import PartitionSpec as P

ROWS = ("chan", "filt")


def shift_pairs(n, k):
    return [(i, (i + k) % n) for i in range(n)]


def order_blocks(pieces, me, dim):
    n = len(pieces)
    if n == 1:
        return pieces[0]
    if n == 2:
        return jnp.where(me % 2 == 0, jnp.concatenate(pieces, axis=dim), jnp.concatenate(pieces[::-1], axis=dim))
    block = pieces[0].shape[dim]
    stacked = jnp.concatenate(pieces[::-1], axis=dim)
    return jnp.roll(stacked, (me + 1) * block, axis=dim)


def gather_blocks(x, axis, dim):
    n = lax.axis_size(axis)
    me = lax.axis_index(axis)
    pieces = [x] + [lax.ppermute(x, axis, shift_pairs(n, k)) for k in range(1, n)]
    return order_blocks(pieces, me, dim)


def scatter_blocks(x, axis, dim, gather_dim):
    n = lax.axis_size(axis)
    me = lax.axis_index(axis)
    size = x.shape[dim] // n
    take = lambda t: lax.dynamic_slice_in_dim(x, t * size, size, dim)
    pieces = [take(me)]
    for k in range(1, n):
        pieces.append(lax.ppermute(take((me + k) % n), axis, shift_pairs(n, k)))
    return order_blocks(pieces, me, gather_dim)


def halo(x, axis, dim, place=None):
    n = lax.axis_size(axis)
    place = place or (lambda i: i)
    up = [(place(i), place(i + 1)) for i in range(n - 1)]
    down = [(place(i + 1), place(i)) for i in range(n - 1)]
    length = x.shape[dim]
    before = lax.ppermute(lax.slice_in_dim(x, length - 1, length, axis=dim), axis, up)
    after = lax.ppermute(lax.slice_in_dim(x, 0, 1, axis=dim), axis, down)
    return jnp.concatenate([before, x, after], axis=dim)


def plane_conv(rows, weight, spec):
    return lax.conv_general_dilated(
        rows,
        weight,
        window_strides=(1, 1),
        padding=((0, 0), (1, 1)),
        dimension_numbers=("CNHW", spec, "CNHW"),
        preferred_element_type=jnp.float32,
    )


def depth_conv(padded, weight, spec):
    out = lax.conv_general_dilated(
        padded[None],
        weight[:, None, None],
        window_strides=(1, 1, 1),
        padding=((0, 0), (0, 0), (0, 0)),
        dimension_numbers=("NCDHW", spec, "NCDHW"),
        preferred_element_type=jnp.float32,
    )
    return out[0]


def gather_weight(weight):
    filts = lax.axis_size("filt")
    chans = lax.axis_size("chan")
    slabs = lax.axis_size("slab")
    core = lax.axis_index("slab") % 2
    c_loc = weight.shape[2]
    half = c_loc // 2
    mine = lax.dynamic_slice_in_dim(weight, core * half, half, 2)
    spread = jnp.broadcast_to(mine[None], (filts,) + mine.shape)
    got = lax.all_to_all(spread, "filt", 0, 4, tiled=True)[0]
    by_filt = jnp.concatenate([got] + [lax.ppermute(got, "chan", shift_pairs(chans, k)) for k in range(1, chans)], axis=2)
    other = lax.ppermute(by_filt, "slab", [(i, i ^ 1) for i in range(slabs)])
    first = jnp.where(core == 0, by_filt, other)
    second = jnp.where(core == 0, other, by_filt)
    split = lambda w: w.reshape(3, 3, chans, 1, half, w.shape[-1])
    whole = jnp.concatenate([split(first), split(second)], axis=3)
    return whole.reshape(3, 3, chans * c_loc, whole.shape[-1])


def sub_block(chan, filt, filts):
    return jnp.where(chan % 2 == 0, filt, filts - 1 - filt)


def sub_block_of(c, f, filts):
    return f if c % 2 == 0 else filts - 1 - f


def forward(volume, weight, depth_weight):
    chans = lax.axis_size("chan")
    filts = lax.axis_size("filt")
    chan = lax.axis_index("chan")
    filt = lax.axis_index("filt")
    rows = volume.shape[2] // (chans * filts)
    padded = jnp.pad(volume, ((0, 0), (0, 0), (1, 1), (0, 0)))
    window = lambda c: lax.dynamic_slice_in_dim(padded, (c * filts + filt) * rows, rows + 2, 2)
    pieces = [window(chan)]
    for k in range(1, chans):
        pieces.append(lax.ppermute(window((chan + k) % chans), "chan", shift_pairs(chans, k)))
    all_channels = jnp.concatenate(pieces, axis=0)
    return plane_conv(all_channels, weight, "HWIO").astype(jnp.bfloat16)


def forward_out(deep, depth_weight):
    chans = lax.axis_size("chan")
    filts = lax.axis_size("filt")
    chan = lax.axis_index("chan")
    rows = deep.shape[2]
    out = depth_conv(deep, depth_weight, "DHWOI").astype(jnp.bfloat16)
    return lax.all_to_all(out, "filt", 0, 2, tiled=True)


def backward(grad_out, weight, depth_weight):
    chans = lax.axis_size("chan")
    filts = lax.axis_size("filt")
    chan = lax.axis_index("chan")
    filt = lax.axis_index("filt")
    rows = grad_out.shape[2] // filts
    turn = lambda f, r: r if f % 2 == 0 else chans - 1 - r
    place = lambda g: turn(g // chans, g % chans) * filts + g // chans
    group_of = lambda c, f: f * chans + turn(f, c)
    need = [[[f for f in range(filts) if group_of(t, f) // filts == r] for r in range(chans)] for t in range(chans)]
    per = max(len(need[t][r]) for t in range(chans) for r in range(chans))
    pick = lambda t, r: [group_of(t, f) % filts for f in need[t][r]] + [0] * (per - len(need[t][r]))
    received = []
    for k in range(chans):
        table = jnp.array([pick((r + k) % chans, r) for r in range(chans)], jnp.int32)[chan]
        send = jnp.stack([lax.dynamic_slice_in_dim(grad_out, table[q] * rows, rows, 2) for q in range(per)])
        received.append(send if k == 0 else lax.ppermute(send, "chan", shift_pairs(chans, k)))
    received = jnp.concatenate(received)
    slot = [[0] * filts for _ in range(chans)]
    for t in range(chans):
        for k in range(chans):
            r = (t - k) % chans
            for q, f in enumerate(need[t][r]):
                slot[t][f] = k * per + q
    blocks = jnp.take(received, jnp.array(slot, jnp.int32)[chan], axis=0)
    all_filters = lax.all_to_all(blocks, "filt", 0, 0, tiled=True)
    return all_filters.reshape((-1,) + all_filters.shape[2:])


def backward_in(deep, weight, depth_weight):
    chans = lax.axis_size("chan")
    filts = lax.axis_size("filt")
    filt = lax.axis_index("filt")
    rows = deep.shape[2]
    turn = lambda f, r: r if f % 2 == 0 else chans - 1 - r
    place = lambda g: turn(g // chans, g % chans) * filts + g // chans
    taps = depth_weight.shape[0]
    flipped = jnp.concatenate([depth_weight[t : t + 1] for t in reversed(range(taps))])
    grad_mid = depth_conv(deep, flipped, "DHWIO").astype(jnp.bfloat16)
    rimmed = halo(grad_mid, ROWS, 2, place)
    grad_in = plane_conv(rimmed, weight[::-1, ::-1], "HWOI").astype(jnp.bfloat16)
    chan = lax.axis_index("chan")
    c_loc = grad_in.shape[0] // chans
    even = filt % 2 == 0
    pieces = [grad_in[:c_loc]]
    for k in range(1, chans):
        target = jnp.where(even, (chan + k) % chans, (chan - k) % chans)
        pairs = [(c * filts + f, (((c + k) if f % 2 == 0 else (c - k)) % chans) * filts + f)
                 for c in range(chans) for f in range(filts)]
        at = (chan - target) % chans
        pieces.append(lax.ppermute(lax.dynamic_slice_in_dim(grad_in, at * c_loc, c_loc, 0), ROWS, pairs))
    return order_blocks(pieces, jnp.where(even, chan, chans - 1 - chan), 2)


def local(volume, plane_weight, depth_weight, grad_out):
    weight = gather_weight(plane_weight)
    mid = forward(volume, weight, depth_weight)
    all_filters = backward(grad_out, weight, depth_weight)
    deep = halo(jnp.concatenate([mid, all_filters]), "slab", 1)
    output = forward_out(deep[: mid.shape[0]], depth_weight)
    grad_in = backward_in(deep[mid.shape[0] :], weight, depth_weight)
    return (output, grad_in)


def solution(mesh):
    placed = (
        P("chan", "slab", None, None),
        P(None, None, "chan", "filt"),
        P(),
        P("filt", "slab", "chan", None),
    )
    return jax.shard_map(
        local,
        mesh=mesh,
        in_specs=placed,
        out_specs=(P("filt", "slab", "chan", None), P("chan", "slab", "filt", None)),
        check_vma=False,
    )
```
